32 devices in a mesh: req: 8 (over y, x, core), tp: 4 (over z).
Axes of the slice: x: 2, y: 2, z: 4, core: 2. Of those that a mesh axis runs over, the one named last changes fastest.
Arguments:
- residual: bfloat16 [2048, 2048], P('req', 'tp'), may hold values from -0.29882812 to 0.29882812
- queries: bfloat16 [2048, 1280], P('req', 'tp'), may hold values from -6 to 6
- suffix_kv: bfloat16 [2048, 4, 256], P('req', 'tp'), may hold values from -4 to 4
- prefix_cache: bfloat16 [8192, 4, 256], P('req', 'tp'), may hold values from -6 to 6
- out_weight: bfloat16 [1280, 2048], P('tp'), may hold values from -0.15625 to 0.15625
- norm_gain: bfloat16 [2048], replicated, may hold values from 0.5 to 1.5
- next_query_weight: bfloat16 [2048, 1280], P(None, 'tp'), may hold values from -0.125 to 0.125
- lengths: int32 [8, 4], P('req'), may hold values from 1 to 128, 256 in all within a row
- tenant: int32 [8, 4], P('req'), may hold values from 0 to 3
- owners: int32 [4], replicated, may hold values from 0 to 7, as said below
Outputs:
- new_residual: bfloat16 [2048, 2048], P('req', 'tp')
- next_queries: bfloat16 [2048, 1280], P('req', 'tp')
The draws below stay inside these ranges and needn't reach their ends.
Inputs may be any that keep to these rules, and one draw needn't show every extreme that they name: `lengths`: each device's 4 requests fill its 256 rows in order. `owners`: distinct.
All inputs are finite; a program needn't handle non-finite values.
Results may differ from the reference program's by a relative error of at most 0.0065.
Values may be sent and summed in bfloat16 or wider, within the bound.
No kernel may reach another device: no remote copies, remote signals or barrier semaphores. Data moves between devices by JAX's collectives and lax.ppermute only.
A program may use at most 64 MiB of HBM per device.

```python
import math
import jax
import jax.numpy as jnp
import numpy as np
from jax import lax

D = 2048
QH = 20
KVH = 5
HD = 64
ROWS = 256
PREF = 1024
TENANTS = 4
RPD = 4
MOSTLEN = 128
TOKENS = 2048
SLOTS = 8192
N_REQ = 8
N_TP = 4


def draw_queries(key, part):
    own_key = jax.random.fold_in(key, 11)
    base = jnp.clip(jax.random.normal(own_key, (TOKENS, QH, HD), jnp.float32), -4.0, 4.0)
    return base.reshape(TOKENS, QH * HD).astype(jnp.bfloat16)


def draw_prefix_cache(key, part):
    own_key = jax.random.fold_in(key, 23)
    shape = (SLOTS, N_TP, 2, 2, HD)
    base = jnp.clip(jax.random.normal(own_key, shape, jnp.float32), -4.0, 4.0)
    return base.reshape(SLOTS, N_TP, 4 * HD).astype(jnp.bfloat16)


def draw_owners(key, part):
    quarter = N_REQ // TENANTS
    offsets = jax.random.randint(jax.random.fold_in(key, 31), (TENANTS,), 0, quarter)
    offsets = offsets.at[0].set(0)
    offsets = offsets.at[TENANTS - 1].set(quarter - 1)
    base = N_REQ - 1 - jnp.arange(TENANTS) * quarter - offsets
    order = jax.random.permutation(jax.random.fold_in(key, 37), TENANTS)
    return base[order].astype(jnp.int32)


def touch_ends(result, key, smallest, top_value):
    dims = result.shape
    spot = [jax.random.randint(jax.random.fold_in(key, axis), (), 0, dims[axis]) for axis in range(len(dims))]
    result = result.at[tuple(spot)].set(smallest)
    longest = dims.index(max(dims))
    spot[longest] = (spot[longest] + 1) % dims[longest]
    return result.at[tuple(spot)].set(top_value)


def steps_of(rng, dims, cuts, smallest, high):
    level = 1.0
    for dim, parts in cuts:
        heights = jax.random.uniform(jax.random.fold_in(jax.random.fold_in(rng, 6), dim), (parts,), jnp.float32, smallest / len(cuts), high / len(cuts))
        level = level * jnp.repeat(jnp.exp(heights), dims[dim] // parts).reshape((-1,) + (1,) * (len(dims) - 1 - dim))
    return level


def split_up(amount, total, bound, skew):
    weights = [(1 << 20) // math.isqrt(rank ** skew) + 1 for rank in range(2, amount + 1)]
    surplus, holding = total - bound - (amount - 1), [1] * (amount - 1)
    while surplus > 0:
        candidates = [i for i in range(amount - 1) if holding[i] < bound]
        mass, budget = sum([weights[i] for i in candidates]), surplus
        for i in candidates:
            more = min(bound - holding[i], max(1, budget * weights[i] // mass), surplus)
            holding[i] = holding[i] + more
            surplus = surplus - more
    return np.array([bound] + holding)


def uneven_parts(rng, number_of, total, limit, skew):
    if number_of == 2:
        one = jax.random.randint(rng, (), max(1, total - limit), min(limit, total - 1) + 1)
        return jnp.stack([one, total - one])
    tallies = jnp.asarray(split_up(number_of, total, limit, skew), jnp.int32)
    twos = (number_of - 1) // 2
    donor, sink = tallies[1:1 + 2 * twos:2], tallies[2:2 + 2 * twos:2]
    margin = jnp.minimum(donor - 1, limit - sink)
    moved = jax.random.randint(jax.random.fold_in(rng, 1), (twos,), 0, 1 << 20) % (margin + 1)
    tallies = tallies.at[1:1 + 2 * twos:2].set(donor - moved).at[2:2 + 2 * twos:2].set(sink + moved)
    return tallies[jax.random.permutation(jax.random.fold_in(rng, 2), number_of)]


def normal_values(rng, extent, deviation, most, pieces=(), held_as=jnp.bfloat16):
    values = jax.random.normal(rng, extent, jnp.float32) * deviation
    if len(pieces) > 0:
        values = steps_of(rng, extent, pieces, -0.22, 0.18) * values
    return jnp.clip(values, min=-most, max=most).astype(held_as)


def setup_inputs(seed: int = 0) -> dict:
    splits = jax.random.split(jax.random.key(seed), 11)
    return {
        "residual": normal_values(splits[0], (TOKENS, D), 0.05, 0.29882812, ((0, 8), (1, 4))),
        "queries": draw_queries(jax.random.fold_in(splits[10], 71), 0),
        "suffix_kv": normal_values(splits[2], (TOKENS, N_TP, 4 * HD), 1.0, 4.0, ((0, 8), (1, 4))),
        "prefix_cache": draw_prefix_cache(jax.random.fold_in(splits[10], 71), 0),
        "out_weight": normal_values(splits[4], (QH * HD, D), (QH * HD) ** -0.5, 0.15625, ((0, 4),)),
        "norm_gain": jnp.clip(1.0 + 0.1 * jax.random.normal(splits[5], (D,), jnp.float32), 0.5, 1.5).astype(jnp.bfloat16),
        "next_query_weight": normal_values(splits[6], (D, QH * HD), D ** -0.5, 0.125, ((1, 4),)),
        "lengths": jax.vmap(lambda own: uneven_parts(own, RPD, ROWS, MOSTLEN, 2))(jax.random.split(splits[7], N_REQ)).reshape((N_REQ, RPD)).astype(jnp.int32),
        "tenant": touch_ends(jax.random.randint(splits[8], (N_REQ, RPD), 0, TENANTS), jax.random.fold_in(splits[8], 1), 0, TENANTS - 1).astype(jnp.int32),
        "owners": draw_owners(jax.random.fold_in(splits[10], 71), 0),
    }


def reference(residual, queries, suffix_kv, prefix_cache, out_weight, norm_gain, next_query_weight, lengths, tenant, owners):
    per_block = QH // N_TP
    group_size = QH // KVH
    head_ids = np.arange(QH)
    slot_index = head_ids // per_block * 2 + (head_ids // group_size - head_ids // per_block)
    cache_rows = prefix_cache.reshape(N_REQ * PREF, N_TP * 2, 2, HD)
    stacked = jnp.stack([lax.dynamic_slice_in_dim(cache_rows, (owners[tenant_id] * PREF).astype(jnp.int32), PREF, 0) for tenant_id in range(TENANTS)])
    prefix_keys = stacked[:, :, slot_index, 0, :].astype(jnp.float32)
    prefix_values = stacked[:, :, slot_index, 1, :].astype(jnp.float32)
    score_scale = HD ** (-0.5)

    def one_device(inputs):
        query_rows, pair_rows, req_lengths, req_tenant = inputs
        query_heads = query_rows.astype(jnp.float32).reshape(ROWS, QH, HD)
        pairs = pair_rows.reshape(ROWS, N_TP * 2, 2, HD)
        suffix_keys = pairs[:, slot_index, 0, :].astype(jnp.float32)
        suffix_values = pairs[:, slot_index, 1, :].astype(jnp.float32)
        req_ends = jnp.cumsum(req_lengths)
        req_starts = req_ends - req_lengths
        position = jnp.arange(ROWS, dtype=jnp.int32)
        request_ids = lax.optimization_barrier(jnp.sum((position[:, None] >= req_ends[None, :]).astype(jnp.int32), axis=1))
        member = request_ids[:, None] == jnp.arange(RPD, dtype=jnp.int32)[None, :]
        row_start = lax.optimization_barrier(jnp.sum(jnp.where(member, req_starts[None, :], 0), axis=1))
        row_tenant = lax.optimization_barrier(jnp.sum(jnp.where(member, req_tenant[None, :], 0), axis=1))
        prefix_scores = jnp.einsum('rhd,gphd->hrgp', query_heads, prefix_keys) * score_scale
        prefix_mask = (row_tenant[:, None] == jnp.arange(TENANTS, dtype=jnp.int32)[None, :])[None, :, :, None]
        suffix_scores = jnp.einsum('rhd,khd->hrk', query_heads, suffix_keys) * score_scale
        suffix_mask = ((position[None, :] >= row_start[:, None]) & (position[None, :] <= position[:, None]))[None]
        row_top = jnp.maximum(lax.optimization_barrier(jnp.max(jnp.where(prefix_mask, prefix_scores, -jnp.inf), axis=(2, 3))), lax.optimization_barrier(jnp.max(jnp.where(suffix_mask, suffix_scores, -jnp.inf), axis=2)))
        prefix_weights = jnp.where(prefix_mask, jnp.exp(prefix_scores - row_top[:, :, None, None]), 0.0)
        suffix_weights = jnp.where(suffix_mask, jnp.exp(suffix_scores - row_top[:, :, None]), 0.0)
        denominator = lax.optimization_barrier(jnp.sum(prefix_weights, axis=(2, 3))) + lax.optimization_barrier(jnp.sum(suffix_weights, axis=2))
        prefix_probs = lax.optimization_barrier(prefix_weights.astype(jnp.bfloat16)).astype(jnp.float32)
        suffix_probs = lax.optimization_barrier(suffix_weights.astype(jnp.bfloat16)).astype(jnp.float32)
        accumulated = jnp.einsum('hrgp,gphd->rhd', prefix_probs, prefix_values) + jnp.einsum('hrk,khd->rhd', suffix_probs, suffix_values)
        attended_rows = accumulated / jnp.transpose(denominator)[:, :, None]
        return attended_rows.astype(jnp.bfloat16).reshape(ROWS, QH * HD)
    attended = lax.map(one_device, (queries.reshape(N_REQ, ROWS, QH * HD), suffix_kv.reshape(N_REQ, ROWS, N_TP, 4 * HD), lengths, tenant))
    attended = attended.reshape(TOKENS, QH * HD)
    projected = jnp.dot(attended, out_weight, preferred_element_type=jnp.float32)
    new_residual = (residual.astype(jnp.float32) + projected).astype(jnp.bfloat16)
    widened = new_residual.astype(jnp.float32)
    mean_square = lax.optimization_barrier(jnp.mean(widened * widened, axis=1, keepdims=True))
    normed = (widened * lax.rsqrt(mean_square + 1e-05) * norm_gain.astype(jnp.float32)).astype(jnp.bfloat16)
    next_queries = jnp.dot(normed, next_query_weight, preferred_element_type=jnp.float32).astype(jnp.bfloat16)
    return (new_residual, next_queries)
```

```python
import jax
import jax.numpy as jnp
from jax import lax
from jax.sharding import PartitionSpec as P

QH = 20
KVH = 5
HD = 64
TENANTS = 4
GATHER_SLOTS_MAX = 16


def from_root(block, axis, source):
    block = jnp.where(lax.axis_index(axis) == source, block, jnp.zeros_like(block))
    return lax.psum(block, axis)


def pick_heads(pair_rows, select):
    split_pair = pair_rows.reshape(pair_rows.shape[0], 2, 2, HD)
    key_heads = jnp.einsum(
        "njd,hj->nhd", split_pair[:, :, 0], select, preferred_element_type=jnp.float32
    ).astype(jnp.bfloat16)
    value_heads = jnp.einsum(
        "njd,hj->nhd", split_pair[:, :, 1], select, preferred_element_type=jnp.float32
    ).astype(jnp.bfloat16)
    return (key_heads, value_heads)


def tenant_prefixes(own_slot, owners, n_req):
    slot_rows = own_slot.shape[0]
    if n_req <= GATHER_SLOTS_MAX:
        every_slot = lax.all_gather(own_slot, "req", axis=0, tiled=True)
        return [
            lax.dynamic_slice_in_dim(every_slot, owners[tenant_id] * slot_rows, slot_rows, 0)
            for tenant_id in range(TENANTS)
        ]
    return [from_root(own_slot, "req", owners[tenant_id]) for tenant_id in range(TENANTS)]


def shifted(block, shift, n_tp):
    pairs = [(source, (source + shift) % n_tp) for source in range(n_tp)]
    return lax.ppermute(block, "tp", pairs)


def local(
    residual,
    queries,
    suffix_kv,
    prefix_cache,
    out_weight,
    norm_gain,
    next_query_weight,
    lengths,
    tenant,
    owners,
    n_req,
    n_tp,
):
    row_count = queries.shape[0]
    head_count = queries.shape[1] // HD
    width = residual.shape[1]
    tp_index = lax.axis_index("tp")

    weight_pieces = []
    for shift in range(n_tp):
        target = (tp_index + shift) % n_tp
        piece = lax.dynamic_slice_in_dim(out_weight, target * width, width, 1)
        weight_pieces.append(piece if shift == 0 else shifted(piece, shift, n_tp))

    head_ids = tp_index * head_count + jnp.arange(head_count, dtype=jnp.int32)
    pair_ids = head_ids // (QH // KVH) - tp_index
    select = (pair_ids[:, None] == jnp.arange(2, dtype=jnp.int32)[None, :]).astype(jnp.bfloat16)
    req_lengths = lengths[0]
    req_tenant = tenant[0]
    req_ends = jnp.cumsum(req_lengths)
    req_starts = req_ends - req_lengths
    position = jnp.arange(row_count, dtype=jnp.int32)
    request_ids = jnp.sum((position[:, None] >= req_ends[None, :]).astype(jnp.int32), axis=1)
    member = request_ids[:, None] == jnp.arange(req_lengths.shape[0], dtype=jnp.int32)[None, :]
    row_start = jnp.sum(jnp.where(member, req_starts[None, :], 0), axis=1)
    row_tenant = jnp.sum(jnp.where(member, req_tenant[None, :], 0), axis=1)
    score_scale = HD ** (-0.5)
    query_heads = queries.reshape(row_count, head_count, HD)
    suffix_keys, suffix_values = pick_heads(suffix_kv.reshape(row_count, -1), select)
    suffix_scores = (
        jnp.einsum("rhd,khd->hrk", query_heads, suffix_keys, preferred_element_type=jnp.float32)
        * score_scale
    )
    suffix_mask = (
        (position[None, :] >= row_start[:, None]) & (position[None, :] <= position[:, None])
    )[None]
    own_slot = prefix_cache.reshape(prefix_cache.shape[0], -1)
    prefix_blocks = tenant_prefixes(own_slot, owners, n_req)
    picked = [pick_heads(block_rows, select) for block_rows in prefix_blocks]
    row_top = jnp.max(jnp.where(suffix_mask, suffix_scores, -jnp.inf), axis=2)
    for tenant_id in range(TENANTS):
        tenant_mask = (row_tenant == tenant_id)[None, :, None]
        prefix_scores = (
            jnp.einsum(
                "rhd,phd->hrp",
                query_heads,
                picked[tenant_id][0],
                preferred_element_type=jnp.float32,
            )
            * score_scale
        )
        row_top = jnp.maximum(
            row_top, jnp.max(jnp.where(tenant_mask, prefix_scores, -jnp.inf), axis=2)
        )
    suffix_weights = jnp.where(suffix_mask, jnp.exp(suffix_scores - row_top[:, :, None]), 0.0)
    denominator = jnp.sum(suffix_weights, axis=2)
    accumulated = jnp.einsum(
        "hrk,khd->rhd",
        suffix_weights.astype(jnp.bfloat16),
        suffix_values,
        preferred_element_type=jnp.float32,
    )
    for tenant_id in range(TENANTS):
        tenant_mask = (row_tenant == tenant_id)[None, :, None]
        prefix_scores = (
            jnp.einsum(
                "rhd,phd->hrp",
                query_heads,
                picked[tenant_id][0],
                preferred_element_type=jnp.float32,
            )
            * score_scale
        )
        prefix_weights = jnp.where(tenant_mask, jnp.exp(prefix_scores - row_top[:, :, None]), 0.0)
        denominator = denominator + jnp.sum(prefix_weights, axis=2)
        accumulated = accumulated + jnp.einsum(
            "hrp,phd->rhd",
            prefix_weights.astype(jnp.bfloat16),
            picked[tenant_id][1],
            preferred_element_type=jnp.float32,
        )
    attended = (
        (accumulated / jnp.transpose(denominator)[:, :, None])
        .astype(jnp.bfloat16)
        .reshape(row_count, -1)
    )

    projected = jnp.dot(attended, weight_pieces[0], preferred_element_type=jnp.float32)
    for shift in range(1, n_tp):
        head_block = shifted(attended, shift, n_tp)
        projected = projected + jnp.dot(
            head_block, weight_pieces[shift], preferred_element_type=jnp.float32
        )
    new_residual = (residual.astype(jnp.float32) + projected).astype(jnp.bfloat16)

    full_new = lax.all_gather(new_residual, "tp", axis=1, tiled=True)
    widened = full_new.astype(jnp.float32)
    mean_square = jnp.mean(widened * widened, axis=1, keepdims=True)
    normed = (widened * lax.rsqrt(mean_square + 1e-05) * norm_gain.astype(jnp.float32)).astype(
        jnp.bfloat16
    )
    next_sums = jnp.dot(normed, next_query_weight, preferred_element_type=jnp.float32)
    return (new_residual, next_sums.astype(jnp.bfloat16))


def solution(mesh):
    n_req = mesh.shape["req"]
    n_tp = mesh.shape["tp"]

    def body(*args):
        return local(*args, n_req=n_req, n_tp=n_tp)

    return jax.shard_map(
        body,
        mesh=mesh,
        in_specs=(
            P("req", "tp"),
            P("req", "tp"),
            P("req", "tp", None),
            P("req", "tp", None),
            P("tp", None),
            P(),
            P(None, "tp"),
            P("req", None),
            P("req", None),
            P(),
        ),
        out_specs=(P("req", "tp"), P("req", "tp")),
        check_vma=False,
    )
```

```python
import jax
import jax.numpy as jnp
from jax import lax
from jax.sharding import PartitionSpec as P

QH = 20
KVH = 5
HD = 64
TENANTS = 4
GATHER_SLOTS_MAX = 16


def from_root(block, axis, source):
    block = jnp.where(lax.axis_index(axis) == source, block, jnp.zeros_like(block))
    return lax.psum(block, axis)


def pick_heads(pair_rows, select):
    split_pair = pair_rows.reshape(pair_rows.shape[0], 2, 2, HD)
    key_heads = jnp.einsum(
        "njd,hj->nhd", split_pair[:, :, 0], select, preferred_element_type=jnp.float32
    ).astype(jnp.bfloat16)
    value_heads = jnp.einsum(
        "njd,hj->nhd", split_pair[:, :, 1], select, preferred_element_type=jnp.float32
    ).astype(jnp.bfloat16)
    return (key_heads, value_heads)


def xor_permute(block, mask, n_req):
    pairs = [(source, source ^ mask) for source in range(n_req)]
    return lax.ppermute(block, "req", pairs)


def tenant_prefixes(own_slot, owners, n_req):
    slot_rows = own_slot.shape[0]
    if n_req <= GATHER_SLOTS_MAX and n_req % 2 == 0 and (n_req & (n_req - 1)) == 0:
        n_chips = n_req // 2
        req_index = lax.axis_index("req")
        same_core = [own_slot] + [
            xor_permute(own_slot, 2 * chip_mask, n_req) for chip_mask in range(1, n_chips)
        ]
        own_stack = jnp.stack(same_core)
        other_stack = xor_permute(own_stack, 1, n_req)
        blocks = []
        for tenant_id in range(TENANTS):
            owner = owners[tenant_id]
            position = (owner // 2) ^ (req_index // 2)
            mine = lax.dynamic_index_in_dim(own_stack, position, 0, keepdims=False)
            theirs = lax.dynamic_index_in_dim(other_stack, position, 0, keepdims=False)
            blocks.append(jnp.where(owner % 2 == req_index % 2, mine, theirs))
        return blocks
    return [from_root(own_slot, "req", owners[tenant_id]) for tenant_id in range(TENANTS)]


def shifted(block, shift, n_tp):
    pairs = [(source, (source + shift) % n_tp) for source in range(n_tp)]
    return lax.ppermute(block, "tp", pairs)


def local(
    residual,
    queries,
    suffix_kv,
    prefix_cache,
    out_weight,
    norm_gain,
    next_query_weight,
    lengths,
    tenant,
    owners,
    n_req,
    n_tp,
):
    row_count = queries.shape[0]
    head_count = queries.shape[1] // HD
    width = residual.shape[1]
    tp_index = lax.axis_index("tp")

    weight_pieces = []
    for shift in range(n_tp):
        target = (tp_index + shift) % n_tp
        piece = lax.dynamic_slice_in_dim(out_weight, target * width, width, 1)
        weight_pieces.append(piece if shift == 0 else shifted(piece, shift, n_tp))

    head_ids = tp_index * head_count + jnp.arange(head_count, dtype=jnp.int32)
    pair_ids = head_ids // (QH // KVH) - tp_index
    select = (pair_ids[:, None] == jnp.arange(2, dtype=jnp.int32)[None, :]).astype(jnp.bfloat16)
    req_lengths = lengths[0]
    req_tenant = tenant[0]
    req_ends = jnp.cumsum(req_lengths)
    req_starts = req_ends - req_lengths
    position = jnp.arange(row_count, dtype=jnp.int32)
    request_ids = jnp.sum((position[:, None] >= req_ends[None, :]).astype(jnp.int32), axis=1)
    member = request_ids[:, None] == jnp.arange(req_lengths.shape[0], dtype=jnp.int32)[None, :]
    row_start = jnp.sum(jnp.where(member, req_starts[None, :], 0), axis=1)
    row_tenant = jnp.sum(jnp.where(member, req_tenant[None, :], 0), axis=1)
    score_scale = HD ** (-0.5)
    query_heads = queries.reshape(row_count, head_count, HD)
    suffix_keys, suffix_values = pick_heads(suffix_kv.reshape(row_count, -1), select)
    suffix_scores = (
        jnp.einsum("rhd,khd->hrk", query_heads, suffix_keys, preferred_element_type=jnp.float32)
        * score_scale
    )
    suffix_mask = (
        (position[None, :] >= row_start[:, None]) & (position[None, :] <= position[:, None])
    )[None]
    own_slot = prefix_cache.reshape(prefix_cache.shape[0], -1)
    prefix_blocks = tenant_prefixes(own_slot, owners, n_req)
    picked = [pick_heads(block_rows, select) for block_rows in prefix_blocks]
    row_top = jnp.max(jnp.where(suffix_mask, suffix_scores, -jnp.inf), axis=2)
    for tenant_id in range(TENANTS):
        tenant_mask = (row_tenant == tenant_id)[None, :, None]
        prefix_scores = (
            jnp.einsum(
                "rhd,phd->hrp",
                query_heads,
                picked[tenant_id][0],
                preferred_element_type=jnp.float32,
            )
            * score_scale
        )
        row_top = jnp.maximum(
            row_top, jnp.max(jnp.where(tenant_mask, prefix_scores, -jnp.inf), axis=2)
        )
    suffix_weights = jnp.where(suffix_mask, jnp.exp(suffix_scores - row_top[:, :, None]), 0.0)
    denominator = jnp.sum(suffix_weights, axis=2)
    accumulated = jnp.einsum(
        "hrk,khd->rhd",
        suffix_weights.astype(jnp.bfloat16),
        suffix_values,
        preferred_element_type=jnp.float32,
    )
    for tenant_id in range(TENANTS):
        tenant_mask = (row_tenant == tenant_id)[None, :, None]
        prefix_scores = (
            jnp.einsum(
                "rhd,phd->hrp",
                query_heads,
                picked[tenant_id][0],
                preferred_element_type=jnp.float32,
            )
            * score_scale
        )
        prefix_weights = jnp.where(tenant_mask, jnp.exp(prefix_scores - row_top[:, :, None]), 0.0)
        denominator = denominator + jnp.sum(prefix_weights, axis=2)
        accumulated = accumulated + jnp.einsum(
            "hrp,phd->rhd",
            prefix_weights.astype(jnp.bfloat16),
            picked[tenant_id][1],
            preferred_element_type=jnp.float32,
        )
    attended = (
        (accumulated / jnp.transpose(denominator)[:, :, None])
        .astype(jnp.bfloat16)
        .reshape(row_count, -1)
    )

    projected = jnp.dot(attended, weight_pieces[0], preferred_element_type=jnp.float32)
    for shift in range(1, n_tp):
        head_block = shifted(attended, shift, n_tp)
        projected = projected + jnp.dot(
            head_block, weight_pieces[shift], preferred_element_type=jnp.float32
        )
    new_residual = (residual.astype(jnp.float32) + projected).astype(jnp.bfloat16)

    full_new = lax.all_gather(new_residual, "tp", axis=1, tiled=True)
    widened = full_new.astype(jnp.float32)
    mean_square = jnp.mean(widened * widened, axis=1, keepdims=True)
    normed = (widened * lax.rsqrt(mean_square + 1e-05) * norm_gain.astype(jnp.float32)).astype(
        jnp.bfloat16
    )
    next_sums = jnp.dot(normed, next_query_weight, preferred_element_type=jnp.float32)
    return (new_residual, next_sums.astype(jnp.bfloat16))


def solution(mesh):
    n_req = mesh.shape["req"]
    n_tp = mesh.shape["tp"]

    def body(*args):
        return local(*args, n_req=n_req, n_tp=n_tp)

    return jax.shard_map(
        body,
        mesh=mesh,
        in_specs=(
            P("req", "tp"),
            P("req", "tp"),
            P("req", "tp", None),
            P("req", "tp", None),
            P("tp", None),
            P(),
            P(None, "tp"),
            P("req", None),
            P("req", None),
            P(),
        ),
        out_specs=(P("req", "tp"), P("req", "tp")),
        check_vma=False,
    )
```

```python
import jax
import jax.numpy as jnp
from jax import lax
from jax.sharding import PartitionSpec as P

QH = 20
KVH = 5
HD = 64
TENANTS = 4
GATHER_SLOTS_MAX = 16


def from_root(block, axis, source):
    block = jnp.where(lax.axis_index(axis) == source, block, jnp.zeros_like(block))
    return lax.psum(block, axis)


def pick_heads(pair_rows, select):
    split_pair = pair_rows.reshape(pair_rows.shape[0], 2, 2, HD)
    key_heads = jnp.einsum(
        "njd,hj->nhd", split_pair[:, :, 0], select, preferred_element_type=jnp.float32
    ).astype(jnp.bfloat16)
    value_heads = jnp.einsum(
        "njd,hj->nhd", split_pair[:, :, 1], select, preferred_element_type=jnp.float32
    ).astype(jnp.bfloat16)
    return (key_heads, value_heads)


def every_slot_of(part, n_req):
    return lax.all_gather(part, "req", axis=0, tiled=True)


def slots_of_tenants(part, every_slot, owners, n_req):
    slot_rows = part.shape[0]
    if n_req <= GATHER_SLOTS_MAX:
        return [
            lax.dynamic_slice_in_dim(every_slot, owners[tenant_id] * slot_rows, slot_rows, 0)
            for tenant_id in range(TENANTS)
        ]
    return [from_root(part, "req", owners[tenant_id]) for tenant_id in range(TENANTS)]


def pick_part(part_rows, select):
    return jnp.einsum(
        "njd,hj->nhd", part_rows, select, preferred_element_type=jnp.float32
    ).astype(jnp.bfloat16)


def shifted(block, shift, n_tp):
    pairs = [(source, (source + shift) % n_tp) for source in range(n_tp)]
    return lax.ppermute(block, "tp", pairs)


def local(
    residual,
    queries,
    suffix_kv,
    prefix_cache,
    out_weight,
    norm_gain,
    next_query_weight,
    lengths,
    tenant,
    owners,
    n_req,
    n_tp,
):
    row_count = queries.shape[0]
    head_count = queries.shape[1] // HD
    width = residual.shape[1]
    tp_index = lax.axis_index("tp")

    weight_pieces = []
    for shift in range(n_tp):
        target = (tp_index + shift) % n_tp
        piece = lax.dynamic_slice_in_dim(out_weight, target * width, width, 1)
        weight_pieces.append(piece if shift == 0 else shifted(piece, shift, n_tp))

    head_ids = tp_index * head_count + jnp.arange(head_count, dtype=jnp.int32)
    pair_ids = head_ids // (QH // KVH) - tp_index
    select = (pair_ids[:, None] == jnp.arange(2, dtype=jnp.int32)[None, :]).astype(jnp.bfloat16)
    req_lengths = lengths[0]
    req_tenant = tenant[0]
    req_ends = jnp.cumsum(req_lengths)
    req_starts = req_ends - req_lengths
    position = jnp.arange(row_count, dtype=jnp.int32)
    request_ids = jnp.sum((position[:, None] >= req_ends[None, :]).astype(jnp.int32), axis=1)
    member = request_ids[:, None] == jnp.arange(req_lengths.shape[0], dtype=jnp.int32)[None, :]
    row_start = jnp.sum(jnp.where(member, req_starts[None, :], 0), axis=1)
    row_tenant = jnp.sum(jnp.where(member, req_tenant[None, :], 0), axis=1)
    score_scale = HD ** (-0.5)
    query_heads = queries.reshape(row_count, head_count, HD)
    suffix_keys, suffix_values = pick_heads(suffix_kv.reshape(row_count, -1), select)
    suffix_scores = (
        jnp.einsum("rhd,khd->hrk", query_heads, suffix_keys, preferred_element_type=jnp.float32)
        * score_scale
    )
    suffix_mask = (
        (position[None, :] >= row_start[:, None]) & (position[None, :] <= position[:, None])
    )[None]
    own_slot = prefix_cache.reshape(prefix_cache.shape[0], 2, 2, HD)
    own_keys = own_slot[:, :, 0]
    own_values = own_slot[:, :, 1]
    if n_req <= GATHER_SLOTS_MAX:
        every_key = every_slot_of(own_keys, n_req)
        own_values, every_key = lax.optimization_barrier((own_values, every_key))
        every_value = every_slot_of(own_values, n_req)
    else:
        every_key = every_value = None
    key_blocks = slots_of_tenants(own_keys, every_key, owners, n_req)
    value_blocks = slots_of_tenants(own_values, every_value, owners, n_req)
    picked = [
        (pick_part(key_rows, select), pick_part(value_rows, select))
        for key_rows, value_rows in zip(key_blocks, value_blocks)
    ]
    row_top = jnp.max(jnp.where(suffix_mask, suffix_scores, -jnp.inf), axis=2)
    for tenant_id in range(TENANTS):
        tenant_mask = (row_tenant == tenant_id)[None, :, None]
        prefix_scores = (
            jnp.einsum(
                "rhd,phd->hrp",
                query_heads,
                picked[tenant_id][0],
                preferred_element_type=jnp.float32,
            )
            * score_scale
        )
        row_top = jnp.maximum(
            row_top, jnp.max(jnp.where(tenant_mask, prefix_scores, -jnp.inf), axis=2)
        )
    suffix_weights = jnp.where(suffix_mask, jnp.exp(suffix_scores - row_top[:, :, None]), 0.0)
    denominator = jnp.sum(suffix_weights, axis=2)
    accumulated = jnp.einsum(
        "hrk,khd->rhd",
        suffix_weights.astype(jnp.bfloat16),
        suffix_values,
        preferred_element_type=jnp.float32,
    )
    for tenant_id in range(TENANTS):
        tenant_mask = (row_tenant == tenant_id)[None, :, None]
        prefix_scores = (
            jnp.einsum(
                "rhd,phd->hrp",
                query_heads,
                picked[tenant_id][0],
                preferred_element_type=jnp.float32,
            )
            * score_scale
        )
        prefix_weights = jnp.where(tenant_mask, jnp.exp(prefix_scores - row_top[:, :, None]), 0.0)
        denominator = denominator + jnp.sum(prefix_weights, axis=2)
        accumulated = accumulated + jnp.einsum(
            "hrp,phd->rhd",
            prefix_weights.astype(jnp.bfloat16),
            picked[tenant_id][1],
            preferred_element_type=jnp.float32,
        )
    attended = (
        (accumulated / jnp.transpose(denominator)[:, :, None])
        .astype(jnp.bfloat16)
        .reshape(row_count, -1)
    )

    projected = jnp.dot(attended, weight_pieces[0], preferred_element_type=jnp.float32)
    for shift in range(1, n_tp):
        head_block = shifted(attended, shift, n_tp)
        projected = projected + jnp.dot(
            head_block, weight_pieces[shift], preferred_element_type=jnp.float32
        )
    new_residual = (residual.astype(jnp.float32) + projected).astype(jnp.bfloat16)

    full_new = lax.all_gather(new_residual, "tp", axis=1, tiled=True)
    widened = full_new.astype(jnp.float32)
    mean_square = jnp.mean(widened * widened, axis=1, keepdims=True)
    normed = (widened * lax.rsqrt(mean_square + 1e-05) * norm_gain.astype(jnp.float32)).astype(
        jnp.bfloat16
    )
    next_sums = jnp.dot(normed, next_query_weight, preferred_element_type=jnp.float32)
    return (new_residual, next_sums.astype(jnp.bfloat16))


def solution(mesh):
    n_req = mesh.shape["req"]
    n_tp = mesh.shape["tp"]

    def body(*args):
        return local(*args, n_req=n_req, n_tp=n_tp)

    return jax.shard_map(
        body,
        mesh=mesh,
        in_specs=(
            P("req", "tp"),
            P("req", "tp"),
            P("req", "tp", None),
            P("req", "tp", None),
            P("tp", None),
            P(),
            P(None, "tp"),
            P("req", None),
            P("req", None),
            P(),
        ),
        out_specs=(P("req", "tp"), P("req", "tp")),
        check_vma=False,
    )
```

```python
import jax
import jax.numpy as jnp
from jax import lax
from jax.sharding import PartitionSpec as P

QH = 20
KVH = 5
HD = 64
TENANTS = 4
GATHER_SLOTS_MAX = 16


def from_root(block, axis, source):
    block = jnp.where(lax.axis_index(axis) == source, block, jnp.zeros_like(block))
    return lax.psum(block, axis)


def pick_heads(pair_rows, select):
    split_pair = pair_rows.reshape(pair_rows.shape[0], 2, 2, HD)
    key_heads = jnp.einsum(
        "njd,hj->nhd", split_pair[:, :, 0], select, preferred_element_type=jnp.float32
    ).astype(jnp.bfloat16)
    value_heads = jnp.einsum(
        "njd,hj->nhd", split_pair[:, :, 1], select, preferred_element_type=jnp.float32
    ).astype(jnp.bfloat16)
    return (key_heads, value_heads)


def tenant_prefixes(own_slot, owners, n_req):
    slot_rows = own_slot.shape[0]
    if n_req <= GATHER_SLOTS_MAX:
        every_slot = lax.all_gather(own_slot, "req", axis=0, tiled=True)
        return [
            lax.dynamic_slice_in_dim(every_slot, owners[tenant_id] * slot_rows, slot_rows, 0)
            for tenant_id in range(TENANTS)
        ]
    return [from_root(own_slot, "req", owners[tenant_id]) for tenant_id in range(TENANTS)]


def shifted(block, shift, n_tp):
    pairs = [(source, (source + shift) % n_tp) for source in range(n_tp)]
    return lax.ppermute(block, "tp", pairs)


def local(
    residual,
    queries,
    suffix_kv,
    prefix_cache,
    out_weight,
    norm_gain,
    next_query_weight,
    lengths,
    tenant,
    owners,
    n_req,
    n_tp,
):
    row_count = queries.shape[0]
    head_count = queries.shape[1] // HD
    width = residual.shape[1]
    tp_index = lax.axis_index("tp")

    weight_pieces = []
    for shift in range(n_tp):
        target = (tp_index + shift) % n_tp
        piece = lax.dynamic_slice_in_dim(out_weight, target * width, width, 1)
        weight_pieces.append(piece if shift == 0 else shifted(piece, shift, n_tp))

    head_ids = tp_index * head_count + jnp.arange(head_count, dtype=jnp.int32)
    pair_ids = head_ids // (QH // KVH) - tp_index
    select = (pair_ids[:, None] == jnp.arange(2, dtype=jnp.int32)[None, :]).astype(jnp.bfloat16)
    req_lengths = lengths[0]
    req_tenant = tenant[0]
    req_ends = jnp.cumsum(req_lengths)
    req_starts = req_ends - req_lengths
    position = jnp.arange(row_count, dtype=jnp.int32)
    request_ids = jnp.sum((position[:, None] >= req_ends[None, :]).astype(jnp.int32), axis=1)
    member = request_ids[:, None] == jnp.arange(req_lengths.shape[0], dtype=jnp.int32)[None, :]
    row_start = jnp.sum(jnp.where(member, req_starts[None, :], 0), axis=1)
    row_tenant = jnp.sum(jnp.where(member, req_tenant[None, :], 0), axis=1)
    score_scale = HD ** (-0.5)
    query_heads = queries.reshape(row_count, head_count, HD)
    suffix_keys, suffix_values = pick_heads(suffix_kv.reshape(row_count, -1), select)
    suffix_scores = (
        jnp.einsum("rhd,khd->hrk", query_heads, suffix_keys, preferred_element_type=jnp.float32)
        * score_scale
    )
    suffix_mask = (
        (position[None, :] >= row_start[:, None]) & (position[None, :] <= position[:, None])
    )[None]
    own_slot = prefix_cache.reshape(prefix_cache.shape[0], -1)
    prefix_blocks = tenant_prefixes(own_slot, owners, n_req)
    picked = [pick_heads(block_rows, select) for block_rows in prefix_blocks]
    row_top = jnp.max(jnp.where(suffix_mask, suffix_scores, -jnp.inf), axis=2)
    for tenant_id in range(TENANTS):
        tenant_mask = (row_tenant == tenant_id)[None, :, None]
        prefix_scores = (
            jnp.einsum(
                "rhd,phd->hrp",
                query_heads,
                picked[tenant_id][0],
                preferred_element_type=jnp.float32,
            )
            * score_scale
        )
        row_top = jnp.maximum(
            row_top, jnp.max(jnp.where(tenant_mask, prefix_scores, -jnp.inf), axis=2)
        )
    suffix_weights = jnp.where(suffix_mask, jnp.exp(suffix_scores - row_top[:, :, None]), 0.0)
    denominator = jnp.sum(suffix_weights, axis=2)
    accumulated = jnp.einsum(
        "hrk,khd->rhd",
        suffix_weights.astype(jnp.bfloat16),
        suffix_values,
        preferred_element_type=jnp.float32,
    )
    for tenant_id in range(TENANTS):
        tenant_mask = (row_tenant == tenant_id)[None, :, None]
        prefix_scores = (
            jnp.einsum(
                "rhd,phd->hrp",
                query_heads,
                picked[tenant_id][0],
                preferred_element_type=jnp.float32,
            )
            * score_scale
        )
        prefix_weights = jnp.where(tenant_mask, jnp.exp(prefix_scores - row_top[:, :, None]), 0.0)
        denominator = denominator + jnp.sum(prefix_weights, axis=2)
        accumulated = accumulated + jnp.einsum(
            "hrp,phd->rhd",
            prefix_weights.astype(jnp.bfloat16),
            picked[tenant_id][1],
            preferred_element_type=jnp.float32,
        )
    attended = (
        (accumulated / jnp.transpose(denominator)[:, :, None])
        .astype(jnp.bfloat16)
        .reshape(row_count, -1)
    )

    projected = jnp.dot(attended, weight_pieces[0], preferred_element_type=jnp.float32)
    for shift in range(1, n_tp):
        head_block = shifted(attended, shift, n_tp)
        projected = projected + jnp.dot(
            head_block, weight_pieces[shift], preferred_element_type=jnp.float32
        )
    new_residual = (residual.astype(jnp.float32) + projected).astype(jnp.bfloat16)

    blocks = [new_residual] + [shifted(new_residual, shift, n_tp) for shift in range(1, n_tp)]
    widened = [block.astype(jnp.float32) for block in blocks]
    square_sums = sum(jnp.sum(block * block, axis=1, keepdims=True) for block in widened)
    mean_square = square_sums / (width * n_tp)
    scale = lax.rsqrt(mean_square + 1e-05)
    gain = norm_gain.astype(jnp.float32)
    next_sums = None
    for shift in range(n_tp):
        source = (tp_index - shift) % n_tp
        block_gain = lax.dynamic_slice_in_dim(gain, source * width, width, 0)
        block_weight = lax.dynamic_slice_in_dim(next_query_weight, source * width, width, 0)
        normed = (widened[shift] * scale * block_gain).astype(jnp.bfloat16)
        part = jnp.dot(normed, block_weight, preferred_element_type=jnp.float32)
        next_sums = part if next_sums is None else next_sums + part
    return (new_residual, next_sums.astype(jnp.bfloat16))


def solution(mesh):
    n_req = mesh.shape["req"]
    n_tp = mesh.shape["tp"]

    def body(*args):
        return local(*args, n_req=n_req, n_tp=n_tp)

    return jax.shard_map(
        body,
        mesh=mesh,
        in_specs=(
            P("req", "tp"),
            P("req", "tp"),
            P("req", "tp", None),
            P("req", "tp", None),
            P("tp", None),
            P(),
            P(None, "tp"),
            P("req", None),
            P("req", None),
            P(),
        ),
        out_specs=(P("req", "tp"), P("req", "tp")),
        check_vma=False,
    )
```

```python
import jax
import jax.numpy as jnp
from jax import lax
from jax.sharding import PartitionSpec as P

QH = 20
KVH = 5
HD = 64
TENANTS = 4
GATHER_SLOTS_MAX = 16
N_CHUNKS = 2


def from_root(block, axis, source):
    block = jnp.where(lax.axis_index(axis) == source, block, jnp.zeros_like(block))
    return lax.psum(block, axis)


def pick_heads(pair_rows, select):
    split_pair = pair_rows.reshape(pair_rows.shape[0], 2, 2, HD)
    key_heads = jnp.einsum(
        "njd,hj->nhd", split_pair[:, :, 0], select, preferred_element_type=jnp.float32
    ).astype(jnp.bfloat16)
    value_heads = jnp.einsum(
        "njd,hj->nhd", split_pair[:, :, 1], select, preferred_element_type=jnp.float32
    ).astype(jnp.bfloat16)
    return (key_heads, value_heads)


def tenant_prefixes(own_slot, owners, n_req):
    slot_rows = own_slot.shape[0]
    if n_req <= GATHER_SLOTS_MAX:
        every_slot = lax.all_gather(own_slot, "req", axis=0, tiled=True)
        return [
            lax.dynamic_slice_in_dim(every_slot, owners[tenant_id] * slot_rows, slot_rows, 0)
            for tenant_id in range(TENANTS)
        ]
    return [from_root(own_slot, "req", owners[tenant_id]) for tenant_id in range(TENANTS)]


def shifted(block, shift, n_tp):
    pairs = [(source, (source + shift) % n_tp) for source in range(n_tp)]
    return lax.ppermute(block, "tp", pairs)


def local(
    residual,
    queries,
    suffix_kv,
    prefix_cache,
    out_weight,
    norm_gain,
    next_query_weight,
    lengths,
    tenant,
    owners,
    n_req,
    n_tp,
):
    row_count = queries.shape[0]
    head_count = queries.shape[1] // HD
    width = residual.shape[1]
    tp_index = lax.axis_index("tp")

    weight_pieces = []
    for shift in range(n_tp):
        target = (tp_index + shift) % n_tp
        piece = lax.dynamic_slice_in_dim(out_weight, target * width, width, 1)
        weight_pieces.append(piece if shift == 0 else shifted(piece, shift, n_tp))

    head_ids = tp_index * head_count + jnp.arange(head_count, dtype=jnp.int32)
    pair_ids = head_ids // (QH // KVH) - tp_index
    select = (pair_ids[:, None] == jnp.arange(2, dtype=jnp.int32)[None, :]).astype(jnp.bfloat16)
    req_lengths = lengths[0]
    req_tenant = tenant[0]
    req_ends = jnp.cumsum(req_lengths)
    req_starts = req_ends - req_lengths
    position = jnp.arange(row_count, dtype=jnp.int32)
    request_ids = jnp.sum((position[:, None] >= req_ends[None, :]).astype(jnp.int32), axis=1)
    member = request_ids[:, None] == jnp.arange(req_lengths.shape[0], dtype=jnp.int32)[None, :]
    row_start = jnp.sum(jnp.where(member, req_starts[None, :], 0), axis=1)
    row_tenant = jnp.sum(jnp.where(member, req_tenant[None, :], 0), axis=1)
    score_scale = HD ** (-0.5)
    query_heads = queries.reshape(row_count, head_count, HD)
    suffix_keys, suffix_values = pick_heads(suffix_kv.reshape(row_count, -1), select)
    own_slot = prefix_cache.reshape(prefix_cache.shape[0], -1)
    prefix_blocks = tenant_prefixes(own_slot, owners, n_req)
    picked = [pick_heads(block_rows, select) for block_rows in prefix_blocks]
    gain = norm_gain.astype(jnp.float32)

    def attend(first, count):
        rows = slice(first, first + count)
        chunk_queries = query_heads[rows]
        chunk_tenant = row_tenant[rows]
        chunk_position = position[rows]
        suffix_scores = (
            jnp.einsum(
                "rhd,khd->hrk", chunk_queries, suffix_keys, preferred_element_type=jnp.float32
            )
            * score_scale
        )
        suffix_mask = (
            (position[None, :] >= row_start[rows][:, None])
            & (position[None, :] <= chunk_position[:, None])
        )[None]
        row_top = jnp.max(jnp.where(suffix_mask, suffix_scores, -jnp.inf), axis=2)
        prefix_scores = []
        for tenant_id in range(TENANTS):
            tenant_mask = (chunk_tenant == tenant_id)[None, :, None]
            scores = (
                jnp.einsum(
                    "rhd,phd->hrp",
                    chunk_queries,
                    picked[tenant_id][0],
                    preferred_element_type=jnp.float32,
                )
                * score_scale
            )
            prefix_scores.append(scores)
            row_top = jnp.maximum(
                row_top, jnp.max(jnp.where(tenant_mask, scores, -jnp.inf), axis=2)
            )
        suffix_weights = jnp.where(
            suffix_mask, jnp.exp(suffix_scores - row_top[:, :, None]), 0.0
        )
        denominator = jnp.sum(suffix_weights, axis=2)
        accumulated = jnp.einsum(
            "hrk,khd->rhd",
            suffix_weights.astype(jnp.bfloat16),
            suffix_values,
            preferred_element_type=jnp.float32,
        )
        for tenant_id in range(TENANTS):
            tenant_mask = (chunk_tenant == tenant_id)[None, :, None]
            prefix_weights = jnp.where(
                tenant_mask, jnp.exp(prefix_scores[tenant_id] - row_top[:, :, None]), 0.0
            )
            denominator = denominator + jnp.sum(prefix_weights, axis=2)
            accumulated = accumulated + jnp.einsum(
                "hrp,phd->rhd",
                prefix_weights.astype(jnp.bfloat16),
                picked[tenant_id][1],
                preferred_element_type=jnp.float32,
            )
        return (
            (accumulated / jnp.transpose(denominator)[:, :, None])
            .astype(jnp.bfloat16)
            .reshape(count, -1)
        )

    def finish(first, count, attended):
        projected = jnp.dot(attended, weight_pieces[0], preferred_element_type=jnp.float32)
        for shift in range(1, n_tp):
            head_block = shifted(attended, shift, n_tp)
            projected = projected + jnp.dot(
                head_block, weight_pieces[shift], preferred_element_type=jnp.float32
            )
        chunk_residual = residual[first:first + count]
        new_residual = (chunk_residual.astype(jnp.float32) + projected).astype(jnp.bfloat16)

        blocks = [new_residual] + [
            shifted(new_residual, shift, n_tp) for shift in range(1, n_tp)
        ]
        widened = [block.astype(jnp.float32) for block in blocks]
        square_sums = sum(jnp.sum(block * block, axis=1, keepdims=True) for block in widened)
        mean_square = square_sums / (width * n_tp)
        scale = lax.rsqrt(mean_square + 1e-05)
        next_sums = None
        for shift in range(n_tp):
            source = (tp_index - shift) % n_tp
            block_gain = lax.dynamic_slice_in_dim(gain, source * width, width, 0)
            block_weight = lax.dynamic_slice_in_dim(next_query_weight, source * width, width, 0)
            normed = (widened[shift] * scale * block_gain).astype(jnp.bfloat16)
            part = jnp.dot(normed, block_weight, preferred_element_type=jnp.float32)
            next_sums = part if next_sums is None else next_sums + part
        return new_residual, next_sums.astype(jnp.bfloat16)

    chunk = row_count // N_CHUNKS if row_count % (8 * N_CHUNKS) == 0 else row_count
    results = []
    for first in range(0, row_count, chunk):
        results.append(finish(first, chunk, attend(first, chunk)))
    if len(results) == 1:
        return results[0]
    return (
        jnp.concatenate([result[0] for result in results], axis=0),
        jnp.concatenate([result[1] for result in results], axis=0),
    )


def solution(mesh):
    n_req = mesh.shape["req"]
    n_tp = mesh.shape["tp"]

    def body(*args):
        return local(*args, n_req=n_req, n_tp=n_tp)

    return jax.shard_map(
        body,
        mesh=mesh,
        in_specs=(
            P("req", "tp"),
            P("req", "tp"),
            P("req", "tp", None),
            P("req", "tp", None),
            P("tp", None),
            P(),
            P(None, "tp"),
            P("req", None),
            P("req", None),
            P(),
        ),
        out_specs=(P("req", "tp"), P("req", "tp")),
        check_vma=False,
    )
```

```python
import jax
import jax.numpy as jnp
from jax import lax
from jax.sharding import PartitionSpec as P

QH = 20
KVH = 5
HD = 64
TENANTS = 4
GATHER_SLOTS_MAX = 16


def from_root(block, axis, source):
    block = jnp.where(lax.axis_index(axis) == source, block, jnp.zeros_like(block))
    return lax.psum(block, axis)


def pick_heads(pair_rows, select):
    split_pair = pair_rows.reshape(pair_rows.shape[0], 2, 2, HD)
    key_heads = jnp.einsum(
        "njd,hj->nhd", split_pair[:, :, 0], select, preferred_element_type=jnp.float32
    ).astype(jnp.bfloat16)
    value_heads = jnp.einsum(
        "njd,hj->nhd", split_pair[:, :, 1], select, preferred_element_type=jnp.float32
    ).astype(jnp.bfloat16)
    return (key_heads, value_heads)


def tenant_prefixes(own_slot, owners, n_req):
    slot_rows = own_slot.shape[0]
    if n_req <= GATHER_SLOTS_MAX:
        every_slot = lax.all_gather(own_slot, "req", axis=0, tiled=True)
        return [
            lax.dynamic_slice_in_dim(every_slot, owners[tenant_id] * slot_rows, slot_rows, 0)
            for tenant_id in range(TENANTS)
        ]
    return [from_root(own_slot, "req", owners[tenant_id]) for tenant_id in range(TENANTS)]


def everyone(block, n_tp):
    copies = jnp.broadcast_to(block[None], (n_tp,) + block.shape)
    return lax.all_to_all(copies, "tp", 0, 0, tiled=False)


def shifted(block, shift, n_tp):
    pairs = [(source, (source + shift) % n_tp) for source in range(n_tp)]
    return lax.ppermute(block, "tp", pairs)


def local(
    residual,
    queries,
    suffix_kv,
    prefix_cache,
    out_weight,
    norm_gain,
    next_query_weight,
    lengths,
    tenant,
    owners,
    n_req,
    n_tp,
):
    row_count = queries.shape[0]
    head_count = queries.shape[1] // HD
    width = residual.shape[1]
    tp_index = lax.axis_index("tp")

    weight_pieces = lax.all_to_all(
        out_weight.reshape(out_weight.shape[0], n_tp, width), "tp", 1, 0, tiled=False
    )

    head_ids = tp_index * head_count + jnp.arange(head_count, dtype=jnp.int32)
    pair_ids = head_ids // (QH // KVH) - tp_index
    select = (pair_ids[:, None] == jnp.arange(2, dtype=jnp.int32)[None, :]).astype(jnp.bfloat16)
    req_lengths = lengths[0]
    req_tenant = tenant[0]
    req_ends = jnp.cumsum(req_lengths)
    req_starts = req_ends - req_lengths
    position = jnp.arange(row_count, dtype=jnp.int32)
    request_ids = jnp.sum((position[:, None] >= req_ends[None, :]).astype(jnp.int32), axis=1)
    member = request_ids[:, None] == jnp.arange(req_lengths.shape[0], dtype=jnp.int32)[None, :]
    row_start = jnp.sum(jnp.where(member, req_starts[None, :], 0), axis=1)
    row_tenant = jnp.sum(jnp.where(member, req_tenant[None, :], 0), axis=1)
    score_scale = HD ** (-0.5)
    query_heads = queries.reshape(row_count, head_count, HD)
    suffix_keys, suffix_values = pick_heads(suffix_kv.reshape(row_count, -1), select)
    suffix_scores = (
        jnp.einsum("rhd,khd->hrk", query_heads, suffix_keys, preferred_element_type=jnp.float32)
        * score_scale
    )
    suffix_mask = (
        (position[None, :] >= row_start[:, None]) & (position[None, :] <= position[:, None])
    )[None]
    own_slot = prefix_cache.reshape(prefix_cache.shape[0], -1)
    prefix_blocks = tenant_prefixes(own_slot, owners, n_req)
    picked = [pick_heads(block_rows, select) for block_rows in prefix_blocks]
    row_top = jnp.max(jnp.where(suffix_mask, suffix_scores, -jnp.inf), axis=2)
    for tenant_id in range(TENANTS):
        tenant_mask = (row_tenant == tenant_id)[None, :, None]
        prefix_scores = (
            jnp.einsum(
                "rhd,phd->hrp",
                query_heads,
                picked[tenant_id][0],
                preferred_element_type=jnp.float32,
            )
            * score_scale
        )
        row_top = jnp.maximum(
            row_top, jnp.max(jnp.where(tenant_mask, prefix_scores, -jnp.inf), axis=2)
        )
    suffix_weights = jnp.where(suffix_mask, jnp.exp(suffix_scores - row_top[:, :, None]), 0.0)
    denominator = jnp.sum(suffix_weights, axis=2)
    accumulated = jnp.einsum(
        "hrk,khd->rhd",
        suffix_weights.astype(jnp.bfloat16),
        suffix_values,
        preferred_element_type=jnp.float32,
    )
    for tenant_id in range(TENANTS):
        tenant_mask = (row_tenant == tenant_id)[None, :, None]
        prefix_scores = (
            jnp.einsum(
                "rhd,phd->hrp",
                query_heads,
                picked[tenant_id][0],
                preferred_element_type=jnp.float32,
            )
            * score_scale
        )
        prefix_weights = jnp.where(tenant_mask, jnp.exp(prefix_scores - row_top[:, :, None]), 0.0)
        denominator = denominator + jnp.sum(prefix_weights, axis=2)
        accumulated = accumulated + jnp.einsum(
            "hrp,phd->rhd",
            prefix_weights.astype(jnp.bfloat16),
            picked[tenant_id][1],
            preferred_element_type=jnp.float32,
        )
    attended = (
        (accumulated / jnp.transpose(denominator)[:, :, None])
        .astype(jnp.bfloat16)
        .reshape(row_count, -1)
    )

    head_blocks = everyone(attended, n_tp)
    projected = None
    for source in range(n_tp):
        part = jnp.dot(head_blocks[source], weight_pieces[source], preferred_element_type=jnp.float32)
        projected = part if projected is None else projected + part
    new_residual = (residual.astype(jnp.float32) + projected).astype(jnp.bfloat16)

    blocks = everyone(new_residual, n_tp)
    widened = [blocks[source].astype(jnp.float32) for source in range(n_tp)]
    square_sums = sum(jnp.sum(block * block, axis=1, keepdims=True) for block in widened)
    mean_square = square_sums / (width * n_tp)
    scale = lax.rsqrt(mean_square + 1e-05)
    gain = norm_gain.astype(jnp.float32)
    next_sums = None
    for source in range(n_tp):
        block_gain = gain[source * width:(source + 1) * width]
        block_weight = next_query_weight[source * width:(source + 1) * width]
        normed = (widened[source] * scale * block_gain).astype(jnp.bfloat16)
        part = jnp.dot(normed, block_weight, preferred_element_type=jnp.float32)
        next_sums = part if next_sums is None else next_sums + part
    return (new_residual, next_sums.astype(jnp.bfloat16))


def solution(mesh):
    n_req = mesh.shape["req"]
    n_tp = mesh.shape["tp"]

    def body(*args):
        return local(*args, n_req=n_req, n_tp=n_tp)

    return jax.shard_map(
        body,
        mesh=mesh,
        in_specs=(
            P("req", "tp"),
            P("req", "tp"),
            P("req", "tp", None),
            P("req", "tp", None),
            P("tp", None),
            P(),
            P(None, "tp"),
            P("req", None),
            P("req", None),
            P(),
        ),
        out_specs=(P("req", "tp"), P("req", "tp")),
        check_vma=False,
    )
```

```python
import jax
import jax.numpy as jnp
from jax import lax
from jax.sharding import PartitionSpec as P

QH = 20
KVH = 5
HD = 64
TENANTS = 4
MOSTLEN = 128
GATHER_SLOTS_MAX = 16


def from_root(block, axis, source):
    block = jnp.where(lax.axis_index(axis) == source, block, jnp.zeros_like(block))
    return lax.psum(block, axis)


def pick_heads(pair_rows, select):
    split_pair = pair_rows.reshape(pair_rows.shape[0], 2, 2, HD)
    key_heads = jnp.einsum(
        "njd,hj->nhd", split_pair[:, :, 0], select, preferred_element_type=jnp.float32
    ).astype(jnp.bfloat16)
    value_heads = jnp.einsum(
        "njd,hj->nhd", split_pair[:, :, 1], select, preferred_element_type=jnp.float32
    ).astype(jnp.bfloat16)
    return (key_heads, value_heads)


def tenant_slots(own_slot, owners, n_req):
    slot_rows = own_slot.shape[0]
    if n_req <= GATHER_SLOTS_MAX:
        gathered = lax.all_gather(own_slot, "req", axis=0, tiled=True)

        def slot_of(tenant_id):
            owner = owners[tenant_id]
            return lax.dynamic_slice_in_dim(gathered, owner * slot_rows, slot_rows, 0)

        return slot_of
    blocks = jnp.stack(
        [from_root(own_slot, "req", owners[tenant_id]) for tenant_id in range(TENANTS)]
    )

    def slot_of(tenant_id):
        return lax.dynamic_index_in_dim(blocks, tenant_id, 0, keepdims=False)

    return slot_of


def shifted(block, shift, n_tp):
    pairs = [(source, (source + shift) % n_tp) for source in range(n_tp)]
    return lax.ppermute(block, "tp", pairs)


def local(
    residual,
    queries,
    suffix_kv,
    prefix_cache,
    out_weight,
    norm_gain,
    next_query_weight,
    lengths,
    tenant,
    owners,
    n_req,
    n_tp,
):
    row_count = queries.shape[0]
    head_count = queries.shape[1] // HD
    width = residual.shape[1]
    tp_index = lax.axis_index("tp")

    weight_pieces = []
    for shift in range(n_tp):
        target = (tp_index + shift) % n_tp
        piece = lax.dynamic_slice_in_dim(out_weight, target * width, width, 1)
        weight_pieces.append(piece if shift == 0 else shifted(piece, shift, n_tp))

    head_ids = tp_index * head_count + jnp.arange(head_count, dtype=jnp.int32)
    pair_ids = head_ids // (QH // KVH) - tp_index
    select = (pair_ids[:, None] == jnp.arange(2, dtype=jnp.int32)[None, :]).astype(jnp.bfloat16)
    req_lengths = lengths[0]
    req_tenant = tenant[0]
    req_ends = jnp.cumsum(req_lengths)
    req_starts = req_ends - req_lengths
    position = jnp.arange(row_count, dtype=jnp.int32)
    request_ids = jnp.sum((position[:, None] >= req_ends[None, :]).astype(jnp.int32), axis=1)
    member = request_ids[:, None] == jnp.arange(req_lengths.shape[0], dtype=jnp.int32)[None, :]
    row_start = jnp.sum(jnp.where(member, req_starts[None, :], 0), axis=1)
    row_tenant = jnp.sum(jnp.where(member, req_tenant[None, :], 0), axis=1)
    score_scale = HD ** (-0.5)
    pair_select = select[None, :, :, None]
    own_slot = prefix_cache.reshape(prefix_cache.shape[0], 2, 2, HD)
    every_slot = tenant_slots(own_slot, owners, n_req)
    suffix_pairs = suffix_kv.reshape(row_count, 2, 2, HD)
    window = min(MOSTLEN, row_count)
    attended = jnp.zeros((row_count, head_count * HD), jnp.bfloat16)
    for request in range(req_lengths.shape[0]):
        first = jnp.minimum(req_starts[request], row_count - window)
        window_queries = lax.dynamic_slice_in_dim(queries, first, window, 0)
        spread = window_queries.reshape(window, head_count, 1, HD) * pair_select
        window_pairs = lax.dynamic_slice_in_dim(suffix_pairs, first, window, 0)
        prefix_pairs = every_slot(req_tenant[request])
        key_position = first + jnp.arange(window, dtype=jnp.int32)
        suffix_mask = (
            (key_position[None, :] >= req_starts[request]) & (key_position[None, :] <= key_position[:, None])
        )[None]
        prefix_scores = (
            jnp.einsum("rhjd,pjd->hrp", spread, prefix_pairs[:, :, 0], preferred_element_type=jnp.float32)
            * score_scale
        )
        suffix_scores = (
            jnp.einsum("rhjd,kjd->hrk", spread, window_pairs[:, :, 0], preferred_element_type=jnp.float32)
            * score_scale
        )
        row_top = jnp.maximum(
            jnp.max(prefix_scores, axis=2),
            jnp.max(jnp.where(suffix_mask, suffix_scores, -jnp.inf), axis=2),
        )
        prefix_weights = jnp.exp(prefix_scores - row_top[:, :, None])
        suffix_weights = jnp.where(suffix_mask, jnp.exp(suffix_scores - row_top[:, :, None]), 0.0)
        denominator = jnp.sum(prefix_weights, axis=2) + jnp.sum(suffix_weights, axis=2)
        both_pairs = jnp.einsum(
            "hrp,pjd->rhjd",
            prefix_weights.astype(jnp.bfloat16),
            prefix_pairs[:, :, 1],
            preferred_element_type=jnp.float32,
        ) + jnp.einsum(
            "hrk,kjd->rhjd",
            suffix_weights.astype(jnp.bfloat16),
            window_pairs[:, :, 1],
            preferred_element_type=jnp.float32,
        )
        accumulated = jnp.sum(jnp.where(pair_select > 0, both_pairs, 0.0), axis=2)
        window_attended = (
            (accumulated / jnp.transpose(denominator)[:, :, None])
            .astype(jnp.bfloat16)
            .reshape(window, -1)
        )
        placed = lax.dynamic_update_slice_in_dim(
            jnp.zeros_like(attended), window_attended, first, 0
        )
        attended = jnp.where((request_ids == request)[:, None], placed, attended)

    projected = jnp.dot(attended, weight_pieces[0], preferred_element_type=jnp.float32)
    for shift in range(1, n_tp):
        head_block = shifted(attended, shift, n_tp)
        projected = projected + jnp.dot(
            head_block, weight_pieces[shift], preferred_element_type=jnp.float32
        )
    new_residual = (residual.astype(jnp.float32) + projected).astype(jnp.bfloat16)

    blocks = [new_residual] + [shifted(new_residual, shift, n_tp) for shift in range(1, n_tp)]
    widened = [block.astype(jnp.float32) for block in blocks]
    square_sums = sum(jnp.sum(block * block, axis=1, keepdims=True) for block in widened)
    mean_square = square_sums / (width * n_tp)
    scale = lax.rsqrt(mean_square + 1e-05)
    gain = norm_gain.astype(jnp.float32)
    next_sums = None
    for shift in range(n_tp):
        source = (tp_index - shift) % n_tp
        block_gain = lax.dynamic_slice_in_dim(gain, source * width, width, 0)
        block_weight = lax.dynamic_slice_in_dim(next_query_weight, source * width, width, 0)
        normed = (widened[shift] * scale * block_gain).astype(jnp.bfloat16)
        part = jnp.dot(normed, block_weight, preferred_element_type=jnp.float32)
        next_sums = part if next_sums is None else next_sums + part
    return (new_residual, next_sums.astype(jnp.bfloat16))


def solution(mesh):
    n_req = mesh.shape["req"]
    n_tp = mesh.shape["tp"]

    def body(*args):
        return local(*args, n_req=n_req, n_tp=n_tp)

    return jax.shard_map(
        body,
        mesh=mesh,
        in_specs=(
            P("req", "tp"),
            P("req", "tp"),
            P("req", "tp", None),
            P("req", "tp", None),
            P("tp", None),
            P(),
            P(None, "tp"),
            P("req", None),
            P("req", None),
            P(),
        ),
        out_specs=(P("req", "tp"), P("req", "tp")),
        check_vma=False,
    )
```

```python
import jax
import jax.numpy as jnp
from jax import lax
from jax.experimental import pallas as pl
from jax.experimental.pallas import tpu as pltpu
from jax.sharding import PartitionSpec as P

QH = 20
KVH = 5
HD = 64
TENANTS = 4
MOSTLEN = 128
GATHER_SLOTS_MAX = 16


def from_root(block, axis, source):
    block = jnp.where(lax.axis_index(axis) == source, block, jnp.zeros_like(block))
    return lax.psum(block, axis)


def pick_heads(pair_rows, select):
    split_pair = pair_rows.reshape(pair_rows.shape[0], 2, 2, HD)
    key_heads = jnp.einsum(
        "njd,hj->nhd", split_pair[:, :, 0], select, preferred_element_type=jnp.float32
    ).astype(jnp.bfloat16)
    value_heads = jnp.einsum(
        "njd,hj->nhd", split_pair[:, :, 1], select, preferred_element_type=jnp.float32
    ).astype(jnp.bfloat16)
    return (key_heads, value_heads)


def tenant_slots(own_slot, owners, n_req):
    if n_req <= GATHER_SLOTS_MAX:
        return lax.all_gather(own_slot, "req", axis=0, tiled=True), owners
    blocks = [from_root(own_slot, "req", owners[tenant_id]) for tenant_id in range(TENANTS)]
    return jnp.concatenate(blocks, axis=0), jnp.arange(TENANTS, dtype=jnp.int32)


def attention_kernel(slot_ref, first_ref, start_ref, query_ref, prefix_ref, suffix_ref, row_ref, out_ref):
    request = pl.program_id(0)
    first = first_ref[request]
    start = start_ref[request]
    spread = query_ref[...]
    prefix_rows = prefix_ref[...]
    suffix_rows = suffix_ref[...]
    contract = (((1,), (1,)), ((), ()))
    score_scale = HD ** (-0.5)
    prefix_scores = lax.dot_general(
        spread, prefix_rows, contract, preferred_element_type=jnp.float32
    ) * score_scale
    suffix_scores = lax.dot_general(
        spread, suffix_rows, contract, preferred_element_type=jnp.float32
    ) * score_scale
    key_position = first + lax.broadcasted_iota(jnp.int32, suffix_scores.shape, 1)
    query_position = first + row_ref[...]
    allowed = (key_position >= start) & (key_position <= query_position)
    suffix_scores = jnp.where(allowed, suffix_scores, -jnp.inf)
    row_top = jnp.maximum(
        jnp.max(prefix_scores, axis=1, keepdims=True),
        jnp.max(suffix_scores, axis=1, keepdims=True),
    )
    prefix_weights = jnp.exp(prefix_scores - row_top)
    suffix_weights = jnp.where(allowed, jnp.exp(suffix_scores - row_top), 0.0)
    denominator = jnp.sum(prefix_weights, axis=1, keepdims=True) + jnp.sum(
        suffix_weights, axis=1, keepdims=True
    )
    accumulated = jnp.dot(
        prefix_weights.astype(jnp.bfloat16), prefix_rows, preferred_element_type=jnp.float32
    ) + jnp.dot(suffix_weights.astype(jnp.bfloat16), suffix_rows, preferred_element_type=jnp.float32)
    out_ref[...] = accumulated / denominator


def window_attention(slot_index, firsts, starts, spread, slots, suffix_windows, query_rows, slot_rows):
    requests, flat_rows, lanes = spread.shape
    window = suffix_windows.shape[1]
    grid_spec = pltpu.PrefetchScalarGridSpec(
        num_scalar_prefetch=3,
        grid=(requests,),
        in_specs=[
            pl.BlockSpec((None, flat_rows, lanes), lambda k, slot, first, start: (k, 0, 0)),
            pl.BlockSpec((slot_rows, lanes), lambda k, slot, first, start: (slot[k], 0)),
            pl.BlockSpec((None, window, lanes), lambda k, slot, first, start: (k, 0, 0)),
            pl.BlockSpec((flat_rows, 1), lambda k, slot, first, start: (0, 0)),
        ],
        out_specs=pl.BlockSpec((None, flat_rows, lanes), lambda k, slot, first, start: (k, 0, 0)),
    )
    return pl.pallas_call(
        attention_kernel,
        grid_spec=grid_spec,
        out_shape=jax.ShapeDtypeStruct((requests, flat_rows, lanes), jnp.float32),
    )(slot_index, firsts, starts, spread, slots, suffix_windows, query_rows)


def shifted(block, shift, n_tp):
    pairs = [(source, (source + shift) % n_tp) for source in range(n_tp)]
    return lax.ppermute(block, "tp", pairs)


def local(
    residual,
    queries,
    suffix_kv,
    prefix_cache,
    out_weight,
    norm_gain,
    next_query_weight,
    lengths,
    tenant,
    owners,
    n_req,
    n_tp,
):
    row_count = queries.shape[0]
    head_count = queries.shape[1] // HD
    width = residual.shape[1]
    tp_index = lax.axis_index("tp")

    weight_pieces = []
    for shift in range(n_tp):
        target = (tp_index + shift) % n_tp
        piece = lax.dynamic_slice_in_dim(out_weight, target * width, width, 1)
        weight_pieces.append(piece if shift == 0 else shifted(piece, shift, n_tp))

    head_ids = tp_index * head_count + jnp.arange(head_count, dtype=jnp.int32)
    pair_ids = head_ids // (QH // KVH) - tp_index
    select = (pair_ids[:, None] == jnp.arange(2, dtype=jnp.int32)[None, :]).astype(jnp.bfloat16)
    req_lengths = lengths[0]
    req_tenant = tenant[0]
    req_ends = jnp.cumsum(req_lengths)
    req_starts = req_ends - req_lengths
    position = jnp.arange(row_count, dtype=jnp.int32)
    request_ids = jnp.sum((position[:, None] >= req_ends[None, :]).astype(jnp.int32), axis=1)
    member = request_ids[:, None] == jnp.arange(req_lengths.shape[0], dtype=jnp.int32)[None, :]
    row_start = jnp.sum(jnp.where(member, req_starts[None, :], 0), axis=1)
    row_tenant = jnp.sum(jnp.where(member, req_tenant[None, :], 0), axis=1)
    score_scale = HD ** (-0.5)
    own_slot = prefix_cache.reshape(prefix_cache.shape[0], -1)
    slots, slot_of_tenant = tenant_slots(own_slot, owners, n_req)
    suffix_rows = suffix_kv.reshape(row_count, -1)
    window = min(MOSTLEN, row_count)
    firsts = jnp.minimum(req_starts, row_count - window).astype(jnp.int32)
    zeros = jnp.zeros((window, head_count, HD), queries.dtype)
    spreads = []
    suffix_windows = []
    for request in range(req_lengths.shape[0]):
        window_queries = lax.dynamic_slice_in_dim(queries, firsts[request], window, 0)
        window_queries = window_queries.reshape(window, head_count, HD)
        spread = jnp.concatenate(
            [
                window_queries * select[None, :, 0:1],
                zeros,
                window_queries * select[None, :, 1:2],
                zeros,
            ],
            axis=2,
        )
        spreads.append(spread.reshape(window * head_count, 4 * HD))
        suffix_windows.append(lax.dynamic_slice_in_dim(suffix_rows, firsts[request], window, 0))
    query_rows = (jnp.arange(window * head_count, dtype=jnp.int32) // head_count)[:, None]
    slot_index = slot_of_tenant[req_tenant].astype(jnp.int32)
    results = window_attention(
        slot_index,
        firsts,
        req_starts.astype(jnp.int32),
        jnp.stack(spreads),
        slots,
        jnp.stack(suffix_windows),
        query_rows,
        own_slot.shape[0],
    ).reshape(-1, window, head_count, 4 * HD)
    value_of_pair = jnp.where(
        select[None, None, :, 0:1] > 0, results[..., HD:2 * HD], results[..., 3 * HD:]
    )
    attended = jnp.zeros((row_count, head_count * HD), jnp.bfloat16)
    for request in range(req_lengths.shape[0]):
        window_attended = value_of_pair[request].astype(jnp.bfloat16).reshape(window, -1)
        placed = lax.dynamic_update_slice_in_dim(
            jnp.zeros_like(attended), window_attended, firsts[request], 0
        )
        attended = jnp.where((request_ids == request)[:, None], placed, attended)

    projected = jnp.dot(attended, weight_pieces[0], preferred_element_type=jnp.float32)
    for shift in range(1, n_tp):
        head_block = shifted(attended, shift, n_tp)
        projected = projected + jnp.dot(
            head_block, weight_pieces[shift], preferred_element_type=jnp.float32
        )
    new_residual = (residual.astype(jnp.float32) + projected).astype(jnp.bfloat16)

    blocks = [new_residual] + [shifted(new_residual, shift, n_tp) for shift in range(1, n_tp)]
    widened = [block.astype(jnp.float32) for block in blocks]
    square_sums = sum(jnp.sum(block * block, axis=1, keepdims=True) for block in widened)
    mean_square = square_sums / (width * n_tp)
    scale = lax.rsqrt(mean_square + 1e-05)
    gain = norm_gain.astype(jnp.float32)
    next_sums = None
    for shift in range(n_tp):
        source = (tp_index - shift) % n_tp
        block_gain = lax.dynamic_slice_in_dim(gain, source * width, width, 0)
        block_weight = lax.dynamic_slice_in_dim(next_query_weight, source * width, width, 0)
        normed = (widened[shift] * scale * block_gain).astype(jnp.bfloat16)
        part = jnp.dot(normed, block_weight, preferred_element_type=jnp.float32)
        next_sums = part if next_sums is None else next_sums + part
    return (new_residual, next_sums.astype(jnp.bfloat16))


def solution(mesh):
    n_req = mesh.shape["req"]
    n_tp = mesh.shape["tp"]

    def body(*args):
        return local(*args, n_req=n_req, n_tp=n_tp)

    return jax.shard_map(
        body,
        mesh=mesh,
        in_specs=(
            P("req", "tp"),
            P("req", "tp"),
            P("req", "tp", None),
            P("req", "tp", None),
            P("tp", None),
            P(),
            P(None, "tp"),
            P("req", None),
            P("req", None),
            P(),
        ),
        out_specs=(P("req", "tp"), P("req", "tp")),
        check_vma=False,
    )
```

```python
import jax
import jax.numpy as jnp
from jax import lax
from jax.experimental import pallas as pl
from jax.experimental.pallas import tpu as pltpu
from jax.sharding import PartitionSpec as P

QH = 20
KVH = 5
HD = 64
TENANTS = 4
MOSTLEN = 128
GATHER_SLOTS_MAX = 16


def from_root(block, axis, source):
    block = jnp.where(lax.axis_index(axis) == source, block, jnp.zeros_like(block))
    return lax.psum(block, axis)


def pick_heads(pair_rows, select):
    split_pair = pair_rows.reshape(pair_rows.shape[0], 2, 2, HD)
    key_heads = jnp.einsum(
        "njd,hj->nhd", split_pair[:, :, 0], select, preferred_element_type=jnp.float32
    ).astype(jnp.bfloat16)
    value_heads = jnp.einsum(
        "njd,hj->nhd", split_pair[:, :, 1], select, preferred_element_type=jnp.float32
    ).astype(jnp.bfloat16)
    return (key_heads, value_heads)


def tenant_slots(own_slot, owners, n_req):
    if n_req <= GATHER_SLOTS_MAX:
        return lax.all_gather(own_slot, "req", axis=0, tiled=True), owners
    blocks = [from_root(own_slot, "req", owners[tenant_id]) for tenant_id in range(TENANTS)]
    return jnp.concatenate(blocks, axis=0), jnp.arange(TENANTS, dtype=jnp.int32)


def attention_kernel(
    slot_ref, first_ref, start_ref, query_ref, prefix_ref, suffix_ref, row_ref, pair_ref, out_ref
):
    request = pl.program_id(0)
    first = first_ref[request]
    start = start_ref[request]
    spread = query_ref[...]
    prefix_rows = prefix_ref[...]
    suffix_rows = suffix_ref[...]
    contract = (((1,), (1,)), ((), ()))
    score_scale = HD ** (-0.5)
    prefix_scores = lax.dot_general(
        spread, prefix_rows, contract, preferred_element_type=jnp.float32
    ) * score_scale
    suffix_scores = lax.dot_general(
        spread, suffix_rows, contract, preferred_element_type=jnp.float32
    ) * score_scale
    key_position = first + lax.broadcasted_iota(jnp.int32, suffix_scores.shape, 1)
    query_position = first + row_ref[...]
    allowed = (key_position >= start) & (key_position <= query_position)
    suffix_scores = jnp.where(allowed, suffix_scores, -jnp.inf)
    row_top = jnp.maximum(
        jnp.max(prefix_scores, axis=1, keepdims=True),
        jnp.max(suffix_scores, axis=1, keepdims=True),
    )
    prefix_weights = jnp.exp(prefix_scores - row_top)
    suffix_weights = jnp.where(allowed, jnp.exp(suffix_scores - row_top), 0.0)
    denominator = jnp.sum(prefix_weights, axis=1, keepdims=True) + jnp.sum(
        suffix_weights, axis=1, keepdims=True
    )
    accumulated = jnp.dot(
        prefix_weights.astype(jnp.bfloat16), prefix_rows, preferred_element_type=jnp.float32
    ) + jnp.dot(suffix_weights.astype(jnp.bfloat16), suffix_rows, preferred_element_type=jnp.float32)
    attended = accumulated / denominator
    first_pair = attended[:, HD:2 * HD]
    second_pair = attended[:, 3 * HD:]
    out_ref[...] = jnp.where(pair_ref[...] > 0, second_pair, first_pair).astype(out_ref.dtype)


def window_attention(
    slot_index, firsts, starts, spread, slots, suffix_windows, query_rows, row_pairs, slot_rows
):
    requests, flat_rows, lanes = spread.shape
    window = suffix_windows.shape[1]
    grid_spec = pltpu.PrefetchScalarGridSpec(
        num_scalar_prefetch=3,
        grid=(requests,),
        in_specs=[
            pl.BlockSpec((None, flat_rows, lanes), lambda k, slot, first, start: (k, 0, 0)),
            pl.BlockSpec((slot_rows, lanes), lambda k, slot, first, start: (slot[k], 0)),
            pl.BlockSpec((None, window, lanes), lambda k, slot, first, start: (k, 0, 0)),
            pl.BlockSpec((flat_rows, 1), lambda k, slot, first, start: (0, 0)),
            pl.BlockSpec((flat_rows, 1), lambda k, slot, first, start: (0, 0)),
        ],
        out_specs=pl.BlockSpec((None, flat_rows, HD), lambda k, slot, first, start: (k, 0, 0)),
    )
    return pl.pallas_call(
        attention_kernel,
        grid_spec=grid_spec,
        out_shape=jax.ShapeDtypeStruct((requests, flat_rows, HD), jnp.bfloat16),
    )(slot_index, firsts, starts, spread, slots, suffix_windows, query_rows, row_pairs)


def shifted(block, shift, n_tp):
    pairs = [(source, (source + shift) % n_tp) for source in range(n_tp)]
    return lax.ppermute(block, "tp", pairs)


def local(
    residual,
    queries,
    suffix_kv,
    prefix_cache,
    out_weight,
    norm_gain,
    next_query_weight,
    lengths,
    tenant,
    owners,
    n_req,
    n_tp,
):
    row_count = queries.shape[0]
    head_count = queries.shape[1] // HD
    width = residual.shape[1]
    tp_index = lax.axis_index("tp")

    weight_pieces = []
    for shift in range(n_tp):
        target = (tp_index + shift) % n_tp
        piece = lax.dynamic_slice_in_dim(out_weight, target * width, width, 1)
        weight_pieces.append(piece if shift == 0 else shifted(piece, shift, n_tp))

    head_ids = tp_index * head_count + jnp.arange(head_count, dtype=jnp.int32)
    pair_ids = head_ids // (QH // KVH) - tp_index
    select = (pair_ids[:, None] == jnp.arange(2, dtype=jnp.int32)[None, :]).astype(jnp.bfloat16)
    req_lengths = lengths[0]
    req_tenant = tenant[0]
    req_ends = jnp.cumsum(req_lengths)
    req_starts = req_ends - req_lengths
    position = jnp.arange(row_count, dtype=jnp.int32)
    request_ids = jnp.sum((position[:, None] >= req_ends[None, :]).astype(jnp.int32), axis=1)
    member = request_ids[:, None] == jnp.arange(req_lengths.shape[0], dtype=jnp.int32)[None, :]
    row_start = jnp.sum(jnp.where(member, req_starts[None, :], 0), axis=1)
    row_tenant = jnp.sum(jnp.where(member, req_tenant[None, :], 0), axis=1)
    score_scale = HD ** (-0.5)
    own_slot = prefix_cache.reshape(prefix_cache.shape[0], -1)
    slots, slot_of_tenant = tenant_slots(own_slot, owners, n_req)
    suffix_rows = suffix_kv.reshape(row_count, -1)
    window = min(MOSTLEN, row_count)
    firsts = jnp.minimum(req_starts, row_count - window).astype(jnp.int32)
    zeros = jnp.zeros((head_count, window, HD), queries.dtype)
    head_select = jnp.transpose(select)[:, :, None, None]
    spreads = []
    suffix_windows = []
    for request in range(req_lengths.shape[0]):
        window_queries = lax.dynamic_slice_in_dim(queries, firsts[request], window, 0)
        window_queries = jnp.transpose(window_queries.reshape(window, head_count, HD), (1, 0, 2))
        spread = jnp.concatenate(
            [window_queries * head_select[0], zeros, window_queries * head_select[1], zeros],
            axis=2,
        )
        spreads.append(spread.reshape(head_count * window, 4 * HD))
        suffix_windows.append(lax.dynamic_slice_in_dim(suffix_rows, firsts[request], window, 0))
    query_rows = (jnp.arange(head_count * window, dtype=jnp.int32) % window)[:, None]
    row_pairs = jnp.repeat(pair_ids.astype(jnp.int32), window)[:, None]
    slot_index = slot_of_tenant[req_tenant].astype(jnp.int32)
    results = window_attention(
        slot_index,
        firsts,
        req_starts.astype(jnp.int32),
        jnp.stack(spreads),
        slots,
        jnp.stack(suffix_windows),
        query_rows,
        row_pairs,
        own_slot.shape[0],
    ).reshape(-1, head_count, window, HD)
    attended = jnp.zeros((row_count, head_count * HD), jnp.bfloat16)
    for request in range(req_lengths.shape[0]):
        window_attended = jnp.transpose(results[request], (1, 0, 2)).reshape(window, -1)
        placed = lax.dynamic_update_slice_in_dim(
            jnp.zeros_like(attended), window_attended, firsts[request], 0
        )
        attended = jnp.where((request_ids == request)[:, None], placed, attended)

    projected = jnp.dot(attended, weight_pieces[0], preferred_element_type=jnp.float32)
    for shift in range(1, n_tp):
        head_block = shifted(attended, shift, n_tp)
        projected = projected + jnp.dot(
            head_block, weight_pieces[shift], preferred_element_type=jnp.float32
        )
    new_residual = (residual.astype(jnp.float32) + projected).astype(jnp.bfloat16)

    blocks = [new_residual] + [shifted(new_residual, shift, n_tp) for shift in range(1, n_tp)]
    widened = [block.astype(jnp.float32) for block in blocks]
    square_sums = sum(jnp.sum(block * block, axis=1, keepdims=True) for block in widened)
    mean_square = square_sums / (width * n_tp)
    scale = lax.rsqrt(mean_square + 1e-05)
    gain = norm_gain.astype(jnp.float32)
    next_sums = None
    for shift in range(n_tp):
        source = (tp_index - shift) % n_tp
        block_gain = lax.dynamic_slice_in_dim(gain, source * width, width, 0)
        block_weight = lax.dynamic_slice_in_dim(next_query_weight, source * width, width, 0)
        normed = (widened[shift] * scale * block_gain).astype(jnp.bfloat16)
        part = jnp.dot(normed, block_weight, preferred_element_type=jnp.float32)
        next_sums = part if next_sums is None else next_sums + part
    return (new_residual, next_sums.astype(jnp.bfloat16))


def solution(mesh):
    n_req = mesh.shape["req"]
    n_tp = mesh.shape["tp"]

    def body(*args):
        return local(*args, n_req=n_req, n_tp=n_tp)

    return jax.shard_map(
        body,
        mesh=mesh,
        in_specs=(
            P("req", "tp"),
            P("req", "tp"),
            P("req", "tp", None),
            P("req", "tp", None),
            P("tp", None),
            P(),
            P(None, "tp"),
            P("req", None),
            P("req", None),
            P(),
        ),
        out_specs=(P("req", "tp"), P("req", "tp")),
        check_vma=False,
    )
```

```python
import jax
import jax.numpy as jnp
from jax import lax
from jax.experimental import pallas as pl
from jax.experimental.pallas import tpu as pltpu
from jax.sharding import PartitionSpec as P

QH = 20
KVH = 5
HD = 64
TENANTS = 4
MOSTLEN = 128
GATHER_SLOTS_MAX = 16


def from_root(block, axis, source):
    block = jnp.where(lax.axis_index(axis) == source, block, jnp.zeros_like(block))
    return lax.psum(block, axis)


def pick_heads(pair_rows, select):
    split_pair = pair_rows.reshape(pair_rows.shape[0], 2, 2, HD)
    key_heads = jnp.einsum(
        "njd,hj->nhd", split_pair[:, :, 0], select, preferred_element_type=jnp.float32
    ).astype(jnp.bfloat16)
    value_heads = jnp.einsum(
        "njd,hj->nhd", split_pair[:, :, 1], select, preferred_element_type=jnp.float32
    ).astype(jnp.bfloat16)
    return (key_heads, value_heads)


def tenant_slots(own_slot, owners, n_req):
    if n_req <= GATHER_SLOTS_MAX:
        return lax.all_gather(own_slot, "req", axis=0, tiled=True), owners
    blocks = [from_root(own_slot, "req", owners[tenant_id]) for tenant_id in range(TENANTS)]
    return jnp.concatenate(blocks, axis=0), jnp.arange(TENANTS, dtype=jnp.int32)


def attention_kernel(
    slot_ref, first_ref, start_ref, query_ref, prefix_ref, suffix_ref, row_ref, pair_ref, out_ref
):
    request = pl.program_id(0)
    first = first_ref[request]
    start = start_ref[request]
    spread = query_ref[...]
    prefix_rows = prefix_ref[...]
    suffix_rows = suffix_ref[...]
    contract = (((1,), (1,)), ((), ()))
    score_scale = HD ** (-0.5)
    prefix_scores = lax.dot_general(
        spread, prefix_rows, contract, preferred_element_type=jnp.float32
    ) * score_scale
    suffix_scores = lax.dot_general(
        spread, suffix_rows, contract, preferred_element_type=jnp.float32
    ) * score_scale
    key_position = first + lax.broadcasted_iota(jnp.int32, suffix_scores.shape, 1)
    query_position = first + row_ref[...]
    allowed = (key_position >= start) & (key_position <= query_position)
    suffix_scores = jnp.where(allowed, suffix_scores, -jnp.inf)
    row_top = jnp.maximum(
        jnp.max(prefix_scores, axis=1, keepdims=True),
        jnp.max(suffix_scores, axis=1, keepdims=True),
    )
    prefix_weights = jnp.exp(prefix_scores - row_top)
    suffix_weights = jnp.where(allowed, jnp.exp(suffix_scores - row_top), 0.0)
    denominator = jnp.sum(prefix_weights, axis=1, keepdims=True) + jnp.sum(
        suffix_weights, axis=1, keepdims=True
    )
    accumulated = jnp.dot(
        prefix_weights.astype(jnp.bfloat16), prefix_rows, preferred_element_type=jnp.float32
    ) + jnp.dot(suffix_weights.astype(jnp.bfloat16), suffix_rows, preferred_element_type=jnp.float32)
    attended = accumulated / denominator
    first_pair = attended[:, HD:2 * HD]
    second_pair = attended[:, 3 * HD:]
    picked = jnp.where(pair_ref[...] > 0, second_pair, first_pair).astype(out_ref.dtype)
    window = out_ref.shape[0]
    for head in range(out_ref.shape[1] // HD):
        out_ref[:, head * HD:(head + 1) * HD] = picked[head * window:(head + 1) * window]


def window_attention(
    slot_index, firsts, starts, spread, slots, suffix_windows, query_rows, row_pairs, slot_rows
):
    requests, flat_rows, lanes = spread.shape
    window = suffix_windows.shape[1]
    head_count = flat_rows // window
    grid_spec = pltpu.PrefetchScalarGridSpec(
        num_scalar_prefetch=3,
        grid=(requests,),
        in_specs=[
            pl.BlockSpec((None, flat_rows, lanes), lambda k, slot, first, start: (k, 0, 0)),
            pl.BlockSpec((slot_rows, lanes), lambda k, slot, first, start: (slot[k], 0)),
            pl.BlockSpec((None, window, lanes), lambda k, slot, first, start: (k, 0, 0)),
            pl.BlockSpec((flat_rows, 1), lambda k, slot, first, start: (0, 0)),
            pl.BlockSpec((flat_rows, 1), lambda k, slot, first, start: (0, 0)),
        ],
        out_specs=pl.BlockSpec((None, window, head_count * HD), lambda k, slot, first, start: (k, 0, 0)),
    )
    return pl.pallas_call(
        attention_kernel,
        grid_spec=grid_spec,
        out_shape=jax.ShapeDtypeStruct((requests, window, head_count * HD), jnp.bfloat16),
    )(slot_index, firsts, starts, spread, slots, suffix_windows, query_rows, row_pairs)


def shifted(block, shift, n_tp):
    pairs = [(source, (source + shift) % n_tp) for source in range(n_tp)]
    return lax.ppermute(block, "tp", pairs)


def local(
    residual,
    queries,
    suffix_kv,
    prefix_cache,
    out_weight,
    norm_gain,
    next_query_weight,
    lengths,
    tenant,
    owners,
    n_req,
    n_tp,
):
    row_count = queries.shape[0]
    head_count = queries.shape[1] // HD
    width = residual.shape[1]
    tp_index = lax.axis_index("tp")

    weight_pieces = []
    for shift in range(n_tp):
        target = (tp_index + shift) % n_tp
        piece = lax.dynamic_slice_in_dim(out_weight, target * width, width, 1)
        weight_pieces.append(piece if shift == 0 else shifted(piece, shift, n_tp))

    head_ids = tp_index * head_count + jnp.arange(head_count, dtype=jnp.int32)
    pair_ids = head_ids // (QH // KVH) - tp_index
    select = (pair_ids[:, None] == jnp.arange(2, dtype=jnp.int32)[None, :]).astype(jnp.bfloat16)
    req_lengths = lengths[0]
    req_tenant = tenant[0]
    req_ends = jnp.cumsum(req_lengths)
    req_starts = req_ends - req_lengths
    position = jnp.arange(row_count, dtype=jnp.int32)
    request_ids = jnp.sum((position[:, None] >= req_ends[None, :]).astype(jnp.int32), axis=1)
    member = request_ids[:, None] == jnp.arange(req_lengths.shape[0], dtype=jnp.int32)[None, :]
    row_start = jnp.sum(jnp.where(member, req_starts[None, :], 0), axis=1)
    row_tenant = jnp.sum(jnp.where(member, req_tenant[None, :], 0), axis=1)
    score_scale = HD ** (-0.5)
    own_slot = prefix_cache.reshape(prefix_cache.shape[0], -1)
    slots, slot_of_tenant = tenant_slots(own_slot, owners, n_req)
    suffix_rows = suffix_kv.reshape(row_count, -1)
    window = min(MOSTLEN, row_count)
    firsts = jnp.minimum(req_starts, row_count - window).astype(jnp.int32)
    zeros = jnp.zeros((head_count, window, HD), queries.dtype)
    head_select = jnp.transpose(select)[:, :, None, None]
    spreads = []
    suffix_windows = []
    for request in range(req_lengths.shape[0]):
        window_queries = lax.dynamic_slice_in_dim(queries, firsts[request], window, 0)
        window_queries = jnp.transpose(window_queries.reshape(window, head_count, HD), (1, 0, 2))
        spread = jnp.concatenate(
            [window_queries * head_select[0], zeros, window_queries * head_select[1], zeros],
            axis=2,
        )
        spreads.append(spread.reshape(head_count * window, 4 * HD))
        suffix_windows.append(lax.dynamic_slice_in_dim(suffix_rows, firsts[request], window, 0))
    query_rows = (jnp.arange(head_count * window, dtype=jnp.int32) % window)[:, None]
    row_pairs = jnp.repeat(pair_ids.astype(jnp.int32), window)[:, None]
    slot_index = slot_of_tenant[req_tenant].astype(jnp.int32)
    results = window_attention(
        slot_index,
        firsts,
        req_starts.astype(jnp.int32),
        jnp.stack(spreads),
        slots,
        jnp.stack(suffix_windows),
        query_rows,
        row_pairs,
        own_slot.shape[0],
    ).reshape(-1, head_count * HD)
    source_rows = request_ids * window + position - firsts[request_ids]
    attended = jnp.take(results, source_rows, axis=0)

    projected = jnp.dot(attended, weight_pieces[0], preferred_element_type=jnp.float32)
    for shift in range(1, n_tp):
        head_block = shifted(attended, shift, n_tp)
        projected = projected + jnp.dot(
            head_block, weight_pieces[shift], preferred_element_type=jnp.float32
        )
    new_residual = (residual.astype(jnp.float32) + projected).astype(jnp.bfloat16)

    blocks = [new_residual] + [shifted(new_residual, shift, n_tp) for shift in range(1, n_tp)]
    widened = [block.astype(jnp.float32) for block in blocks]
    square_sums = sum(jnp.sum(block * block, axis=1, keepdims=True) for block in widened)
    mean_square = square_sums / (width * n_tp)
    scale = lax.rsqrt(mean_square + 1e-05)
    gain = norm_gain.astype(jnp.float32)
    next_sums = None
    for shift in range(n_tp):
        source = (tp_index - shift) % n_tp
        block_gain = lax.dynamic_slice_in_dim(gain, source * width, width, 0)
        block_weight = lax.dynamic_slice_in_dim(next_query_weight, source * width, width, 0)
        normed = (widened[shift] * scale * block_gain).astype(jnp.bfloat16)
        part = jnp.dot(normed, block_weight, preferred_element_type=jnp.float32)
        next_sums = part if next_sums is None else next_sums + part
    return (new_residual, next_sums.astype(jnp.bfloat16))


def solution(mesh):
    n_req = mesh.shape["req"]
    n_tp = mesh.shape["tp"]

    def body(*args):
        return local(*args, n_req=n_req, n_tp=n_tp)

    return jax.shard_map(
        body,
        mesh=mesh,
        in_specs=(
            P("req", "tp"),
            P("req", "tp"),
            P("req", "tp", None),
            P("req", "tp", None),
            P("tp", None),
            P(),
            P(None, "tp"),
            P("req", None),
            P("req", None),
            P(),
        ),
        out_specs=(P("req", "tp"), P("req", "tp")),
        check_vma=False,
    )
```

```python
import jax
import jax.numpy as jnp
from jax import lax
from jax.experimental import pallas as pl
from jax.experimental.pallas import tpu as pltpu
from jax.sharding import PartitionSpec as P

QH = 20
KVH = 5
HD = 64
TENANTS = 4
MOSTLEN = 128
GATHER_SLOTS_MAX = 16


def from_root(block, axis, source):
    block = jnp.where(lax.axis_index(axis) == source, block, jnp.zeros_like(block))
    return lax.psum(block, axis)


def pick_heads(pair_rows, select):
    split_pair = pair_rows.reshape(pair_rows.shape[0], 2, 2, HD)
    key_heads = jnp.einsum(
        "njd,hj->nhd", split_pair[:, :, 0], select, preferred_element_type=jnp.float32
    ).astype(jnp.bfloat16)
    value_heads = jnp.einsum(
        "njd,hj->nhd", split_pair[:, :, 1], select, preferred_element_type=jnp.float32
    ).astype(jnp.bfloat16)
    return (key_heads, value_heads)


def tenant_slots(own_slot, owners, n_req):
    if n_req <= GATHER_SLOTS_MAX:
        return lax.all_gather(own_slot, "req", axis=0, tiled=True), owners
    blocks = [from_root(own_slot, "req", owners[tenant_id]) for tenant_id in range(TENANTS)]
    return jnp.concatenate(blocks, axis=0), jnp.arange(TENANTS, dtype=jnp.int32)


def attention_kernel(
    slot_ref, first_ref, start_ref, query_ref, prefix_ref, suffix_ref, row_ref, pair_ref, out_ref
):
    request = pl.program_id(0)
    first = first_ref[request]
    start = start_ref[request]
    spread = query_ref[...]
    pair_lanes = 2 * HD
    prefix_keys = prefix_ref[:, :pair_lanes]
    prefix_values = prefix_ref[:, pair_lanes:]
    suffix_keys = suffix_ref[:, :pair_lanes]
    suffix_values = suffix_ref[:, pair_lanes:]
    contract = (((1,), (1,)), ((), ()))
    score_scale = HD ** (-0.5)
    prefix_scores = lax.dot_general(
        spread, prefix_keys, contract, preferred_element_type=jnp.float32
    ) * score_scale
    suffix_scores = lax.dot_general(
        spread, suffix_keys, contract, preferred_element_type=jnp.float32
    ) * score_scale
    key_position = first + lax.broadcasted_iota(jnp.int32, suffix_scores.shape, 1)
    query_position = first + row_ref[...]
    allowed = (key_position >= start) & (key_position <= query_position)
    suffix_scores = jnp.where(allowed, suffix_scores, -jnp.inf)
    row_top = jnp.maximum(
        jnp.max(prefix_scores, axis=1, keepdims=True),
        jnp.max(suffix_scores, axis=1, keepdims=True),
    )
    prefix_weights = jnp.exp(prefix_scores - row_top)
    suffix_weights = jnp.where(allowed, jnp.exp(suffix_scores - row_top), 0.0)
    denominator = jnp.sum(prefix_weights, axis=1, keepdims=True) + jnp.sum(
        suffix_weights, axis=1, keepdims=True
    )
    accumulated = jnp.dot(
        prefix_weights.astype(jnp.bfloat16), prefix_values, preferred_element_type=jnp.float32
    ) + jnp.dot(
        suffix_weights.astype(jnp.bfloat16), suffix_values, preferred_element_type=jnp.float32
    )
    attended = accumulated / denominator
    first_pair = attended[:, :HD]
    second_pair = attended[:, HD:]
    out_ref[...] = jnp.where(pair_ref[...] > 0, second_pair, first_pair).astype(out_ref.dtype)


def window_attention(
    slot_index, firsts, starts, spread, slots, suffix_windows, query_rows, row_pairs, slot_rows
):
    requests, flat_rows, query_lanes = spread.shape
    window = suffix_windows.shape[1]
    lanes = slots.shape[1]
    grid_spec = pltpu.PrefetchScalarGridSpec(
        num_scalar_prefetch=3,
        grid=(requests,),
        in_specs=[
            pl.BlockSpec((None, flat_rows, query_lanes), lambda k, slot, first, start: (k, 0, 0)),
            pl.BlockSpec((slot_rows, lanes), lambda k, slot, first, start: (slot[k], 0)),
            pl.BlockSpec((None, window, lanes), lambda k, slot, first, start: (k, 0, 0)),
            pl.BlockSpec((flat_rows, 1), lambda k, slot, first, start: (0, 0)),
            pl.BlockSpec((flat_rows, 1), lambda k, slot, first, start: (0, 0)),
        ],
        out_specs=pl.BlockSpec((None, flat_rows, HD), lambda k, slot, first, start: (k, 0, 0)),
    )
    return pl.pallas_call(
        attention_kernel,
        grid_spec=grid_spec,
        out_shape=jax.ShapeDtypeStruct((requests, flat_rows, HD), jnp.bfloat16),
    )(slot_index, firsts, starts, spread, slots, suffix_windows, query_rows, row_pairs)


def shifted(block, shift, n_tp):
    pairs = [(source, (source + shift) % n_tp) for source in range(n_tp)]
    return lax.ppermute(block, "tp", pairs)


def local(
    residual,
    queries,
    suffix_kv,
    prefix_cache,
    out_weight,
    norm_gain,
    next_query_weight,
    lengths,
    tenant,
    owners,
    n_req,
    n_tp,
):
    row_count = queries.shape[0]
    head_count = queries.shape[1] // HD
    width = residual.shape[1]
    tp_index = lax.axis_index("tp")

    weight_pieces = []
    for shift in range(n_tp):
        target = (tp_index + shift) % n_tp
        piece = lax.dynamic_slice_in_dim(out_weight, target * width, width, 1)
        weight_pieces.append(piece if shift == 0 else shifted(piece, shift, n_tp))

    head_ids = tp_index * head_count + jnp.arange(head_count, dtype=jnp.int32)
    pair_ids = head_ids // (QH // KVH) - tp_index
    select = (pair_ids[:, None] == jnp.arange(2, dtype=jnp.int32)[None, :]).astype(jnp.bfloat16)
    req_lengths = lengths[0]
    req_tenant = tenant[0]
    req_ends = jnp.cumsum(req_lengths)
    req_starts = req_ends - req_lengths
    position = jnp.arange(row_count, dtype=jnp.int32)
    request_ids = jnp.sum((position[:, None] >= req_ends[None, :]).astype(jnp.int32), axis=1)
    member = request_ids[:, None] == jnp.arange(req_lengths.shape[0], dtype=jnp.int32)[None, :]
    row_start = jnp.sum(jnp.where(member, req_starts[None, :], 0), axis=1)
    row_tenant = jnp.sum(jnp.where(member, req_tenant[None, :], 0), axis=1)
    score_scale = HD ** (-0.5)
    own_slot = jnp.transpose(
        prefix_cache.reshape(prefix_cache.shape[0], 2, 2, HD), (0, 2, 1, 3)
    ).reshape(prefix_cache.shape[0], -1)
    slots, slot_of_tenant = tenant_slots(own_slot, owners, n_req)
    suffix_rows = jnp.transpose(suffix_kv.reshape(row_count, 2, 2, HD), (0, 2, 1, 3)).reshape(
        row_count, -1
    )
    window = min(MOSTLEN, row_count)
    firsts = jnp.minimum(req_starts, row_count - window).astype(jnp.int32)
    head_select = jnp.transpose(select)[:, :, None, None]
    spreads = []
    suffix_windows = []
    for request in range(req_lengths.shape[0]):
        window_queries = lax.dynamic_slice_in_dim(queries, firsts[request], window, 0)
        window_queries = jnp.transpose(window_queries.reshape(window, head_count, HD), (1, 0, 2))
        spread = jnp.concatenate(
            [window_queries * head_select[0], window_queries * head_select[1]], axis=2
        )
        spreads.append(spread.reshape(head_count * window, 2 * HD))
        suffix_windows.append(lax.dynamic_slice_in_dim(suffix_rows, firsts[request], window, 0))
    query_rows = (jnp.arange(head_count * window, dtype=jnp.int32) % window)[:, None]
    row_pairs = jnp.repeat(pair_ids.astype(jnp.int32), window)[:, None]
    slot_index = slot_of_tenant[req_tenant].astype(jnp.int32)
    results = window_attention(
        slot_index,
        firsts,
        req_starts.astype(jnp.int32),
        jnp.stack(spreads),
        slots,
        jnp.stack(suffix_windows),
        query_rows,
        row_pairs,
        own_slot.shape[0],
    ).reshape(-1, head_count, window, HD)
    attended = jnp.zeros((row_count, head_count * HD), jnp.bfloat16)
    for request in range(req_lengths.shape[0]):
        window_attended = jnp.transpose(results[request], (1, 0, 2)).reshape(window, -1)
        placed = lax.dynamic_update_slice_in_dim(
            jnp.zeros_like(attended), window_attended, firsts[request], 0
        )
        attended = jnp.where((request_ids == request)[:, None], placed, attended)

    projected = jnp.dot(attended, weight_pieces[0], preferred_element_type=jnp.float32)
    for shift in range(1, n_tp):
        head_block = shifted(attended, shift, n_tp)
        projected = projected + jnp.dot(
            head_block, weight_pieces[shift], preferred_element_type=jnp.float32
        )
    new_residual = (residual.astype(jnp.float32) + projected).astype(jnp.bfloat16)

    blocks = [new_residual] + [shifted(new_residual, shift, n_tp) for shift in range(1, n_tp)]
    widened = [block.astype(jnp.float32) for block in blocks]
    square_sums = sum(jnp.sum(block * block, axis=1, keepdims=True) for block in widened)
    mean_square = square_sums / (width * n_tp)
    scale = lax.rsqrt(mean_square + 1e-05)
    gain = norm_gain.astype(jnp.float32)
    next_sums = None
    for shift in range(n_tp):
        source = (tp_index - shift) % n_tp
        block_gain = lax.dynamic_slice_in_dim(gain, source * width, width, 0)
        block_weight = lax.dynamic_slice_in_dim(next_query_weight, source * width, width, 0)
        normed = (widened[shift] * scale * block_gain).astype(jnp.bfloat16)
        part = jnp.dot(normed, block_weight, preferred_element_type=jnp.float32)
        next_sums = part if next_sums is None else next_sums + part
    return (new_residual, next_sums.astype(jnp.bfloat16))


def solution(mesh):
    n_req = mesh.shape["req"]
    n_tp = mesh.shape["tp"]

    def body(*args):
        return local(*args, n_req=n_req, n_tp=n_tp)

    return jax.shard_map(
        body,
        mesh=mesh,
        in_specs=(
            P("req", "tp"),
            P("req", "tp"),
            P("req", "tp", None),
            P("req", "tp", None),
            P("tp", None),
            P(),
            P(None, "tp"),
            P("req", None),
            P("req", None),
            P(),
        ),
        out_specs=(P("req", "tp"), P("req", "tp")),
        check_vma=False,
    )
```

```python
import jax
import jax.numpy as jnp
from jax import lax
from jax.experimental import pallas as pl
from jax.experimental.pallas import tpu as pltpu
from jax.sharding import PartitionSpec as P

QH = 20
KVH = 5
HD = 64
TENANTS = 4
MOSTLEN = 128
GATHER_SLOTS_MAX = 16


def from_root(block, axis, source):
    block = jnp.where(lax.axis_index(axis) == source, block, jnp.zeros_like(block))
    return lax.psum(block, axis)


def pick_heads(pair_rows, select):
    split_pair = pair_rows.reshape(pair_rows.shape[0], 2, 2, HD)
    key_heads = jnp.einsum(
        "njd,hj->nhd", split_pair[:, :, 0], select, preferred_element_type=jnp.float32
    ).astype(jnp.bfloat16)
    value_heads = jnp.einsum(
        "njd,hj->nhd", split_pair[:, :, 1], select, preferred_element_type=jnp.float32
    ).astype(jnp.bfloat16)
    return (key_heads, value_heads)


def tenant_slots(own_slot, owners, n_req):
    if n_req <= GATHER_SLOTS_MAX:
        return lax.all_gather(own_slot, "req", axis=0, tiled=True), owners
    blocks = [from_root(own_slot, "req", owners[tenant_id]) for tenant_id in range(TENANTS)]
    return jnp.concatenate(blocks, axis=0), jnp.arange(TENANTS, dtype=jnp.int32)


def attention_kernel(
    slot_ref, first_ref, start_ref, end_ref, query_ref, prefix_ref, suffix_ref, row_ref, pair_ref, out_ref
):
    request = pl.program_id(0)
    first = pl.multiple_of(first_ref[request], 8)
    start = start_ref[request]
    spread = query_ref[...]
    pair_lanes = 2 * HD
    prefix_keys = prefix_ref[:, :pair_lanes]
    prefix_values = prefix_ref[:, pair_lanes:]
    suffix_keys = suffix_ref[:, :pair_lanes]
    suffix_values = suffix_ref[:, pair_lanes:]
    contract = (((1,), (1,)), ((), ()))
    score_scale = HD ** (-0.5)
    prefix_scores = lax.dot_general(
        spread, prefix_keys, contract, preferred_element_type=jnp.float32
    ) * score_scale
    suffix_scores = lax.dot_general(
        spread, suffix_keys, contract, preferred_element_type=jnp.float32
    ) * score_scale
    key_position = first + lax.broadcasted_iota(jnp.int32, suffix_scores.shape, 1)
    query_position = first + row_ref[...]
    allowed = (key_position >= start) & (key_position <= query_position)
    suffix_scores = jnp.where(allowed, suffix_scores, -jnp.inf)
    row_top = jnp.maximum(
        jnp.max(prefix_scores, axis=1, keepdims=True),
        jnp.max(suffix_scores, axis=1, keepdims=True),
    )
    prefix_weights = jnp.exp(prefix_scores - row_top)
    suffix_weights = jnp.where(allowed, jnp.exp(suffix_scores - row_top), 0.0)
    denominator = jnp.sum(prefix_weights, axis=1, keepdims=True) + jnp.sum(
        suffix_weights, axis=1, keepdims=True
    )
    accumulated = jnp.dot(
        prefix_weights.astype(jnp.bfloat16), prefix_values, preferred_element_type=jnp.float32
    ) + jnp.dot(
        suffix_weights.astype(jnp.bfloat16), suffix_values, preferred_element_type=jnp.float32
    )
    attended = accumulated / denominator
    first_pair = attended[:, :HD]
    second_pair = attended[:, HD:]
    picked = jnp.where(pair_ref[...] > 0, second_pair, first_pair)
    picked = picked.astype(jnp.bfloat16).astype(out_ref.dtype)
    window = suffix_ref.shape[0]
    row_position = first + lax.broadcasted_iota(jnp.int32, (window, HD), 0)
    mine = (row_position >= start) & (row_position < end_ref[request])
    for head in range(out_ref.shape[1] // HD):
        lanes = slice(head * HD, (head + 1) * HD)
        kept = out_ref[pl.ds(first, window), lanes]
        out_ref[pl.ds(first, window), lanes] = jnp.where(
            mine, picked[head * window:(head + 1) * window], kept
        )


def window_attention(
    slot_index, firsts, starts, ends, spread, slots, suffix_windows, query_rows, row_pairs, slot_rows, row_count
):
    requests, flat_rows, query_lanes = spread.shape
    window = suffix_windows.shape[1]
    lanes = slots.shape[1]
    head_count = flat_rows // window
    grid_spec = pltpu.PrefetchScalarGridSpec(
        num_scalar_prefetch=4,
        grid=(requests,),
        in_specs=[
            pl.BlockSpec((None, flat_rows, query_lanes), lambda k, slot, first, start, end: (k, 0, 0)),
            pl.BlockSpec((slot_rows, lanes), lambda k, slot, first, start, end: (slot[k], 0)),
            pl.BlockSpec((None, window, lanes), lambda k, slot, first, start, end: (k, 0, 0)),
            pl.BlockSpec((flat_rows, 1), lambda k, slot, first, start, end: (0, 0)),
            pl.BlockSpec((flat_rows, 1), lambda k, slot, first, start, end: (0, 0)),
        ],
        out_specs=pl.BlockSpec(
            (row_count, head_count * HD), lambda k, slot, first, start, end: (0, 0)
        ),
    )
    return pl.pallas_call(
        attention_kernel,
        grid_spec=grid_spec,
        out_shape=jax.ShapeDtypeStruct((row_count, head_count * HD), jnp.float32),
    )(slot_index, firsts, starts, ends, spread, slots, suffix_windows, query_rows, row_pairs)


def shifted(block, shift, n_tp):
    pairs = [(source, (source + shift) % n_tp) for source in range(n_tp)]
    return lax.ppermute(block, "tp", pairs)


def local(
    residual,
    queries,
    suffix_kv,
    prefix_cache,
    out_weight,
    norm_gain,
    next_query_weight,
    lengths,
    tenant,
    owners,
    n_req,
    n_tp,
):
    row_count = queries.shape[0]
    head_count = queries.shape[1] // HD
    width = residual.shape[1]
    tp_index = lax.axis_index("tp")

    weight_pieces = []
    for shift in range(n_tp):
        target = (tp_index + shift) % n_tp
        piece = lax.dynamic_slice_in_dim(out_weight, target * width, width, 1)
        weight_pieces.append(piece if shift == 0 else shifted(piece, shift, n_tp))

    head_ids = tp_index * head_count + jnp.arange(head_count, dtype=jnp.int32)
    pair_ids = head_ids // (QH // KVH) - tp_index
    select = (pair_ids[:, None] == jnp.arange(2, dtype=jnp.int32)[None, :]).astype(jnp.bfloat16)
    req_lengths = lengths[0]
    req_tenant = tenant[0]
    req_ends = jnp.cumsum(req_lengths)
    req_starts = req_ends - req_lengths
    position = jnp.arange(row_count, dtype=jnp.int32)
    request_ids = jnp.sum((position[:, None] >= req_ends[None, :]).astype(jnp.int32), axis=1)
    member = request_ids[:, None] == jnp.arange(req_lengths.shape[0], dtype=jnp.int32)[None, :]
    row_start = jnp.sum(jnp.where(member, req_starts[None, :], 0), axis=1)
    row_tenant = jnp.sum(jnp.where(member, req_tenant[None, :], 0), axis=1)
    score_scale = HD ** (-0.5)
    own_slot = jnp.transpose(
        prefix_cache.reshape(prefix_cache.shape[0], 2, 2, HD), (0, 2, 1, 3)
    ).reshape(prefix_cache.shape[0], -1)
    slots, slot_of_tenant = tenant_slots(own_slot, owners, n_req)
    suffix_rows = jnp.transpose(suffix_kv.reshape(row_count, 2, 2, HD), (0, 2, 1, 3)).reshape(
        row_count, -1
    )
    window = min(MOSTLEN + 8, row_count)
    firsts = jnp.minimum(req_starts // 8 * 8, row_count - window).astype(jnp.int32)
    head_select = jnp.transpose(select)[:, :, None, None]
    spreads = []
    suffix_windows = []
    for request in range(req_lengths.shape[0]):
        window_queries = lax.dynamic_slice_in_dim(queries, firsts[request], window, 0)
        window_queries = jnp.transpose(window_queries.reshape(window, head_count, HD), (1, 0, 2))
        spread = jnp.concatenate(
            [window_queries * head_select[0], window_queries * head_select[1]], axis=2
        )
        spreads.append(spread.reshape(head_count * window, 2 * HD))
        suffix_windows.append(lax.dynamic_slice_in_dim(suffix_rows, firsts[request], window, 0))
    query_rows = (jnp.arange(head_count * window, dtype=jnp.int32) % window)[:, None]
    row_pairs = jnp.repeat(pair_ids.astype(jnp.int32), window)[:, None]
    slot_index = slot_of_tenant[req_tenant].astype(jnp.int32)
    attended = window_attention(
        slot_index,
        firsts,
        req_starts.astype(jnp.int32),
        req_ends.astype(jnp.int32),
        jnp.stack(spreads),
        slots,
        jnp.stack(suffix_windows),
        query_rows,
        row_pairs,
        own_slot.shape[0],
        row_count,
    ).astype(jnp.bfloat16)

    projected = jnp.dot(attended, weight_pieces[0], preferred_element_type=jnp.float32)
    for shift in range(1, n_tp):
        head_block = shifted(attended, shift, n_tp)
        projected = projected + jnp.dot(
            head_block, weight_pieces[shift], preferred_element_type=jnp.float32
        )
    new_residual = (residual.astype(jnp.float32) + projected).astype(jnp.bfloat16)

    blocks = [new_residual] + [shifted(new_residual, shift, n_tp) for shift in range(1, n_tp)]
    widened = [block.astype(jnp.float32) for block in blocks]
    square_sums = sum(jnp.sum(block * block, axis=1, keepdims=True) for block in widened)
    mean_square = square_sums / (width * n_tp)
    scale = lax.rsqrt(mean_square + 1e-05)
    gain = norm_gain.astype(jnp.float32)
    next_sums = None
    for shift in range(n_tp):
        source = (tp_index - shift) % n_tp
        block_gain = lax.dynamic_slice_in_dim(gain, source * width, width, 0)
        block_weight = lax.dynamic_slice_in_dim(next_query_weight, source * width, width, 0)
        normed = (widened[shift] * scale * block_gain).astype(jnp.bfloat16)
        part = jnp.dot(normed, block_weight, preferred_element_type=jnp.float32)
        next_sums = part if next_sums is None else next_sums + part
    return (new_residual, next_sums.astype(jnp.bfloat16))


def solution(mesh):
    n_req = mesh.shape["req"]
    n_tp = mesh.shape["tp"]

    def body(*args):
        return local(*args, n_req=n_req, n_tp=n_tp)

    return jax.shard_map(
        body,
        mesh=mesh,
        in_specs=(
            P("req", "tp"),
            P("req", "tp"),
            P("req", "tp", None),
            P("req", "tp", None),
            P("tp", None),
            P(),
            P(None, "tp"),
            P("req", None),
            P("req", None),
            P(),
        ),
        out_specs=(P("req", "tp"), P("req", "tp")),
        check_vma=False,
    )
```

```python
import jax
import jax.numpy as jnp
from jax import lax
from jax.experimental import pallas as pl
from jax.experimental.pallas import tpu as pltpu
from jax.sharding import PartitionSpec as P

QH = 20
KVH = 5
HD = 64
TENANTS = 4
MOSTLEN = 128
GATHER_SLOTS_MAX = 16


def from_root(block, axis, source):
    block = jnp.where(lax.axis_index(axis) == source, block, jnp.zeros_like(block))
    return lax.psum(block, axis)


def pick_heads(pair_rows, select):
    split_pair = pair_rows.reshape(pair_rows.shape[0], 2, 2, HD)
    key_heads = jnp.einsum(
        "njd,hj->nhd", split_pair[:, :, 0], select, preferred_element_type=jnp.float32
    ).astype(jnp.bfloat16)
    value_heads = jnp.einsum(
        "njd,hj->nhd", split_pair[:, :, 1], select, preferred_element_type=jnp.float32
    ).astype(jnp.bfloat16)
    return (key_heads, value_heads)


def xor_permute(block, mask, n_req):
    pairs = [(source, source ^ mask) for source in range(n_req)]
    return lax.ppermute(block, "req", pairs)


def tenant_slots(own_slot, owners, n_req):
    if n_req <= GATHER_SLOTS_MAX and n_req % 2 == 0 and (n_req & (n_req - 1)) == 0:
        req_index = lax.axis_index("req")
        mine = [own_slot] + [
            xor_permute(own_slot, 2 * chip_mask, n_req) for chip_mask in range(1, n_req // 2)
        ]
        theirs = [xor_permute(block, 1, n_req) for block in mine]
        slots = jnp.concatenate(
            [block for pair in zip(mine, theirs) for block in pair], axis=0
        )
        chip_offset = (owners // 2) ^ (req_index // 2)
        other_core = (owners % 2) != (req_index % 2)
        return slots, 2 * chip_offset + other_core.astype(jnp.int32)
    blocks = [from_root(own_slot, "req", owners[tenant_id]) for tenant_id in range(TENANTS)]
    return jnp.concatenate(blocks, axis=0), jnp.arange(TENANTS, dtype=jnp.int32)


def attention_kernel(
    slot_ref, first_ref, start_ref, query_ref, prefix_ref, suffix_ref, row_ref, pair_ref, out_ref
):
    request = pl.program_id(0)
    first = first_ref[request]
    start = start_ref[request]
    spread = query_ref[...]
    pair_lanes = 2 * HD
    prefix_keys = prefix_ref[:, :pair_lanes]
    prefix_values = prefix_ref[:, pair_lanes:]
    suffix_keys = suffix_ref[:, :pair_lanes]
    suffix_values = suffix_ref[:, pair_lanes:]
    contract = (((1,), (1,)), ((), ()))
    score_scale = HD ** (-0.5)
    prefix_scores = lax.dot_general(
        spread, prefix_keys, contract, preferred_element_type=jnp.float32
    ) * score_scale
    suffix_scores = lax.dot_general(
        spread, suffix_keys, contract, preferred_element_type=jnp.float32
    ) * score_scale
    key_position = first + lax.broadcasted_iota(jnp.int32, suffix_scores.shape, 1)
    query_position = first + row_ref[...]
    allowed = (key_position >= start) & (key_position <= query_position)
    suffix_scores = jnp.where(allowed, suffix_scores, -jnp.inf)
    row_top = jnp.maximum(
        jnp.max(prefix_scores, axis=1, keepdims=True),
        jnp.max(suffix_scores, axis=1, keepdims=True),
    )
    prefix_weights = jnp.exp(prefix_scores - row_top)
    suffix_weights = jnp.where(allowed, jnp.exp(suffix_scores - row_top), 0.0)
    denominator = jnp.sum(prefix_weights, axis=1, keepdims=True) + jnp.sum(
        suffix_weights, axis=1, keepdims=True
    )
    accumulated = jnp.dot(
        prefix_weights.astype(jnp.bfloat16), prefix_values, preferred_element_type=jnp.float32
    ) + jnp.dot(
        suffix_weights.astype(jnp.bfloat16), suffix_values, preferred_element_type=jnp.float32
    )
    attended = accumulated / denominator
    first_pair = attended[:, :HD]
    second_pair = attended[:, HD:]
    out_ref[...] = jnp.where(pair_ref[...] > 0, second_pair, first_pair).astype(out_ref.dtype)


def window_attention(
    slot_index, firsts, starts, spread, slots, suffix_windows, query_rows, row_pairs, slot_rows
):
    requests, flat_rows, query_lanes = spread.shape
    window = suffix_windows.shape[1]
    lanes = slots.shape[1]
    grid_spec = pltpu.PrefetchScalarGridSpec(
        num_scalar_prefetch=3,
        grid=(requests,),
        in_specs=[
            pl.BlockSpec((None, flat_rows, query_lanes), lambda k, slot, first, start: (k, 0, 0)),
            pl.BlockSpec((slot_rows, lanes), lambda k, slot, first, start: (slot[k], 0)),
            pl.BlockSpec((None, window, lanes), lambda k, slot, first, start: (k, 0, 0)),
            pl.BlockSpec((flat_rows, 1), lambda k, slot, first, start: (0, 0)),
            pl.BlockSpec((flat_rows, 1), lambda k, slot, first, start: (0, 0)),
        ],
        out_specs=pl.BlockSpec((None, flat_rows, HD), lambda k, slot, first, start: (k, 0, 0)),
    )
    return pl.pallas_call(
        attention_kernel,
        grid_spec=grid_spec,
        out_shape=jax.ShapeDtypeStruct((requests, flat_rows, HD), jnp.bfloat16),
    )(slot_index, firsts, starts, spread, slots, suffix_windows, query_rows, row_pairs)


def shifted(block, shift, n_tp):
    pairs = [(source, (source + shift) % n_tp) for source in range(n_tp)]
    return lax.ppermute(block, "tp", pairs)


def local(
    residual,
    queries,
    suffix_kv,
    prefix_cache,
    out_weight,
    norm_gain,
    next_query_weight,
    lengths,
    tenant,
    owners,
    n_req,
    n_tp,
):
    row_count = queries.shape[0]
    head_count = queries.shape[1] // HD
    width = residual.shape[1]
    tp_index = lax.axis_index("tp")

    weight_pieces = []
    for shift in range(n_tp):
        target = (tp_index + shift) % n_tp
        piece = lax.dynamic_slice_in_dim(out_weight, target * width, width, 1)
        weight_pieces.append(piece if shift == 0 else shifted(piece, shift, n_tp))

    head_ids = tp_index * head_count + jnp.arange(head_count, dtype=jnp.int32)
    pair_ids = head_ids // (QH // KVH) - tp_index
    select = (pair_ids[:, None] == jnp.arange(2, dtype=jnp.int32)[None, :]).astype(jnp.bfloat16)
    req_lengths = lengths[0]
    req_tenant = tenant[0]
    req_ends = jnp.cumsum(req_lengths)
    req_starts = req_ends - req_lengths
    position = jnp.arange(row_count, dtype=jnp.int32)
    request_ids = jnp.sum((position[:, None] >= req_ends[None, :]).astype(jnp.int32), axis=1)
    member = request_ids[:, None] == jnp.arange(req_lengths.shape[0], dtype=jnp.int32)[None, :]
    row_start = jnp.sum(jnp.where(member, req_starts[None, :], 0), axis=1)
    row_tenant = jnp.sum(jnp.where(member, req_tenant[None, :], 0), axis=1)
    score_scale = HD ** (-0.5)
    own_slot = jnp.transpose(
        prefix_cache.reshape(prefix_cache.shape[0], 2, 2, HD), (0, 2, 1, 3)
    ).reshape(prefix_cache.shape[0], -1)
    slots, slot_of_tenant = tenant_slots(own_slot, owners, n_req)
    suffix_rows = jnp.transpose(suffix_kv.reshape(row_count, 2, 2, HD), (0, 2, 1, 3)).reshape(
        row_count, -1
    )
    window = min(MOSTLEN, row_count)
    firsts = jnp.minimum(req_starts, row_count - window).astype(jnp.int32)
    head_select = jnp.transpose(select)[:, :, None, None]
    spreads = []
    suffix_windows = []
    for request in range(req_lengths.shape[0]):
        window_queries = lax.dynamic_slice_in_dim(queries, firsts[request], window, 0)
        window_queries = jnp.transpose(window_queries.reshape(window, head_count, HD), (1, 0, 2))
        spread = jnp.concatenate(
            [window_queries * head_select[0], window_queries * head_select[1]], axis=2
        )
        spreads.append(spread.reshape(head_count * window, 2 * HD))
        suffix_windows.append(lax.dynamic_slice_in_dim(suffix_rows, firsts[request], window, 0))
    query_rows = (jnp.arange(head_count * window, dtype=jnp.int32) % window)[:, None]
    row_pairs = jnp.repeat(pair_ids.astype(jnp.int32), window)[:, None]
    slot_index = slot_of_tenant[req_tenant].astype(jnp.int32)
    results = window_attention(
        slot_index,
        firsts,
        req_starts.astype(jnp.int32),
        jnp.stack(spreads),
        slots,
        jnp.stack(suffix_windows),
        query_rows,
        row_pairs,
        own_slot.shape[0],
    ).reshape(-1, head_count, window, HD)
    attended = jnp.zeros((row_count, head_count * HD), jnp.bfloat16)
    for request in range(req_lengths.shape[0]):
        window_attended = jnp.transpose(results[request], (1, 0, 2)).reshape(window, -1)
        placed = lax.dynamic_update_slice_in_dim(
            jnp.zeros_like(attended), window_attended, firsts[request], 0
        )
        attended = jnp.where((request_ids == request)[:, None], placed, attended)

    projected = jnp.dot(attended, weight_pieces[0], preferred_element_type=jnp.float32)
    for shift in range(1, n_tp):
        head_block = shifted(attended, shift, n_tp)
        projected = projected + jnp.dot(
            head_block, weight_pieces[shift], preferred_element_type=jnp.float32
        )
    new_residual = (residual.astype(jnp.float32) + projected).astype(jnp.bfloat16)

    blocks = [new_residual] + [shifted(new_residual, shift, n_tp) for shift in range(1, n_tp)]
    widened = [block.astype(jnp.float32) for block in blocks]
    square_sums = sum(jnp.sum(block * block, axis=1, keepdims=True) for block in widened)
    mean_square = square_sums / (width * n_tp)
    scale = lax.rsqrt(mean_square + 1e-05)
    gain = norm_gain.astype(jnp.float32)
    next_sums = None
    for shift in range(n_tp):
        source = (tp_index - shift) % n_tp
        block_gain = lax.dynamic_slice_in_dim(gain, source * width, width, 0)
        block_weight = lax.dynamic_slice_in_dim(next_query_weight, source * width, width, 0)
        normed = (widened[shift] * scale * block_gain).astype(jnp.bfloat16)
        part = jnp.dot(normed, block_weight, preferred_element_type=jnp.float32)
        next_sums = part if next_sums is None else next_sums + part
    return (new_residual, next_sums.astype(jnp.bfloat16))


def solution(mesh):
    n_req = mesh.shape["req"]
    n_tp = mesh.shape["tp"]

    def body(*args):
        return local(*args, n_req=n_req, n_tp=n_tp)

    return jax.shard_map(
        body,
        mesh=mesh,
        in_specs=(
            P("req", "tp"),
            P("req", "tp"),
            P("req", "tp", None),
            P("req", "tp", None),
            P("tp", None),
            P(),
            P(None, "tp"),
            P("req", None),
            P("req", None),
            P(),
        ),
        out_specs=(P("req", "tp"), P("req", "tp")),
        check_vma=False,
    )
```

```python
import jax
import jax.numpy as jnp
from jax import lax
from jax.experimental import pallas as pl
from jax.experimental.pallas import tpu as pltpu
from jax.sharding import PartitionSpec as P

QH = 20
KVH = 5
HD = 64
TENANTS = 4
MOSTLEN = 128
GATHER_SLOTS_MAX = 16


def from_root(block, axis, source):
    block = jnp.where(lax.axis_index(axis) == source, block, jnp.zeros_like(block))
    return lax.psum(block, axis)


def pick_heads(pair_rows, select):
    split_pair = pair_rows.reshape(pair_rows.shape[0], 2, 2, HD)
    key_heads = jnp.einsum(
        "njd,hj->nhd", split_pair[:, :, 0], select, preferred_element_type=jnp.float32
    ).astype(jnp.bfloat16)
    value_heads = jnp.einsum(
        "njd,hj->nhd", split_pair[:, :, 1], select, preferred_element_type=jnp.float32
    ).astype(jnp.bfloat16)
    return (key_heads, value_heads)


def xor_permute(block, mask, n_req):
    pairs = [(source, source ^ mask) for source in range(n_req)]
    return lax.ppermute(block, "req", pairs)


def tenant_slots(own_slot, owners, n_req):
    if n_req <= GATHER_SLOTS_MAX and n_req % 2 == 0 and (n_req & (n_req - 1)) == 0:
        req_index = lax.axis_index("req")
        mine = [own_slot] + [
            xor_permute(own_slot, 2 * chip_mask, n_req) for chip_mask in range(1, n_req // 2)
        ]
        theirs = [xor_permute(block, 1, n_req) for block in mine]
        slots = jnp.concatenate(
            [block for pair in zip(mine, theirs) for block in pair], axis=0
        )
        chip_offset = (owners // 2) ^ (req_index // 2)
        other_core = (owners % 2) != (req_index % 2)
        return slots, 2 * chip_offset + other_core.astype(jnp.int32)
    blocks = [from_root(own_slot, "req", owners[tenant_id]) for tenant_id in range(TENANTS)]
    return jnp.concatenate(blocks, axis=0), jnp.arange(TENANTS, dtype=jnp.int32)


def attention_kernel(
    slot_ref, first_ref, start_ref, query_ref, prefix_ref, suffix_ref, row_ref, pair_ref, out_ref
):
    request = pl.program_id(0)
    first = first_ref[request]
    start = start_ref[request]
    spread = query_ref[...]
    pair_lanes = 2 * HD
    prefix_keys = prefix_ref[:, :pair_lanes]
    prefix_values = prefix_ref[:, pair_lanes:]
    suffix_keys = suffix_ref[:, :pair_lanes]
    suffix_values = suffix_ref[:, pair_lanes:]
    contract = (((1,), (1,)), ((), ()))
    score_scale = HD ** (-0.5)
    prefix_scores = lax.dot_general(
        spread, prefix_keys, contract, preferred_element_type=jnp.float32
    ) * score_scale
    suffix_scores = lax.dot_general(
        spread, suffix_keys, contract, preferred_element_type=jnp.float32
    ) * score_scale
    key_position = first + lax.broadcasted_iota(jnp.int32, suffix_scores.shape, 1)
    query_position = first + row_ref[...]
    allowed = (key_position >= start) & (key_position <= query_position)
    suffix_scores = jnp.where(allowed, suffix_scores, -jnp.inf)
    row_top = jnp.maximum(
        jnp.max(prefix_scores, axis=1, keepdims=True),
        jnp.max(suffix_scores, axis=1, keepdims=True),
    )
    prefix_weights = jnp.exp(prefix_scores - row_top)
    suffix_weights = jnp.where(allowed, jnp.exp(suffix_scores - row_top), 0.0)
    denominator = jnp.sum(prefix_weights, axis=1, keepdims=True) + jnp.sum(
        suffix_weights, axis=1, keepdims=True
    )
    accumulated = jnp.dot(
        prefix_weights.astype(jnp.bfloat16), prefix_values, preferred_element_type=jnp.float32
    ) + jnp.dot(
        suffix_weights.astype(jnp.bfloat16), suffix_values, preferred_element_type=jnp.float32
    )
    attended = accumulated / denominator
    first_pair = attended[:, :HD]
    second_pair = attended[:, HD:]
    out_ref[...] = jnp.where(pair_ref[...] > 0, second_pair, first_pair).astype(out_ref.dtype)


def window_attention(
    slot_index, firsts, starts, spread, slots, suffix_windows, query_rows, row_pairs, slot_rows
):
    requests, flat_rows, query_lanes = spread.shape
    window = suffix_windows.shape[1]
    lanes = slots.shape[1]
    grid_spec = pltpu.PrefetchScalarGridSpec(
        num_scalar_prefetch=3,
        grid=(requests,),
        in_specs=[
            pl.BlockSpec((None, flat_rows, query_lanes), lambda k, slot, first, start: (k, 0, 0)),
            pl.BlockSpec((slot_rows, lanes), lambda k, slot, first, start: (slot[k], 0)),
            pl.BlockSpec((None, window, lanes), lambda k, slot, first, start: (k, 0, 0)),
            pl.BlockSpec((flat_rows, 1), lambda k, slot, first, start: (0, 0)),
            pl.BlockSpec((flat_rows, 1), lambda k, slot, first, start: (0, 0)),
        ],
        out_specs=pl.BlockSpec((None, flat_rows, HD), lambda k, slot, first, start: (k, 0, 0)),
    )
    return pl.pallas_call(
        attention_kernel,
        grid_spec=grid_spec,
        out_shape=jax.ShapeDtypeStruct((requests, flat_rows, HD), jnp.bfloat16),
    )(slot_index, firsts, starts, spread, slots, suffix_windows, query_rows, row_pairs)


def xor_tp(block, mask, n_tp):
    pairs = [(source, source ^ mask) for source in range(n_tp)]
    return lax.ppermute(block, "tp", pairs)


def from_partners(block, n_tp):
    if n_tp == 4:
        near = xor_tp(block, 1, n_tp)
        across = xor_tp(block, 2, n_tp)
        return [block, near, across, xor_tp(across, 1, n_tp)]
    return [block] + [xor_tp(block, mask, n_tp) for mask in range(1, n_tp)]


def shifted(block, shift, n_tp):
    pairs = [(source, (source + shift) % n_tp) for source in range(n_tp)]
    return lax.ppermute(block, "tp", pairs)


def local(
    residual,
    queries,
    suffix_kv,
    prefix_cache,
    out_weight,
    norm_gain,
    next_query_weight,
    lengths,
    tenant,
    owners,
    n_req,
    n_tp,
):
    row_count = queries.shape[0]
    head_count = queries.shape[1] // HD
    width = residual.shape[1]
    tp_index = lax.axis_index("tp")

    weight_pieces = []
    for mask in range(n_tp):
        partner = tp_index ^ mask
        piece = lax.dynamic_slice_in_dim(out_weight, partner * width, width, 1)
        weight_pieces.append(piece if mask == 0 else xor_tp(piece, mask, n_tp))

    head_ids = tp_index * head_count + jnp.arange(head_count, dtype=jnp.int32)
    pair_ids = head_ids // (QH // KVH) - tp_index
    select = (pair_ids[:, None] == jnp.arange(2, dtype=jnp.int32)[None, :]).astype(jnp.bfloat16)
    req_lengths = lengths[0]
    req_tenant = tenant[0]
    req_ends = jnp.cumsum(req_lengths)
    req_starts = req_ends - req_lengths
    position = jnp.arange(row_count, dtype=jnp.int32)
    request_ids = jnp.sum((position[:, None] >= req_ends[None, :]).astype(jnp.int32), axis=1)
    member = request_ids[:, None] == jnp.arange(req_lengths.shape[0], dtype=jnp.int32)[None, :]
    row_start = jnp.sum(jnp.where(member, req_starts[None, :], 0), axis=1)
    row_tenant = jnp.sum(jnp.where(member, req_tenant[None, :], 0), axis=1)
    score_scale = HD ** (-0.5)
    own_slot = jnp.transpose(
        prefix_cache.reshape(prefix_cache.shape[0], 2, 2, HD), (0, 2, 1, 3)
    ).reshape(prefix_cache.shape[0], -1)
    slots, slot_of_tenant = tenant_slots(own_slot, owners, n_req)
    suffix_rows = jnp.transpose(suffix_kv.reshape(row_count, 2, 2, HD), (0, 2, 1, 3)).reshape(
        row_count, -1
    )
    window = min(MOSTLEN, row_count)
    firsts = jnp.minimum(req_starts, row_count - window).astype(jnp.int32)
    head_select = jnp.transpose(select)[:, :, None, None]
    spreads = []
    suffix_windows = []
    for request in range(req_lengths.shape[0]):
        window_queries = lax.dynamic_slice_in_dim(queries, firsts[request], window, 0)
        window_queries = jnp.transpose(window_queries.reshape(window, head_count, HD), (1, 0, 2))
        spread = jnp.concatenate(
            [window_queries * head_select[0], window_queries * head_select[1]], axis=2
        )
        spreads.append(spread.reshape(head_count * window, 2 * HD))
        suffix_windows.append(lax.dynamic_slice_in_dim(suffix_rows, firsts[request], window, 0))
    query_rows = (jnp.arange(head_count * window, dtype=jnp.int32) % window)[:, None]
    row_pairs = jnp.repeat(pair_ids.astype(jnp.int32), window)[:, None]
    slot_index = slot_of_tenant[req_tenant].astype(jnp.int32)
    results = window_attention(
        slot_index,
        firsts,
        req_starts.astype(jnp.int32),
        jnp.stack(spreads),
        slots,
        jnp.stack(suffix_windows),
        query_rows,
        row_pairs,
        own_slot.shape[0],
    ).reshape(-1, head_count, window, HD)
    attended = jnp.zeros((row_count, head_count * HD), jnp.bfloat16)
    for request in range(req_lengths.shape[0]):
        window_attended = jnp.transpose(results[request], (1, 0, 2)).reshape(window, -1)
        placed = lax.dynamic_update_slice_in_dim(
            jnp.zeros_like(attended), window_attended, firsts[request], 0
        )
        attended = jnp.where((request_ids == request)[:, None], placed, attended)

    head_blocks = from_partners(attended, n_tp)
    projected = None
    for mask in range(n_tp):
        part = jnp.dot(head_blocks[mask], weight_pieces[mask], preferred_element_type=jnp.float32)
        projected = part if projected is None else projected + part
    new_residual = (residual.astype(jnp.float32) + projected).astype(jnp.bfloat16)

    blocks = from_partners(new_residual, n_tp)
    widened = [block.astype(jnp.float32) for block in blocks]
    square_sums = sum(jnp.sum(block * block, axis=1, keepdims=True) for block in widened)
    mean_square = square_sums / (width * n_tp)
    scale = lax.rsqrt(mean_square + 1e-05)
    gain = norm_gain.astype(jnp.float32)
    next_sums = None
    for mask in range(n_tp):
        source = tp_index ^ mask
        block_gain = lax.dynamic_slice_in_dim(gain, source * width, width, 0)
        block_weight = lax.dynamic_slice_in_dim(next_query_weight, source * width, width, 0)
        normed = (widened[mask] * scale * block_gain).astype(jnp.bfloat16)
        part = jnp.dot(normed, block_weight, preferred_element_type=jnp.float32)
        next_sums = part if next_sums is None else next_sums + part
    return (new_residual, next_sums.astype(jnp.bfloat16))


def solution(mesh):
    n_req = mesh.shape["req"]
    n_tp = mesh.shape["tp"]

    def body(*args):
        return local(*args, n_req=n_req, n_tp=n_tp)

    return jax.shard_map(
        body,
        mesh=mesh,
        in_specs=(
            P("req", "tp"),
            P("req", "tp"),
            P("req", "tp", None),
            P("req", "tp", None),
            P("tp", None),
            P(),
            P(None, "tp"),
            P("req", None),
            P("req", None),
            P(),
        ),
        out_specs=(P("req", "tp"), P("req", "tp")),
        check_vma=False,
    )
```

```python
import jax
import jax.numpy as jnp
from jax import lax
from jax.experimental import pallas as pl
from jax.experimental.pallas import tpu as pltpu
from jax.sharding import PartitionSpec as P

QH = 20
KVH = 5
HD = 64
TENANTS = 4
MOSTLEN = 128
GATHER_SLOTS_MAX = 16


def from_root(block, axis, source):
    block = jnp.where(lax.axis_index(axis) == source, block, jnp.zeros_like(block))
    return lax.psum(block, axis)


def pick_heads(pair_rows, select):
    split_pair = pair_rows.reshape(pair_rows.shape[0], 2, 2, HD)
    key_heads = jnp.einsum(
        "njd,hj->nhd", split_pair[:, :, 0], select, preferred_element_type=jnp.float32
    ).astype(jnp.bfloat16)
    value_heads = jnp.einsum(
        "njd,hj->nhd", split_pair[:, :, 1], select, preferred_element_type=jnp.float32
    ).astype(jnp.bfloat16)
    return (key_heads, value_heads)


def xor_permute(block, mask, n_req):
    pairs = [(source, source ^ mask) for source in range(n_req)]
    return lax.ppermute(block, "req", pairs)


def tenant_slots(own_slot, owners, n_req):
    if n_req <= GATHER_SLOTS_MAX and n_req % 2 == 0 and (n_req & (n_req - 1)) == 0:
        req_index = lax.axis_index("req")
        half = own_slot.shape[0] // 2
        own_halves = [own_slot[:half], own_slot[half:]]
        mine = [own_halves] + [
            [xor_permute(part, 2 * chip_mask, n_req) for part in own_halves]
            for chip_mask in range(1, n_req // 2)
        ]
        theirs = [[xor_permute(part, 1, n_req) for part in halves] for halves in mine]
        slots = jnp.concatenate(
            [part for pair in zip(mine, theirs) for halves in pair for part in halves], axis=0
        )
        chip_offset = (owners // 2) ^ (req_index // 2)
        other_core = (owners % 2) != (req_index % 2)
        return slots, 2 * chip_offset + other_core.astype(jnp.int32)
    blocks = [from_root(own_slot, "req", owners[tenant_id]) for tenant_id in range(TENANTS)]
    return jnp.concatenate(blocks, axis=0), jnp.arange(TENANTS, dtype=jnp.int32)


def attention_kernel(
    slot_ref, first_ref, start_ref, query_ref, prefix_ref, suffix_ref, row_ref, pair_ref, out_ref
):
    request = pl.program_id(0)
    first = first_ref[request]
    start = start_ref[request]
    spread = query_ref[...]
    pair_lanes = 2 * HD
    prefix_keys = prefix_ref[:, :pair_lanes]
    prefix_values = prefix_ref[:, pair_lanes:]
    suffix_keys = suffix_ref[:, :pair_lanes]
    suffix_values = suffix_ref[:, pair_lanes:]
    contract = (((1,), (1,)), ((), ()))
    score_scale = HD ** (-0.5)
    prefix_scores = lax.dot_general(
        spread, prefix_keys, contract, preferred_element_type=jnp.float32
    ) * score_scale
    suffix_scores = lax.dot_general(
        spread, suffix_keys, contract, preferred_element_type=jnp.float32
    ) * score_scale
    key_position = first + lax.broadcasted_iota(jnp.int32, suffix_scores.shape, 1)
    query_position = first + row_ref[...]
    allowed = (key_position >= start) & (key_position <= query_position)
    suffix_scores = jnp.where(allowed, suffix_scores, -jnp.inf)
    row_top = jnp.maximum(
        jnp.max(prefix_scores, axis=1, keepdims=True),
        jnp.max(suffix_scores, axis=1, keepdims=True),
    )
    prefix_weights = jnp.exp(prefix_scores - row_top)
    suffix_weights = jnp.where(allowed, jnp.exp(suffix_scores - row_top), 0.0)
    denominator = jnp.sum(prefix_weights, axis=1, keepdims=True) + jnp.sum(
        suffix_weights, axis=1, keepdims=True
    )
    accumulated = jnp.dot(
        prefix_weights.astype(jnp.bfloat16), prefix_values, preferred_element_type=jnp.float32
    ) + jnp.dot(
        suffix_weights.astype(jnp.bfloat16), suffix_values, preferred_element_type=jnp.float32
    )
    attended = accumulated / denominator
    first_pair = attended[:, :HD]
    second_pair = attended[:, HD:]
    out_ref[...] = jnp.where(pair_ref[...] > 0, second_pair, first_pair).astype(out_ref.dtype)


def window_attention(
    slot_index, firsts, starts, spread, slots, suffix_windows, query_rows, row_pairs, slot_rows
):
    requests, flat_rows, query_lanes = spread.shape
    window = suffix_windows.shape[1]
    lanes = slots.shape[1]
    grid_spec = pltpu.PrefetchScalarGridSpec(
        num_scalar_prefetch=3,
        grid=(requests,),
        in_specs=[
            pl.BlockSpec((None, flat_rows, query_lanes), lambda k, slot, first, start: (k, 0, 0)),
            pl.BlockSpec((slot_rows, lanes), lambda k, slot, first, start: (slot[k], 0)),
            pl.BlockSpec((None, window, lanes), lambda k, slot, first, start: (k, 0, 0)),
            pl.BlockSpec((flat_rows, 1), lambda k, slot, first, start: (0, 0)),
            pl.BlockSpec((flat_rows, 1), lambda k, slot, first, start: (0, 0)),
        ],
        out_specs=pl.BlockSpec((None, flat_rows, HD), lambda k, slot, first, start: (k, 0, 0)),
    )
    return pl.pallas_call(
        attention_kernel,
        grid_spec=grid_spec,
        out_shape=jax.ShapeDtypeStruct((requests, flat_rows, HD), jnp.bfloat16),
    )(slot_index, firsts, starts, spread, slots, suffix_windows, query_rows, row_pairs)


def xor_tp(block, mask, n_tp):
    pairs = [(source, source ^ mask) for source in range(n_tp)]
    return lax.ppermute(block, "tp", pairs)


def from_partners(block, n_tp):
    if n_tp == 4:
        near = xor_tp(block, 1, n_tp)
        across = xor_tp(block, 2, n_tp)
        return [block, near, across, xor_tp(across, 1, n_tp)]
    return [block] + [xor_tp(block, mask, n_tp) for mask in range(1, n_tp)]


def shifted(block, shift, n_tp):
    pairs = [(source, (source + shift) % n_tp) for source in range(n_tp)]
    return lax.ppermute(block, "tp", pairs)


def local(
    residual,
    queries,
    suffix_kv,
    prefix_cache,
    out_weight,
    norm_gain,
    next_query_weight,
    lengths,
    tenant,
    owners,
    n_req,
    n_tp,
):
    row_count = queries.shape[0]
    head_count = queries.shape[1] // HD
    width = residual.shape[1]
    tp_index = lax.axis_index("tp")

    weight_pieces = []
    for mask in range(n_tp):
        partner = tp_index ^ mask
        piece = lax.dynamic_slice_in_dim(out_weight, partner * width, width, 1)
        weight_pieces.append(piece if mask == 0 else xor_tp(piece, mask, n_tp))

    head_ids = tp_index * head_count + jnp.arange(head_count, dtype=jnp.int32)
    pair_ids = head_ids // (QH // KVH) - tp_index
    select = (pair_ids[:, None] == jnp.arange(2, dtype=jnp.int32)[None, :]).astype(jnp.bfloat16)
    req_lengths = lengths[0]
    req_tenant = tenant[0]
    req_ends = jnp.cumsum(req_lengths)
    req_starts = req_ends - req_lengths
    position = jnp.arange(row_count, dtype=jnp.int32)
    request_ids = jnp.sum((position[:, None] >= req_ends[None, :]).astype(jnp.int32), axis=1)
    member = request_ids[:, None] == jnp.arange(req_lengths.shape[0], dtype=jnp.int32)[None, :]
    row_start = jnp.sum(jnp.where(member, req_starts[None, :], 0), axis=1)
    row_tenant = jnp.sum(jnp.where(member, req_tenant[None, :], 0), axis=1)
    score_scale = HD ** (-0.5)
    own_slot = jnp.transpose(
        prefix_cache.reshape(prefix_cache.shape[0], 2, 2, HD), (0, 2, 1, 3)
    ).reshape(prefix_cache.shape[0], -1)
    slots, slot_of_tenant = tenant_slots(own_slot, owners, n_req)
    suffix_rows = jnp.transpose(suffix_kv.reshape(row_count, 2, 2, HD), (0, 2, 1, 3)).reshape(
        row_count, -1
    )
    window = min(MOSTLEN, row_count)
    firsts = jnp.minimum(req_starts, row_count - window).astype(jnp.int32)
    head_select = jnp.transpose(select)[:, :, None, None]
    spreads = []
    suffix_windows = []
    for request in range(req_lengths.shape[0]):
        window_queries = lax.dynamic_slice_in_dim(queries, firsts[request], window, 0)
        window_queries = jnp.transpose(window_queries.reshape(window, head_count, HD), (1, 0, 2))
        spread = jnp.concatenate(
            [window_queries * head_select[0], window_queries * head_select[1]], axis=2
        )
        spreads.append(spread.reshape(head_count * window, 2 * HD))
        suffix_windows.append(lax.dynamic_slice_in_dim(suffix_rows, firsts[request], window, 0))
    query_rows = (jnp.arange(head_count * window, dtype=jnp.int32) % window)[:, None]
    row_pairs = jnp.repeat(pair_ids.astype(jnp.int32), window)[:, None]
    slot_index = slot_of_tenant[req_tenant].astype(jnp.int32)
    results = window_attention(
        slot_index,
        firsts,
        req_starts.astype(jnp.int32),
        jnp.stack(spreads),
        slots,
        jnp.stack(suffix_windows),
        query_rows,
        row_pairs,
        own_slot.shape[0],
    ).reshape(-1, head_count, window, HD)
    attended = jnp.zeros((row_count, head_count * HD), jnp.bfloat16)
    for request in range(req_lengths.shape[0]):
        window_attended = jnp.transpose(results[request], (1, 0, 2)).reshape(window, -1)
        placed = lax.dynamic_update_slice_in_dim(
            jnp.zeros_like(attended), window_attended, firsts[request], 0
        )
        attended = jnp.where((request_ids == request)[:, None], placed, attended)

    head_blocks = from_partners(attended, n_tp)
    projected = None
    for mask in range(n_tp):
        part = jnp.dot(head_blocks[mask], weight_pieces[mask], preferred_element_type=jnp.float32)
        projected = part if projected is None else projected + part
    new_residual = (residual.astype(jnp.float32) + projected).astype(jnp.bfloat16)

    blocks = from_partners(new_residual, n_tp)
    widened = [block.astype(jnp.float32) for block in blocks]
    square_sums = sum(jnp.sum(block * block, axis=1, keepdims=True) for block in widened)
    mean_square = square_sums / (width * n_tp)
    scale = lax.rsqrt(mean_square + 1e-05)
    gain = norm_gain.astype(jnp.float32)
    next_sums = None
    for mask in range(n_tp):
        source = tp_index ^ mask
        block_gain = lax.dynamic_slice_in_dim(gain, source * width, width, 0)
        block_weight = lax.dynamic_slice_in_dim(next_query_weight, source * width, width, 0)
        normed = (widened[mask] * scale * block_gain).astype(jnp.bfloat16)
        part = jnp.dot(normed, block_weight, preferred_element_type=jnp.float32)
        next_sums = part if next_sums is None else next_sums + part
    return (new_residual, next_sums.astype(jnp.bfloat16))


def solution(mesh):
    n_req = mesh.shape["req"]
    n_tp = mesh.shape["tp"]

    def body(*args):
        return local(*args, n_req=n_req, n_tp=n_tp)

    return jax.shard_map(
        body,
        mesh=mesh,
        in_specs=(
            P("req", "tp"),
            P("req", "tp"),
            P("req", "tp", None),
            P("req", "tp", None),
            P("tp", None),
            P(),
            P(None, "tp"),
            P("req", None),
            P("req", None),
            P(),
        ),
        out_specs=(P("req", "tp"), P("req", "tp")),
        check_vma=False,
    )
```

```python
import jax
import jax.numpy as jnp
from jax import lax
from jax.experimental import pallas as pl
from jax.experimental.pallas import tpu as pltpu
from jax.sharding import PartitionSpec as P

QH = 20
KVH = 5
HD = 64
TENANTS = 4
MOSTLEN = 128
GATHER_SLOTS_MAX = 16


def from_root(block, axis, source):
    block = jnp.where(lax.axis_index(axis) == source, block, jnp.zeros_like(block))
    return lax.psum(block, axis)


def pick_heads(pair_rows, select):
    split_pair = pair_rows.reshape(pair_rows.shape[0], 2, 2, HD)
    key_heads = jnp.einsum(
        "njd,hj->nhd", split_pair[:, :, 0], select, preferred_element_type=jnp.float32
    ).astype(jnp.bfloat16)
    value_heads = jnp.einsum(
        "njd,hj->nhd", split_pair[:, :, 1], select, preferred_element_type=jnp.float32
    ).astype(jnp.bfloat16)
    return (key_heads, value_heads)


def xor_permute(block, mask, n_req):
    pairs = [(source, source ^ mask) for source in range(n_req)]
    return lax.ppermute(block, "req", pairs)


def tenant_slots(own_slot, owners, n_req):
    if n_req <= GATHER_SLOTS_MAX and n_req % 2 == 0 and (n_req & (n_req - 1)) == 0:
        req_index = lax.axis_index("req")
        mine = [own_slot] + [
            xor_permute(own_slot, 2 * chip_mask, n_req) for chip_mask in range(1, n_req // 2)
        ]
        theirs = [xor_permute(block, 1, n_req) for block in mine]
        slots = jnp.concatenate(
            [block for pair in zip(mine, theirs) for block in pair], axis=0
        )
        chip_offset = (owners // 2) ^ (req_index // 2)
        other_core = (owners % 2) != (req_index % 2)
        return slots, 2 * chip_offset + other_core.astype(jnp.int32)
    blocks = [from_root(own_slot, "req", owners[tenant_id]) for tenant_id in range(TENANTS)]
    return jnp.concatenate(blocks, axis=0), jnp.arange(TENANTS, dtype=jnp.int32)


def attention_kernel(
    slot_ref, first_ref, start_ref, query_ref, prefix_ref, suffix_ref, row_ref, pair_ref, out_ref
):
    request = pl.program_id(0)
    first = first_ref[request]
    start = start_ref[request]
    spread = query_ref[...]
    pair_lanes = 2 * HD
    prefix_keys = prefix_ref[:, :pair_lanes]
    prefix_values = prefix_ref[:, pair_lanes:]
    suffix_keys = suffix_ref[:, :pair_lanes]
    suffix_values = suffix_ref[:, pair_lanes:]
    contract = (((1,), (1,)), ((), ()))
    score_scale = HD ** (-0.5)
    prefix_scores = lax.dot_general(
        spread, prefix_keys, contract, preferred_element_type=jnp.float32
    ) * score_scale
    suffix_scores = lax.dot_general(
        spread, suffix_keys, contract, preferred_element_type=jnp.float32
    ) * score_scale
    key_position = first + lax.broadcasted_iota(jnp.int32, suffix_scores.shape, 1)
    query_position = first + row_ref[...]
    allowed = (key_position >= start) & (key_position <= query_position)
    suffix_scores = jnp.where(allowed, suffix_scores, -jnp.inf)
    row_top = jnp.maximum(
        jnp.max(prefix_scores, axis=1, keepdims=True),
        jnp.max(suffix_scores, axis=1, keepdims=True),
    )
    prefix_weights = jnp.exp(prefix_scores - row_top)
    suffix_weights = jnp.where(allowed, jnp.exp(suffix_scores - row_top), 0.0)
    denominator = jnp.sum(prefix_weights, axis=1, keepdims=True) + jnp.sum(
        suffix_weights, axis=1, keepdims=True
    )
    accumulated = jnp.dot(
        prefix_weights.astype(jnp.bfloat16), prefix_values, preferred_element_type=jnp.float32
    ) + jnp.dot(
        suffix_weights.astype(jnp.bfloat16), suffix_values, preferred_element_type=jnp.float32
    )
    attended = accumulated / denominator
    first_pair = attended[:, :HD]
    second_pair = attended[:, HD:]
    picked = jnp.where(pair_ref[...] > 0, second_pair, first_pair).astype(out_ref.dtype)
    window = out_ref.shape[0]
    for head in range(out_ref.shape[1] // HD):
        out_ref[:, head * HD:(head + 1) * HD] = picked[head * window:(head + 1) * window]


def window_attention(
    slot_index, firsts, starts, spread, slots, suffix_windows, query_rows, row_pairs, slot_rows
):
    requests, flat_rows, query_lanes = spread.shape
    window = suffix_windows.shape[1]
    lanes = slots.shape[1]
    head_count = flat_rows // window
    grid_spec = pltpu.PrefetchScalarGridSpec(
        num_scalar_prefetch=3,
        grid=(requests,),
        in_specs=[
            pl.BlockSpec((None, flat_rows, query_lanes), lambda k, slot, first, start: (k, 0, 0)),
            pl.BlockSpec((slot_rows, lanes), lambda k, slot, first, start: (slot[k], 0)),
            pl.BlockSpec((None, window, lanes), lambda k, slot, first, start: (k, 0, 0)),
            pl.BlockSpec((flat_rows, 1), lambda k, slot, first, start: (0, 0)),
            pl.BlockSpec((flat_rows, 1), lambda k, slot, first, start: (0, 0)),
        ],
        out_specs=pl.BlockSpec(
            (None, window, head_count * HD), lambda k, slot, first, start: (k, 0, 0)
        ),
    )
    return pl.pallas_call(
        attention_kernel,
        grid_spec=grid_spec,
        out_shape=jax.ShapeDtypeStruct((requests, window, head_count * HD), jnp.bfloat16),
    )(slot_index, firsts, starts, spread, slots, suffix_windows, query_rows, row_pairs)


def xor_tp(block, mask, n_tp):
    pairs = [(source, source ^ mask) for source in range(n_tp)]
    return lax.ppermute(block, "tp", pairs)


def from_partners(block, n_tp):
    if n_tp == 4:
        near = xor_tp(block, 1, n_tp)
        across = xor_tp(block, 2, n_tp)
        return [block, near, across, xor_tp(across, 1, n_tp)]
    return [block] + [xor_tp(block, mask, n_tp) for mask in range(1, n_tp)]


def shifted(block, shift, n_tp):
    pairs = [(source, (source + shift) % n_tp) for source in range(n_tp)]
    return lax.ppermute(block, "tp", pairs)


def local(
    residual,
    queries,
    suffix_kv,
    prefix_cache,
    out_weight,
    norm_gain,
    next_query_weight,
    lengths,
    tenant,
    owners,
    n_req,
    n_tp,
):
    row_count = queries.shape[0]
    head_count = queries.shape[1] // HD
    width = residual.shape[1]
    tp_index = lax.axis_index("tp")

    weight_pieces = []
    for mask in range(n_tp):
        partner = tp_index ^ mask
        piece = lax.dynamic_slice_in_dim(out_weight, partner * width, width, 1)
        weight_pieces.append(piece if mask == 0 else xor_tp(piece, mask, n_tp))

    head_ids = tp_index * head_count + jnp.arange(head_count, dtype=jnp.int32)
    pair_ids = head_ids // (QH // KVH) - tp_index
    select = (pair_ids[:, None] == jnp.arange(2, dtype=jnp.int32)[None, :]).astype(jnp.bfloat16)
    req_lengths = lengths[0]
    req_tenant = tenant[0]
    req_ends = jnp.cumsum(req_lengths)
    req_starts = req_ends - req_lengths
    position = jnp.arange(row_count, dtype=jnp.int32)
    request_ids = jnp.sum((position[:, None] >= req_ends[None, :]).astype(jnp.int32), axis=1)
    member = request_ids[:, None] == jnp.arange(req_lengths.shape[0], dtype=jnp.int32)[None, :]
    row_start = jnp.sum(jnp.where(member, req_starts[None, :], 0), axis=1)
    row_tenant = jnp.sum(jnp.where(member, req_tenant[None, :], 0), axis=1)
    score_scale = HD ** (-0.5)
    own_slot = jnp.transpose(
        prefix_cache.reshape(prefix_cache.shape[0], 2, 2, HD), (0, 2, 1, 3)
    ).reshape(prefix_cache.shape[0], -1)
    slots, slot_of_tenant = tenant_slots(own_slot, owners, n_req)
    suffix_rows = jnp.transpose(suffix_kv.reshape(row_count, 2, 2, HD), (0, 2, 1, 3)).reshape(
        row_count, -1
    )
    window = min(MOSTLEN, row_count)
    firsts = jnp.minimum(req_starts, row_count - window).astype(jnp.int32)
    head_select = jnp.transpose(select)[:, :, None, None]
    spreads = []
    suffix_windows = []
    for request in range(req_lengths.shape[0]):
        window_queries = lax.dynamic_slice_in_dim(queries, firsts[request], window, 0)
        window_queries = jnp.transpose(window_queries.reshape(window, head_count, HD), (1, 0, 2))
        spread = jnp.concatenate(
            [window_queries * head_select[0], window_queries * head_select[1]], axis=2
        )
        spreads.append(spread.reshape(head_count * window, 2 * HD))
        suffix_windows.append(lax.dynamic_slice_in_dim(suffix_rows, firsts[request], window, 0))
    query_rows = (jnp.arange(head_count * window, dtype=jnp.int32) % window)[:, None]
    row_pairs = jnp.repeat(pair_ids.astype(jnp.int32), window)[:, None]
    slot_index = slot_of_tenant[req_tenant].astype(jnp.int32)
    results = window_attention(
        slot_index,
        firsts,
        req_starts.astype(jnp.int32),
        jnp.stack(spreads),
        slots,
        jnp.stack(suffix_windows),
        query_rows,
        row_pairs,
        own_slot.shape[0],
    )
    attended = jnp.zeros((row_count, head_count * HD), jnp.bfloat16)
    for request in range(req_lengths.shape[0]):
        placed = lax.dynamic_update_slice_in_dim(
            jnp.zeros_like(attended), results[request], firsts[request], 0
        )
        attended = jnp.where((request_ids == request)[:, None], placed, attended)

    head_blocks = from_partners(attended, n_tp)
    projected = None
    for mask in range(n_tp):
        part = jnp.dot(head_blocks[mask], weight_pieces[mask], preferred_element_type=jnp.float32)
        projected = part if projected is None else projected + part
    new_residual = (residual.astype(jnp.float32) + projected).astype(jnp.bfloat16)

    blocks = from_partners(new_residual, n_tp)
    widened = [block.astype(jnp.float32) for block in blocks]
    square_sums = sum(jnp.sum(block * block, axis=1, keepdims=True) for block in widened)
    mean_square = square_sums / (width * n_tp)
    scale = lax.rsqrt(mean_square + 1e-05)
    gain = norm_gain.astype(jnp.float32)
    next_sums = None
    for mask in range(n_tp):
        source = tp_index ^ mask
        block_gain = lax.dynamic_slice_in_dim(gain, source * width, width, 0)
        block_weight = lax.dynamic_slice_in_dim(next_query_weight, source * width, width, 0)
        normed = (widened[mask] * scale * block_gain).astype(jnp.bfloat16)
        part = jnp.dot(normed, block_weight, preferred_element_type=jnp.float32)
        next_sums = part if next_sums is None else next_sums + part
    return (new_residual, next_sums.astype(jnp.bfloat16))


def solution(mesh):
    n_req = mesh.shape["req"]
    n_tp = mesh.shape["tp"]

    def body(*args):
        return local(*args, n_req=n_req, n_tp=n_tp)

    return jax.shard_map(
        body,
        mesh=mesh,
        in_specs=(
            P("req", "tp"),
            P("req", "tp"),
            P("req", "tp", None),
            P("req", "tp", None),
            P("tp", None),
            P(),
            P(None, "tp"),
            P("req", None),
            P("req", None),
            P(),
        ),
        out_specs=(P("req", "tp"), P("req", "tp")),
        check_vma=False,
    )
```

```python
import jax
import jax.numpy as jnp
from jax import lax
from jax.experimental import pallas as pl
from jax.experimental.pallas import tpu as pltpu
from jax.sharding import PartitionSpec as P

QH = 20
KVH = 5
HD = 64
TENANTS = 4
MOSTLEN = 128
GATHER_SLOTS_MAX = 16


def from_root(block, axis, source):
    block = jnp.where(lax.axis_index(axis) == source, block, jnp.zeros_like(block))
    return lax.psum(block, axis)


def pick_heads(pair_rows, select):
    split_pair = pair_rows.reshape(pair_rows.shape[0], 2, 2, HD)
    key_heads = jnp.einsum(
        "njd,hj->nhd", split_pair[:, :, 0], select, preferred_element_type=jnp.float32
    ).astype(jnp.bfloat16)
    value_heads = jnp.einsum(
        "njd,hj->nhd", split_pair[:, :, 1], select, preferred_element_type=jnp.float32
    ).astype(jnp.bfloat16)
    return (key_heads, value_heads)


def xor_permute(block, mask, n_req):
    pairs = [(source, source ^ mask) for source in range(n_req)]
    return lax.ppermute(block, "req", pairs)


def tenant_slots(own_slot, owners, n_req):
    if n_req <= GATHER_SLOTS_MAX and n_req % 2 == 0 and (n_req & (n_req - 1)) == 0:
        req_index = lax.axis_index("req")
        mine = [own_slot] + [
            xor_permute(own_slot, 2 * chip_mask, n_req) for chip_mask in range(1, n_req // 2)
        ]
        farthest = n_req // 2 - 1
        theirs = [xor_permute(block, 1, n_req) for block in mine[:farthest]]
        theirs.append(xor_permute(own_slot, 2 * farthest + 1, n_req))
        slots = jnp.concatenate(
            [block for pair in zip(mine, theirs) for block in pair], axis=0
        )
        chip_offset = (owners // 2) ^ (req_index // 2)
        other_core = (owners % 2) != (req_index % 2)
        return slots, 2 * chip_offset + other_core.astype(jnp.int32)
    blocks = [from_root(own_slot, "req", owners[tenant_id]) for tenant_id in range(TENANTS)]
    return jnp.concatenate(blocks, axis=0), jnp.arange(TENANTS, dtype=jnp.int32)


def attention_kernel(
    slot_ref, first_ref, start_ref, query_ref, prefix_ref, suffix_ref, row_ref, pair_ref, out_ref
):
    request = pl.program_id(0)
    first = first_ref[request]
    start = start_ref[request]
    spread = query_ref[...]
    pair_lanes = 2 * HD
    prefix_keys = prefix_ref[:, :pair_lanes]
    prefix_values = prefix_ref[:, pair_lanes:]
    suffix_keys = suffix_ref[:, :pair_lanes]
    suffix_values = suffix_ref[:, pair_lanes:]
    contract = (((1,), (1,)), ((), ()))
    score_scale = HD ** (-0.5)
    prefix_scores = lax.dot_general(
        spread, prefix_keys, contract, preferred_element_type=jnp.float32
    ) * score_scale
    suffix_scores = lax.dot_general(
        spread, suffix_keys, contract, preferred_element_type=jnp.float32
    ) * score_scale
    key_position = first + lax.broadcasted_iota(jnp.int32, suffix_scores.shape, 1)
    query_position = first + row_ref[...]
    allowed = (key_position >= start) & (key_position <= query_position)
    suffix_scores = jnp.where(allowed, suffix_scores, -jnp.inf)
    row_top = jnp.maximum(
        jnp.max(prefix_scores, axis=1, keepdims=True),
        jnp.max(suffix_scores, axis=1, keepdims=True),
    )
    prefix_weights = jnp.exp(prefix_scores - row_top)
    suffix_weights = jnp.where(allowed, jnp.exp(suffix_scores - row_top), 0.0)
    denominator = jnp.sum(prefix_weights, axis=1, keepdims=True) + jnp.sum(
        suffix_weights, axis=1, keepdims=True
    )
    accumulated = jnp.dot(
        prefix_weights.astype(jnp.bfloat16), prefix_values, preferred_element_type=jnp.float32
    ) + jnp.dot(
        suffix_weights.astype(jnp.bfloat16), suffix_values, preferred_element_type=jnp.float32
    )
    attended = accumulated / denominator
    first_pair = attended[:, :HD]
    second_pair = attended[:, HD:]
    out_ref[...] = jnp.where(pair_ref[...] > 0, second_pair, first_pair).astype(out_ref.dtype)


def window_attention(
    slot_index, firsts, starts, spread, slots, suffix_windows, query_rows, row_pairs, slot_rows
):
    requests, flat_rows, query_lanes = spread.shape
    window = suffix_windows.shape[1]
    lanes = slots.shape[1]
    grid_spec = pltpu.PrefetchScalarGridSpec(
        num_scalar_prefetch=3,
        grid=(requests,),
        in_specs=[
            pl.BlockSpec((None, flat_rows, query_lanes), lambda k, slot, first, start: (k, 0, 0)),
            pl.BlockSpec((slot_rows, lanes), lambda k, slot, first, start: (slot[k], 0)),
            pl.BlockSpec((None, window, lanes), lambda k, slot, first, start: (k, 0, 0)),
            pl.BlockSpec((flat_rows, 1), lambda k, slot, first, start: (0, 0)),
            pl.BlockSpec((flat_rows, 1), lambda k, slot, first, start: (0, 0)),
        ],
        out_specs=pl.BlockSpec((None, flat_rows, HD), lambda k, slot, first, start: (k, 0, 0)),
    )
    return pl.pallas_call(
        attention_kernel,
        grid_spec=grid_spec,
        out_shape=jax.ShapeDtypeStruct((requests, flat_rows, HD), jnp.bfloat16),
    )(slot_index, firsts, starts, spread, slots, suffix_windows, query_rows, row_pairs)


def xor_tp(block, mask, n_tp):
    pairs = [(source, source ^ mask) for source in range(n_tp)]
    return lax.ppermute(block, "tp", pairs)


def from_partners(block, n_tp):
    if n_tp == 4:
        near = xor_tp(block, 1, n_tp)
        across = xor_tp(block, 2, n_tp)
        return [block, near, across, xor_tp(across, 1, n_tp)]
    return [block] + [xor_tp(block, mask, n_tp) for mask in range(1, n_tp)]


def shifted(block, shift, n_tp):
    pairs = [(source, (source + shift) % n_tp) for source in range(n_tp)]
    return lax.ppermute(block, "tp", pairs)


def local(
    residual,
    queries,
    suffix_kv,
    prefix_cache,
    out_weight,
    norm_gain,
    next_query_weight,
    lengths,
    tenant,
    owners,
    n_req,
    n_tp,
):
    row_count = queries.shape[0]
    head_count = queries.shape[1] // HD
    width = residual.shape[1]
    tp_index = lax.axis_index("tp")

    weight_pieces = []
    for mask in range(n_tp):
        partner = tp_index ^ mask
        piece = lax.dynamic_slice_in_dim(out_weight, partner * width, width, 1)
        weight_pieces.append(piece if mask == 0 else xor_tp(piece, mask, n_tp))

    head_ids = tp_index * head_count + jnp.arange(head_count, dtype=jnp.int32)
    pair_ids = head_ids // (QH // KVH) - tp_index
    select = (pair_ids[:, None] == jnp.arange(2, dtype=jnp.int32)[None, :]).astype(jnp.bfloat16)
    req_lengths = lengths[0]
    req_tenant = tenant[0]
    req_ends = jnp.cumsum(req_lengths)
    req_starts = req_ends - req_lengths
    position = jnp.arange(row_count, dtype=jnp.int32)
    request_ids = jnp.sum((position[:, None] >= req_ends[None, :]).astype(jnp.int32), axis=1)
    member = request_ids[:, None] == jnp.arange(req_lengths.shape[0], dtype=jnp.int32)[None, :]
    row_start = jnp.sum(jnp.where(member, req_starts[None, :], 0), axis=1)
    row_tenant = jnp.sum(jnp.where(member, req_tenant[None, :], 0), axis=1)
    score_scale = HD ** (-0.5)
    own_slot = jnp.transpose(
        prefix_cache.reshape(prefix_cache.shape[0], 2, 2, HD), (0, 2, 1, 3)
    ).reshape(prefix_cache.shape[0], -1)
    slots, slot_of_tenant = tenant_slots(own_slot, owners, n_req)
    suffix_rows = jnp.transpose(suffix_kv.reshape(row_count, 2, 2, HD), (0, 2, 1, 3)).reshape(
        row_count, -1
    )
    window = min(MOSTLEN, row_count)
    firsts = jnp.minimum(req_starts, row_count - window).astype(jnp.int32)
    head_select = jnp.transpose(select)[:, :, None, None]
    spreads = []
    suffix_windows = []
    for request in range(req_lengths.shape[0]):
        window_queries = lax.dynamic_slice_in_dim(queries, firsts[request], window, 0)
        window_queries = jnp.transpose(window_queries.reshape(window, head_count, HD), (1, 0, 2))
        spread = jnp.concatenate(
            [window_queries * head_select[0], window_queries * head_select[1]], axis=2
        )
        spreads.append(spread.reshape(head_count * window, 2 * HD))
        suffix_windows.append(lax.dynamic_slice_in_dim(suffix_rows, firsts[request], window, 0))
    query_rows = (jnp.arange(head_count * window, dtype=jnp.int32) % window)[:, None]
    row_pairs = jnp.repeat(pair_ids.astype(jnp.int32), window)[:, None]
    slot_index = slot_of_tenant[req_tenant].astype(jnp.int32)
    results = window_attention(
        slot_index,
        firsts,
        req_starts.astype(jnp.int32),
        jnp.stack(spreads),
        slots,
        jnp.stack(suffix_windows),
        query_rows,
        row_pairs,
        own_slot.shape[0],
    ).reshape(-1, head_count, window, HD)
    attended = jnp.zeros((row_count, head_count * HD), jnp.bfloat16)
    for request in range(req_lengths.shape[0]):
        window_attended = jnp.transpose(results[request], (1, 0, 2)).reshape(window, -1)
        placed = lax.dynamic_update_slice_in_dim(
            jnp.zeros_like(attended), window_attended, firsts[request], 0
        )
        attended = jnp.where((request_ids == request)[:, None], placed, attended)

    head_blocks = from_partners(attended, n_tp)
    projected = None
    for mask in range(n_tp):
        part = jnp.dot(head_blocks[mask], weight_pieces[mask], preferred_element_type=jnp.float32)
        projected = part if projected is None else projected + part
    new_residual = (residual.astype(jnp.float32) + projected).astype(jnp.bfloat16)

    blocks = from_partners(new_residual, n_tp)
    widened = [block.astype(jnp.float32) for block in blocks]
    square_sums = sum(jnp.sum(block * block, axis=1, keepdims=True) for block in widened)
    mean_square = square_sums / (width * n_tp)
    scale = lax.rsqrt(mean_square + 1e-05)
    gain = norm_gain.astype(jnp.float32)
    next_sums = None
    for mask in range(n_tp):
        source = tp_index ^ mask
        block_gain = lax.dynamic_slice_in_dim(gain, source * width, width, 0)
        block_weight = lax.dynamic_slice_in_dim(next_query_weight, source * width, width, 0)
        normed = (widened[mask] * scale * block_gain).astype(jnp.bfloat16)
        part = jnp.dot(normed, block_weight, preferred_element_type=jnp.float32)
        next_sums = part if next_sums is None else next_sums + part
    return (new_residual, next_sums.astype(jnp.bfloat16))


def solution(mesh):
    n_req = mesh.shape["req"]
    n_tp = mesh.shape["tp"]

    def body(*args):
        return local(*args, n_req=n_req, n_tp=n_tp)

    return jax.shard_map(
        body,
        mesh=mesh,
        in_specs=(
            P("req", "tp"),
            P("req", "tp"),
            P("req", "tp", None),
            P("req", "tp", None),
            P("tp", None),
            P(),
            P(None, "tp"),
            P("req", None),
            P("req", None),
            P(),
        ),
        out_specs=(P("req", "tp"), P("req", "tp")),
        check_vma=False,
    )
```

```python
import jax
import jax.numpy as jnp
from jax import lax
from jax.experimental import pallas as pl
from jax.experimental.pallas import tpu as pltpu
from jax.sharding import PartitionSpec as P

QH = 20
KVH = 5
HD = 64
TENANTS = 4
MOSTLEN = 128
GATHER_SLOTS_MAX = 16


def from_root(block, axis, source):
    block = jnp.where(lax.axis_index(axis) == source, block, jnp.zeros_like(block))
    return lax.psum(block, axis)


def pick_heads(pair_rows, select):
    split_pair = pair_rows.reshape(pair_rows.shape[0], 2, 2, HD)
    key_heads = jnp.einsum(
        "njd,hj->nhd", split_pair[:, :, 0], select, preferred_element_type=jnp.float32
    ).astype(jnp.bfloat16)
    value_heads = jnp.einsum(
        "njd,hj->nhd", split_pair[:, :, 1], select, preferred_element_type=jnp.float32
    ).astype(jnp.bfloat16)
    return (key_heads, value_heads)


def xor_permute(block, mask, n_req):
    pairs = [(source, source ^ mask) for source in range(n_req)]
    return lax.ppermute(block, "req", pairs)


def keys_first(block):
    rows = block.shape[0]
    return jnp.transpose(block.reshape(rows, 2, 2, HD), (0, 2, 1, 3)).reshape(rows, -1)


def tenant_slots(own_slot, owners, n_req):
    if n_req <= GATHER_SLOTS_MAX and n_req % 2 == 0 and (n_req & (n_req - 1)) == 0:
        req_index = lax.axis_index("req")
        mine = [own_slot] + [
            xor_permute(own_slot, 2 * chip_mask, n_req) for chip_mask in range(1, n_req // 2)
        ]
        theirs = [xor_permute(block, 1, n_req) for block in mine]
        slots = jnp.concatenate(
            [keys_first(block) for pair in zip(mine, theirs) for block in pair], axis=0
        )
        chip_offset = (owners // 2) ^ (req_index // 2)
        other_core = (owners % 2) != (req_index % 2)
        return slots, 2 * chip_offset + other_core.astype(jnp.int32)
    blocks = [from_root(own_slot, "req", owners[tenant_id]) for tenant_id in range(TENANTS)]
    slots = jnp.concatenate([keys_first(block) for block in blocks], axis=0)
    return slots, jnp.arange(TENANTS, dtype=jnp.int32)


def attention_kernel(
    slot_ref, first_ref, start_ref, query_ref, prefix_ref, suffix_ref, row_ref, pair_ref, out_ref
):
    request = pl.program_id(0)
    first = first_ref[request]
    start = start_ref[request]
    spread = query_ref[...]
    pair_lanes = 2 * HD
    prefix_keys = prefix_ref[:, :pair_lanes]
    prefix_values = prefix_ref[:, pair_lanes:]
    suffix_keys = suffix_ref[:, :pair_lanes]
    suffix_values = suffix_ref[:, pair_lanes:]
    contract = (((1,), (1,)), ((), ()))
    score_scale = HD ** (-0.5)
    prefix_scores = lax.dot_general(
        spread, prefix_keys, contract, preferred_element_type=jnp.float32
    ) * score_scale
    suffix_scores = lax.dot_general(
        spread, suffix_keys, contract, preferred_element_type=jnp.float32
    ) * score_scale
    key_position = first + lax.broadcasted_iota(jnp.int32, suffix_scores.shape, 1)
    query_position = first + row_ref[...]
    allowed = (key_position >= start) & (key_position <= query_position)
    suffix_scores = jnp.where(allowed, suffix_scores, -jnp.inf)
    row_top = jnp.maximum(
        jnp.max(prefix_scores, axis=1, keepdims=True),
        jnp.max(suffix_scores, axis=1, keepdims=True),
    )
    prefix_weights = jnp.exp(prefix_scores - row_top)
    suffix_weights = jnp.where(allowed, jnp.exp(suffix_scores - row_top), 0.0)
    denominator = jnp.sum(prefix_weights, axis=1, keepdims=True) + jnp.sum(
        suffix_weights, axis=1, keepdims=True
    )
    accumulated = jnp.dot(
        prefix_weights.astype(jnp.bfloat16), prefix_values, preferred_element_type=jnp.float32
    ) + jnp.dot(
        suffix_weights.astype(jnp.bfloat16), suffix_values, preferred_element_type=jnp.float32
    )
    attended = accumulated / denominator
    first_pair = attended[:, :HD]
    second_pair = attended[:, HD:]
    out_ref[...] = jnp.where(pair_ref[...] > 0, second_pair, first_pair).astype(out_ref.dtype)


def window_attention(
    slot_index, firsts, starts, spread, slots, suffix_windows, query_rows, row_pairs, slot_rows
):
    requests, flat_rows, query_lanes = spread.shape
    window = suffix_windows.shape[1]
    lanes = slots.shape[1]
    grid_spec = pltpu.PrefetchScalarGridSpec(
        num_scalar_prefetch=3,
        grid=(requests,),
        in_specs=[
            pl.BlockSpec((None, flat_rows, query_lanes), lambda k, slot, first, start: (k, 0, 0)),
            pl.BlockSpec((slot_rows, lanes), lambda k, slot, first, start: (slot[k], 0)),
            pl.BlockSpec((None, window, lanes), lambda k, slot, first, start: (k, 0, 0)),
            pl.BlockSpec((flat_rows, 1), lambda k, slot, first, start: (0, 0)),
            pl.BlockSpec((flat_rows, 1), lambda k, slot, first, start: (0, 0)),
        ],
        out_specs=pl.BlockSpec((None, flat_rows, HD), lambda k, slot, first, start: (k, 0, 0)),
    )
    return pl.pallas_call(
        attention_kernel,
        grid_spec=grid_spec,
        out_shape=jax.ShapeDtypeStruct((requests, flat_rows, HD), jnp.bfloat16),
    )(slot_index, firsts, starts, spread, slots, suffix_windows, query_rows, row_pairs)


def xor_tp(block, mask, n_tp):
    pairs = [(source, source ^ mask) for source in range(n_tp)]
    return lax.ppermute(block, "tp", pairs)


def from_partners(block, n_tp):
    if n_tp == 4:
        near = xor_tp(block, 1, n_tp)
        across = xor_tp(block, 2, n_tp)
        return [block, near, across, xor_tp(across, 1, n_tp)]
    return [block] + [xor_tp(block, mask, n_tp) for mask in range(1, n_tp)]


def shifted(block, shift, n_tp):
    pairs = [(source, (source + shift) % n_tp) for source in range(n_tp)]
    return lax.ppermute(block, "tp", pairs)


def local(
    residual,
    queries,
    suffix_kv,
    prefix_cache,
    out_weight,
    norm_gain,
    next_query_weight,
    lengths,
    tenant,
    owners,
    n_req,
    n_tp,
):
    row_count = queries.shape[0]
    head_count = queries.shape[1] // HD
    width = residual.shape[1]
    tp_index = lax.axis_index("tp")

    weight_pieces = []
    for mask in range(n_tp):
        partner = tp_index ^ mask
        piece = lax.dynamic_slice_in_dim(out_weight, partner * width, width, 1)
        weight_pieces.append(piece if mask == 0 else xor_tp(piece, mask, n_tp))

    head_ids = tp_index * head_count + jnp.arange(head_count, dtype=jnp.int32)
    pair_ids = head_ids // (QH // KVH) - tp_index
    select = (pair_ids[:, None] == jnp.arange(2, dtype=jnp.int32)[None, :]).astype(jnp.bfloat16)
    req_lengths = lengths[0]
    req_tenant = tenant[0]
    req_ends = jnp.cumsum(req_lengths)
    req_starts = req_ends - req_lengths
    position = jnp.arange(row_count, dtype=jnp.int32)
    request_ids = jnp.sum((position[:, None] >= req_ends[None, :]).astype(jnp.int32), axis=1)
    member = request_ids[:, None] == jnp.arange(req_lengths.shape[0], dtype=jnp.int32)[None, :]
    row_start = jnp.sum(jnp.where(member, req_starts[None, :], 0), axis=1)
    row_tenant = jnp.sum(jnp.where(member, req_tenant[None, :], 0), axis=1)
    score_scale = HD ** (-0.5)
    own_slot = prefix_cache.reshape(prefix_cache.shape[0], -1)
    slots, slot_of_tenant = tenant_slots(own_slot, owners, n_req)
    suffix_rows = jnp.transpose(suffix_kv.reshape(row_count, 2, 2, HD), (0, 2, 1, 3)).reshape(
        row_count, -1
    )
    window = min(MOSTLEN, row_count)
    firsts = jnp.minimum(req_starts, row_count - window).astype(jnp.int32)
    head_select = jnp.transpose(select)[:, :, None, None]
    spreads = []
    suffix_windows = []
    for request in range(req_lengths.shape[0]):
        window_queries = lax.dynamic_slice_in_dim(queries, firsts[request], window, 0)
        window_queries = jnp.transpose(window_queries.reshape(window, head_count, HD), (1, 0, 2))
        spread = jnp.concatenate(
            [window_queries * head_select[0], window_queries * head_select[1]], axis=2
        )
        spreads.append(spread.reshape(head_count * window, 2 * HD))
        suffix_windows.append(lax.dynamic_slice_in_dim(suffix_rows, firsts[request], window, 0))
    query_rows = (jnp.arange(head_count * window, dtype=jnp.int32) % window)[:, None]
    row_pairs = jnp.repeat(pair_ids.astype(jnp.int32), window)[:, None]
    slot_index = slot_of_tenant[req_tenant].astype(jnp.int32)
    results = window_attention(
        slot_index,
        firsts,
        req_starts.astype(jnp.int32),
        jnp.stack(spreads),
        slots,
        jnp.stack(suffix_windows),
        query_rows,
        row_pairs,
        own_slot.shape[0],
    ).reshape(-1, head_count, window, HD)
    attended = jnp.zeros((row_count, head_count * HD), jnp.bfloat16)
    for request in range(req_lengths.shape[0]):
        window_attended = jnp.transpose(results[request], (1, 0, 2)).reshape(window, -1)
        placed = lax.dynamic_update_slice_in_dim(
            jnp.zeros_like(attended), window_attended, firsts[request], 0
        )
        attended = jnp.where((request_ids == request)[:, None], placed, attended)

    head_blocks = from_partners(attended, n_tp)
    projected = None
    for mask in range(n_tp):
        part = jnp.dot(head_blocks[mask], weight_pieces[mask], preferred_element_type=jnp.float32)
        projected = part if projected is None else projected + part
    new_residual = (residual.astype(jnp.float32) + projected).astype(jnp.bfloat16)

    blocks = from_partners(new_residual, n_tp)
    widened = [block.astype(jnp.float32) for block in blocks]
    square_sums = sum(jnp.sum(block * block, axis=1, keepdims=True) for block in widened)
    mean_square = square_sums / (width * n_tp)
    scale = lax.rsqrt(mean_square + 1e-05)
    gain = norm_gain.astype(jnp.float32)
    next_sums = None
    for mask in range(n_tp):
        source = tp_index ^ mask
        block_gain = lax.dynamic_slice_in_dim(gain, source * width, width, 0)
        block_weight = lax.dynamic_slice_in_dim(next_query_weight, source * width, width, 0)
        normed = (widened[mask] * scale * block_gain).astype(jnp.bfloat16)
        part = jnp.dot(normed, block_weight, preferred_element_type=jnp.float32)
        next_sums = part if next_sums is None else next_sums + part
    return (new_residual, next_sums.astype(jnp.bfloat16))


def solution(mesh):
    n_req = mesh.shape["req"]
    n_tp = mesh.shape["tp"]

    def body(*args):
        return local(*args, n_req=n_req, n_tp=n_tp)

    return jax.shard_map(
        body,
        mesh=mesh,
        in_specs=(
            P("req", "tp"),
            P("req", "tp"),
            P("req", "tp", None),
            P("req", "tp", None),
            P("tp", None),
            P(),
            P(None, "tp"),
            P("req", None),
            P("req", None),
            P(),
        ),
        out_specs=(P("req", "tp"), P("req", "tp")),
        check_vma=False,
    )
```

```python
import jax
import jax.numpy as jnp
from jax import lax
from jax.experimental import pallas as pl
from jax.experimental.pallas import tpu as pltpu
from jax.sharding import PartitionSpec as P

QH = 20
KVH = 5
HD = 64
TENANTS = 4
MOSTLEN = 128
GATHER_SLOTS_MAX = 16


def from_root(block, axis, source):
    block = jnp.where(lax.axis_index(axis) == source, block, jnp.zeros_like(block))
    return lax.psum(block, axis)


def pick_heads(pair_rows, select):
    split_pair = pair_rows.reshape(pair_rows.shape[0], 2, 2, HD)
    key_heads = jnp.einsum(
        "njd,hj->nhd", split_pair[:, :, 0], select, preferred_element_type=jnp.float32
    ).astype(jnp.bfloat16)
    value_heads = jnp.einsum(
        "njd,hj->nhd", split_pair[:, :, 1], select, preferred_element_type=jnp.float32
    ).astype(jnp.bfloat16)
    return (key_heads, value_heads)


def xor_permute(block, mask, n_req):
    pairs = [(source, source ^ mask) for source in range(n_req)]
    return lax.ppermute(block, "req", pairs)


def tenant_slots(own_slot, owners, n_req):
    if n_req <= GATHER_SLOTS_MAX and n_req % 2 == 0 and (n_req & (n_req - 1)) == 0:
        req_index = lax.axis_index("req")
        mine = [own_slot] + [
            xor_permute(own_slot, 2 * chip_mask, n_req) for chip_mask in range(1, n_req // 2)
        ]
        theirs = [xor_permute(block, 1, n_req) for block in mine]
        slots = jnp.concatenate(
            [block for pair in zip(mine, theirs) for block in pair], axis=0
        )
        chip_offset = (owners // 2) ^ (req_index // 2)
        other_core = (owners % 2) != (req_index % 2)
        return slots, 2 * chip_offset + other_core.astype(jnp.int32)
    blocks = [from_root(own_slot, "req", owners[tenant_id]) for tenant_id in range(TENANTS)]
    return jnp.concatenate(blocks, axis=0), jnp.arange(TENANTS, dtype=jnp.int32)


def attention_kernel(
    slot_ref, first_ref, start_ref, query_ref, prefix_ref, suffix_ref, row_ref, pair_ref, out_ref
):
    request = pl.program_id(0)
    first = first_ref[request]
    start = start_ref[request]
    spread = query_ref[...]
    pair_lanes = 2 * HD
    prefix_keys = prefix_ref[:, :pair_lanes]
    prefix_values = prefix_ref[:, pair_lanes:]
    suffix_keys = suffix_ref[:, :pair_lanes]
    suffix_values = suffix_ref[:, pair_lanes:]
    contract = (((1,), (1,)), ((), ()))
    prefix_scores = lax.dot_general(
        spread, prefix_keys, contract, preferred_element_type=jnp.float32
    )
    suffix_scores = lax.dot_general(
        spread, suffix_keys, contract, preferred_element_type=jnp.float32
    )
    key_position = first + lax.broadcasted_iota(jnp.int32, suffix_scores.shape, 1)
    query_position = first + row_ref[...]
    allowed = (key_position >= start) & (key_position <= query_position)
    suffix_scores = jnp.where(allowed, suffix_scores, -jnp.inf)
    row_top = jnp.maximum(
        jnp.max(prefix_scores, axis=1, keepdims=True),
        jnp.max(suffix_scores, axis=1, keepdims=True),
    )
    prefix_weights = jnp.exp(prefix_scores - row_top)
    suffix_weights = jnp.exp(suffix_scores - row_top)
    denominator = jnp.sum(prefix_weights, axis=1, keepdims=True) + jnp.sum(
        suffix_weights, axis=1, keepdims=True
    )
    accumulated = jnp.dot(
        prefix_weights.astype(jnp.bfloat16), prefix_values, preferred_element_type=jnp.float32
    ) + jnp.dot(
        suffix_weights.astype(jnp.bfloat16), suffix_values, preferred_element_type=jnp.float32
    )
    attended = accumulated / denominator
    first_pair = attended[:, :HD]
    second_pair = attended[:, HD:]
    out_ref[...] = jnp.where(pair_ref[...] > 0, second_pair, first_pair).astype(out_ref.dtype)


def window_attention(
    slot_index, firsts, starts, spread, slots, suffix_windows, query_rows, row_pairs, slot_rows
):
    requests, flat_rows, query_lanes = spread.shape
    window = suffix_windows.shape[1]
    lanes = slots.shape[1]
    grid_spec = pltpu.PrefetchScalarGridSpec(
        num_scalar_prefetch=3,
        grid=(requests,),
        in_specs=[
            pl.BlockSpec((None, flat_rows, query_lanes), lambda k, slot, first, start: (k, 0, 0)),
            pl.BlockSpec((slot_rows, lanes), lambda k, slot, first, start: (slot[k], 0)),
            pl.BlockSpec((None, window, lanes), lambda k, slot, first, start: (k, 0, 0)),
            pl.BlockSpec((flat_rows, 1), lambda k, slot, first, start: (0, 0)),
            pl.BlockSpec((flat_rows, 1), lambda k, slot, first, start: (0, 0)),
        ],
        out_specs=pl.BlockSpec((None, flat_rows, HD), lambda k, slot, first, start: (k, 0, 0)),
    )
    return pl.pallas_call(
        attention_kernel,
        grid_spec=grid_spec,
        out_shape=jax.ShapeDtypeStruct((requests, flat_rows, HD), jnp.bfloat16),
    )(slot_index, firsts, starts, spread, slots, suffix_windows, query_rows, row_pairs)


def xor_tp(block, mask, n_tp):
    pairs = [(source, source ^ mask) for source in range(n_tp)]
    return lax.ppermute(block, "tp", pairs)


def from_partners(block, n_tp):
    if n_tp == 4:
        near = xor_tp(block, 1, n_tp)
        across = xor_tp(block, 2, n_tp)
        return [block, near, across, xor_tp(across, 1, n_tp)]
    return [block] + [xor_tp(block, mask, n_tp) for mask in range(1, n_tp)]


def shifted(block, shift, n_tp):
    pairs = [(source, (source + shift) % n_tp) for source in range(n_tp)]
    return lax.ppermute(block, "tp", pairs)


def local(
    residual,
    queries,
    suffix_kv,
    prefix_cache,
    out_weight,
    norm_gain,
    next_query_weight,
    lengths,
    tenant,
    owners,
    n_req,
    n_tp,
):
    row_count = queries.shape[0]
    head_count = queries.shape[1] // HD
    width = residual.shape[1]
    tp_index = lax.axis_index("tp")

    weight_pieces = []
    for mask in range(n_tp):
        partner = tp_index ^ mask
        piece = lax.dynamic_slice_in_dim(out_weight, partner * width, width, 1)
        weight_pieces.append(piece if mask == 0 else xor_tp(piece, mask, n_tp))

    head_ids = tp_index * head_count + jnp.arange(head_count, dtype=jnp.int32)
    pair_ids = head_ids // (QH // KVH) - tp_index
    select = (pair_ids[:, None] == jnp.arange(2, dtype=jnp.int32)[None, :]).astype(jnp.bfloat16)
    req_lengths = lengths[0]
    req_tenant = tenant[0]
    req_ends = jnp.cumsum(req_lengths)
    req_starts = req_ends - req_lengths
    position = jnp.arange(row_count, dtype=jnp.int32)
    request_ids = jnp.sum((position[:, None] >= req_ends[None, :]).astype(jnp.int32), axis=1)
    member = request_ids[:, None] == jnp.arange(req_lengths.shape[0], dtype=jnp.int32)[None, :]
    row_start = jnp.sum(jnp.where(member, req_starts[None, :], 0), axis=1)
    row_tenant = jnp.sum(jnp.where(member, req_tenant[None, :], 0), axis=1)
    score_scale = HD ** (-0.5)
    own_slot = jnp.transpose(
        prefix_cache.reshape(prefix_cache.shape[0], 2, 2, HD), (0, 2, 1, 3)
    ).reshape(prefix_cache.shape[0], -1)
    slots, slot_of_tenant = tenant_slots(own_slot, owners, n_req)
    suffix_rows = jnp.transpose(suffix_kv.reshape(row_count, 2, 2, HD), (0, 2, 1, 3)).reshape(
        row_count, -1
    )
    window = min(MOSTLEN, row_count)
    firsts = jnp.minimum(req_starts, row_count - window).astype(jnp.int32)
    head_select = jnp.transpose(select)[:, :, None, None]
    spreads = []
    suffix_windows = []
    for request in range(req_lengths.shape[0]):
        window_queries = lax.dynamic_slice_in_dim(queries, firsts[request], window, 0)
        window_queries = jnp.transpose(window_queries.reshape(window, head_count, HD), (1, 0, 2))
        spread = jnp.concatenate(
            [window_queries * head_select[0], window_queries * head_select[1]], axis=2
        )
        spreads.append((spread * score_scale).reshape(head_count * window, 2 * HD))
        suffix_windows.append(lax.dynamic_slice_in_dim(suffix_rows, firsts[request], window, 0))
    query_rows = (jnp.arange(head_count * window, dtype=jnp.int32) % window)[:, None]
    row_pairs = jnp.repeat(pair_ids.astype(jnp.int32), window)[:, None]
    slot_index = slot_of_tenant[req_tenant].astype(jnp.int32)
    results = window_attention(
        slot_index,
        firsts,
        req_starts.astype(jnp.int32),
        jnp.stack(spreads),
        slots,
        jnp.stack(suffix_windows),
        query_rows,
        row_pairs,
        own_slot.shape[0],
    ).reshape(-1, head_count, window, HD)
    attended = jnp.zeros((row_count, head_count * HD), jnp.bfloat16)
    for request in range(req_lengths.shape[0]):
        window_attended = jnp.transpose(results[request], (1, 0, 2)).reshape(window, -1)
        placed = lax.dynamic_update_slice_in_dim(
            jnp.zeros_like(attended), window_attended, firsts[request], 0
        )
        attended = jnp.where((request_ids == request)[:, None], placed, attended)

    head_blocks = from_partners(attended, n_tp)
    projected = None
    for mask in range(n_tp):
        part = jnp.dot(head_blocks[mask], weight_pieces[mask], preferred_element_type=jnp.float32)
        projected = part if projected is None else projected + part
    new_residual = (residual.astype(jnp.float32) + projected).astype(jnp.bfloat16)

    blocks = from_partners(new_residual, n_tp)
    widened = [block.astype(jnp.float32) for block in blocks]
    square_sums = sum(jnp.sum(block * block, axis=1, keepdims=True) for block in widened)
    mean_square = square_sums / (width * n_tp)
    scale = lax.rsqrt(mean_square + 1e-05)
    gain = norm_gain.astype(jnp.float32)
    next_sums = None
    for mask in range(n_tp):
        source = tp_index ^ mask
        block_gain = lax.dynamic_slice_in_dim(gain, source * width, width, 0)
        block_weight = lax.dynamic_slice_in_dim(next_query_weight, source * width, width, 0)
        normed = (widened[mask] * scale * block_gain).astype(jnp.bfloat16)
        part = jnp.dot(normed, block_weight, preferred_element_type=jnp.float32)
        next_sums = part if next_sums is None else next_sums + part
    return (new_residual, next_sums.astype(jnp.bfloat16))


def solution(mesh):
    n_req = mesh.shape["req"]
    n_tp = mesh.shape["tp"]

    def body(*args):
        return local(*args, n_req=n_req, n_tp=n_tp)

    return jax.shard_map(
        body,
        mesh=mesh,
        in_specs=(
            P("req", "tp"),
            P("req", "tp"),
            P("req", "tp", None),
            P("req", "tp", None),
            P("tp", None),
            P(),
            P(None, "tp"),
            P("req", None),
            P("req", None),
            P(),
        ),
        out_specs=(P("req", "tp"), P("req", "tp")),
        check_vma=False,
    )
```

```python
import jax
import jax.numpy as jnp
from jax import lax
from jax.experimental import pallas as pl
from jax.experimental.pallas import tpu as pltpu
from jax.sharding import PartitionSpec as P

QH = 20
KVH = 5
HD = 64
TENANTS = 4
MOSTLEN = 128
GATHER_SLOTS_MAX = 16


def from_root(block, axis, source):
    block = jnp.where(lax.axis_index(axis) == source, block, jnp.zeros_like(block))
    return lax.psum(block, axis)


def pick_heads(pair_rows, select):
    split_pair = pair_rows.reshape(pair_rows.shape[0], 2, 2, HD)
    key_heads = jnp.einsum(
        "njd,hj->nhd", split_pair[:, :, 0], select, preferred_element_type=jnp.float32
    ).astype(jnp.bfloat16)
    value_heads = jnp.einsum(
        "njd,hj->nhd", split_pair[:, :, 1], select, preferred_element_type=jnp.float32
    ).astype(jnp.bfloat16)
    return (key_heads, value_heads)


def xor_permute(block, mask, n_req):
    pairs = [(source, source ^ mask) for source in range(n_req)]
    return lax.ppermute(block, "req", pairs)


def tenant_slots(own_slot, owners, n_req):
    if n_req <= GATHER_SLOTS_MAX and n_req % 2 == 0 and (n_req & (n_req - 1)) == 0:
        req_index = lax.axis_index("req")
        mine = [own_slot] + [
            xor_permute(own_slot, 2 * chip_mask, n_req) for chip_mask in range(1, n_req // 2)
        ]
        theirs = [xor_permute(block, 1, n_req) for block in mine]
        slots = jnp.concatenate(
            [block for pair in zip(mine, theirs) for block in pair], axis=0
        )
        chip_offset = (owners // 2) ^ (req_index // 2)
        other_core = (owners % 2) != (req_index % 2)
        return slots, 2 * chip_offset + other_core.astype(jnp.int32)
    blocks = [from_root(own_slot, "req", owners[tenant_id]) for tenant_id in range(TENANTS)]
    return jnp.concatenate(blocks, axis=0), jnp.arange(TENANTS, dtype=jnp.int32)


def attention_kernel(
    slot_ref, first_ref, start_ref, query_ref, prefix_ref, suffix_ref, row_ref, pair_ref, out_ref
):
    request = pl.program_id(0)
    first = first_ref[request]
    start = start_ref[request]
    spread = query_ref[...]
    pair_lanes = 2 * HD
    prefix_keys = prefix_ref[:, :pair_lanes]
    prefix_values = prefix_ref[:, pair_lanes:]
    suffix_keys = suffix_ref[:, :pair_lanes]
    suffix_values = suffix_ref[:, pair_lanes:]
    contract = (((1,), (1,)), ((), ()))
    prefix_scores = lax.dot_general(
        spread, prefix_keys, contract, preferred_element_type=jnp.float32
    )
    suffix_scores = lax.dot_general(
        spread, suffix_keys, contract, preferred_element_type=jnp.float32
    )
    key_position = first + lax.broadcasted_iota(jnp.int32, suffix_scores.shape, 1)
    query_position = first + row_ref[...]
    allowed = (key_position >= start) & (key_position <= query_position)
    suffix_scores = jnp.where(allowed, suffix_scores, -jnp.inf)
    row_top = jnp.maximum(
        jnp.max(prefix_scores, axis=1, keepdims=True),
        jnp.max(suffix_scores, axis=1, keepdims=True),
    )
    prefix_weights = jnp.exp(prefix_scores - row_top)
    suffix_weights = jnp.exp(suffix_scores - row_top)
    denominator = jnp.sum(prefix_weights, axis=1, keepdims=True) + jnp.sum(
        suffix_weights, axis=1, keepdims=True
    )
    accumulated = jnp.dot(
        prefix_weights.astype(jnp.bfloat16), prefix_values, preferred_element_type=jnp.float32
    ) + jnp.dot(
        suffix_weights.astype(jnp.bfloat16), suffix_values, preferred_element_type=jnp.float32
    )
    attended = accumulated / denominator
    first_pair = attended[:, :HD]
    second_pair = attended[:, HD:]
    picked = jnp.where(pair_ref[...] > 0, second_pair, first_pair).astype(out_ref.dtype)
    window = out_ref.shape[0]
    for head in range(out_ref.shape[1] // HD):
        out_ref[:, head * HD:(head + 1) * HD] = picked[head * window:(head + 1) * window]


def window_attention(
    slot_index, firsts, starts, spread, slots, suffix_windows, query_rows, row_pairs, slot_rows
):
    requests, flat_rows, query_lanes = spread.shape
    window = suffix_windows.shape[1]
    lanes = slots.shape[1]
    head_count = flat_rows // window
    grid_spec = pltpu.PrefetchScalarGridSpec(
        num_scalar_prefetch=3,
        grid=(requests,),
        in_specs=[
            pl.BlockSpec((None, flat_rows, query_lanes), lambda k, slot, first, start: (k, 0, 0)),
            pl.BlockSpec((slot_rows, lanes), lambda k, slot, first, start: (slot[k], 0)),
            pl.BlockSpec((None, window, lanes), lambda k, slot, first, start: (k, 0, 0)),
            pl.BlockSpec((flat_rows, 1), lambda k, slot, first, start: (0, 0)),
            pl.BlockSpec((flat_rows, 1), lambda k, slot, first, start: (0, 0)),
        ],
        out_specs=pl.BlockSpec(
            (None, window, head_count * HD), lambda k, slot, first, start: (k, 0, 0)
        ),
    )
    return pl.pallas_call(
        attention_kernel,
        grid_spec=grid_spec,
        out_shape=jax.ShapeDtypeStruct((requests, window, head_count * HD), jnp.bfloat16),
    )(slot_index, firsts, starts, spread, slots, suffix_windows, query_rows, row_pairs)


def xor_tp(block, mask, n_tp):
    pairs = [(source, source ^ mask) for source in range(n_tp)]
    return lax.ppermute(block, "tp", pairs)


def from_partners(block, n_tp):
    if n_tp == 4:
        near = xor_tp(block, 1, n_tp)
        across = xor_tp(block, 2, n_tp)
        return [block, near, across, xor_tp(across, 1, n_tp)]
    return [block] + [xor_tp(block, mask, n_tp) for mask in range(1, n_tp)]


def shifted(block, shift, n_tp):
    pairs = [(source, (source + shift) % n_tp) for source in range(n_tp)]
    return lax.ppermute(block, "tp", pairs)


def local(
    residual,
    queries,
    suffix_kv,
    prefix_cache,
    out_weight,
    norm_gain,
    next_query_weight,
    lengths,
    tenant,
    owners,
    n_req,
    n_tp,
):
    row_count = queries.shape[0]
    head_count = queries.shape[1] // HD
    width = residual.shape[1]
    tp_index = lax.axis_index("tp")

    weight_pieces = []
    for mask in range(n_tp):
        partner = tp_index ^ mask
        piece = lax.dynamic_slice_in_dim(out_weight, partner * width, width, 1)
        weight_pieces.append(piece if mask == 0 else xor_tp(piece, mask, n_tp))

    head_ids = tp_index * head_count + jnp.arange(head_count, dtype=jnp.int32)
    pair_ids = head_ids // (QH // KVH) - tp_index
    select = (pair_ids[:, None] == jnp.arange(2, dtype=jnp.int32)[None, :]).astype(jnp.bfloat16)
    req_lengths = lengths[0]
    req_tenant = tenant[0]
    req_ends = jnp.cumsum(req_lengths)
    req_starts = req_ends - req_lengths
    position = jnp.arange(row_count, dtype=jnp.int32)
    request_ids = jnp.sum((position[:, None] >= req_ends[None, :]).astype(jnp.int32), axis=1)
    member = request_ids[:, None] == jnp.arange(req_lengths.shape[0], dtype=jnp.int32)[None, :]
    row_start = jnp.sum(jnp.where(member, req_starts[None, :], 0), axis=1)
    row_tenant = jnp.sum(jnp.where(member, req_tenant[None, :], 0), axis=1)
    score_scale = HD ** (-0.5)
    own_slot = jnp.transpose(
        prefix_cache.reshape(prefix_cache.shape[0], 2, 2, HD), (0, 2, 1, 3)
    ).reshape(prefix_cache.shape[0], -1)
    slots, slot_of_tenant = tenant_slots(own_slot, owners, n_req)
    suffix_rows = jnp.transpose(suffix_kv.reshape(row_count, 2, 2, HD), (0, 2, 1, 3)).reshape(
        row_count, -1
    )
    window = min(MOSTLEN, row_count)
    firsts = jnp.minimum(req_starts, row_count - window).astype(jnp.int32)
    head_select = jnp.transpose(select)[:, :, None, None]
    spreads = []
    suffix_windows = []
    for request in range(req_lengths.shape[0]):
        window_queries = lax.dynamic_slice_in_dim(queries, firsts[request], window, 0)
        window_queries = jnp.transpose(window_queries.reshape(window, head_count, HD), (1, 0, 2))
        spread = jnp.concatenate(
            [window_queries * head_select[0], window_queries * head_select[1]], axis=2
        )
        spreads.append((spread * score_scale).reshape(head_count * window, 2 * HD))
        suffix_windows.append(lax.dynamic_slice_in_dim(suffix_rows, firsts[request], window, 0))
    query_rows = (jnp.arange(head_count * window, dtype=jnp.int32) % window)[:, None]
    row_pairs = jnp.repeat(pair_ids.astype(jnp.int32), window)[:, None]
    slot_index = slot_of_tenant[req_tenant].astype(jnp.int32)
    results = window_attention(
        slot_index,
        firsts,
        req_starts.astype(jnp.int32),
        jnp.stack(spreads),
        slots,
        jnp.stack(suffix_windows),
        query_rows,
        row_pairs,
        own_slot.shape[0],
    ).reshape(-1, head_count * HD)
    source_rows = request_ids * window + position - firsts[request_ids]
    attended = jnp.take(results, source_rows, axis=0)

    head_blocks = from_partners(attended, n_tp)
    projected = None
    for mask in range(n_tp):
        part = jnp.dot(head_blocks[mask], weight_pieces[mask], preferred_element_type=jnp.float32)
        projected = part if projected is None else projected + part
    new_residual = (residual.astype(jnp.float32) + projected).astype(jnp.bfloat16)

    blocks = from_partners(new_residual, n_tp)
    widened = [block.astype(jnp.float32) for block in blocks]
    square_sums = sum(jnp.sum(block * block, axis=1, keepdims=True) for block in widened)
    mean_square = square_sums / (width * n_tp)
    scale = lax.rsqrt(mean_square + 1e-05)
    gain = norm_gain.astype(jnp.float32)
    next_sums = None
    for mask in range(n_tp):
        source = tp_index ^ mask
        block_gain = lax.dynamic_slice_in_dim(gain, source * width, width, 0)
        block_weight = lax.dynamic_slice_in_dim(next_query_weight, source * width, width, 0)
        normed = (widened[mask] * scale * block_gain).astype(jnp.bfloat16)
        part = jnp.dot(normed, block_weight, preferred_element_type=jnp.float32)
        next_sums = part if next_sums is None else next_sums + part
    return (new_residual, next_sums.astype(jnp.bfloat16))


def solution(mesh):
    n_req = mesh.shape["req"]
    n_tp = mesh.shape["tp"]

    def body(*args):
        return local(*args, n_req=n_req, n_tp=n_tp)

    return jax.shard_map(
        body,
        mesh=mesh,
        in_specs=(
            P("req", "tp"),
            P("req", "tp"),
            P("req", "tp", None),
            P("req", "tp", None),
            P("tp", None),
            P(),
            P(None, "tp"),
            P("req", None),
            P("req", None),
            P(),
        ),
        out_specs=(P("req", "tp"), P("req", "tp")),
        check_vma=False,
    )
```

```python
import jax
import jax.numpy as jnp
from jax import lax
from jax.experimental import pallas as pl
from jax.experimental.pallas import tpu as pltpu
from jax.sharding import PartitionSpec as P

QH = 20
KVH = 5
HD = 64
TENANTS = 4
MOSTLEN = 128
GATHER_SLOTS_MAX = 16


def from_root(block, axis, source):
    block = jnp.where(lax.axis_index(axis) == source, block, jnp.zeros_like(block))
    return lax.psum(block, axis)


def pick_heads(pair_rows, select):
    split_pair = pair_rows.reshape(pair_rows.shape[0], 2, 2, HD)
    key_heads = jnp.einsum(
        "njd,hj->nhd", split_pair[:, :, 0], select, preferred_element_type=jnp.float32
    ).astype(jnp.bfloat16)
    value_heads = jnp.einsum(
        "njd,hj->nhd", split_pair[:, :, 1], select, preferred_element_type=jnp.float32
    ).astype(jnp.bfloat16)
    return (key_heads, value_heads)


def xor_permute(block, mask, n_req):
    pairs = [(source, source ^ mask) for source in range(n_req)]
    return lax.ppermute(block, "req", pairs)


def tenant_slots(own_slot, owners, n_req):
    if n_req <= GATHER_SLOTS_MAX and n_req % 2 == 0 and (n_req & (n_req - 1)) == 0:
        req_index = lax.axis_index("req")
        mine = [own_slot] + [
            xor_permute(own_slot, 2 * chip_mask, n_req) for chip_mask in range(1, n_req // 2)
        ]
        theirs = [xor_permute(block, 1, n_req) for block in mine]
        slots = jnp.concatenate(
            [block for pair in zip(mine, theirs) for block in pair], axis=0
        )
        chip_offset = (owners // 2) ^ (req_index // 2)
        other_core = (owners % 2) != (req_index % 2)
        return slots, 2 * chip_offset + other_core.astype(jnp.int32)
    blocks = [from_root(own_slot, "req", owners[tenant_id]) for tenant_id in range(TENANTS)]
    return jnp.concatenate(blocks, axis=0), jnp.arange(TENANTS, dtype=jnp.int32)


def attention_kernel(
    slot_ref, first_ref, start_ref, query_ref, prefix_ref, suffix_ref, row_ref, pair_ref, out_ref
):
    request = pl.program_id(0)
    first = first_ref[request]
    start = start_ref[request]
    spread = query_ref[...]
    pair_lanes = 2 * HD
    prefix_keys = prefix_ref[:, :pair_lanes]
    prefix_values = prefix_ref[:, pair_lanes:]
    suffix_keys = suffix_ref[:, :pair_lanes]
    suffix_values = suffix_ref[:, pair_lanes:]
    contract = (((1,), (1,)), ((), ()))
    prefix_scores = lax.dot_general(
        spread, prefix_keys, contract, preferred_element_type=jnp.float32
    )
    suffix_scores = lax.dot_general(
        spread, suffix_keys, contract, preferred_element_type=jnp.float32
    )
    key_position = first + lax.broadcasted_iota(jnp.int32, suffix_scores.shape, 1)
    query_position = first + row_ref[...]
    allowed = (key_position >= start) & (key_position <= query_position)
    suffix_scores = jnp.where(allowed, suffix_scores, -jnp.inf)
    row_top = jnp.maximum(
        jnp.max(prefix_scores, axis=1, keepdims=True),
        jnp.max(suffix_scores, axis=1, keepdims=True),
    )
    prefix_weights = jnp.exp(prefix_scores - row_top)
    suffix_weights = jnp.exp(suffix_scores - row_top)
    denominator = jnp.sum(prefix_weights, axis=1, keepdims=True) + jnp.sum(
        suffix_weights, axis=1, keepdims=True
    )
    accumulated = jnp.dot(
        prefix_weights.astype(jnp.bfloat16), prefix_values, preferred_element_type=jnp.float32
    ) + jnp.dot(
        suffix_weights.astype(jnp.bfloat16), suffix_values, preferred_element_type=jnp.float32
    )
    attended = accumulated / denominator
    first_pair = attended[:, :HD]
    second_pair = attended[:, HD:]
    out_ref[...] = jnp.where(pair_ref[...] > 0, second_pair, first_pair).astype(out_ref.dtype)


def window_attention(
    slot_index, firsts, starts, spread, slots, suffix_windows, query_rows, row_pairs, slot_rows
):
    requests, flat_rows, query_lanes = spread.shape
    window = suffix_windows.shape[1]
    lanes = slots.shape[1]
    grid_spec = pltpu.PrefetchScalarGridSpec(
        num_scalar_prefetch=3,
        grid=(requests,),
        in_specs=[
            pl.BlockSpec((None, flat_rows, query_lanes), lambda k, slot, first, start: (k, 0, 0)),
            pl.BlockSpec((slot_rows, lanes), lambda k, slot, first, start: (slot[k], 0)),
            pl.BlockSpec((None, window, lanes), lambda k, slot, first, start: (k, 0, 0)),
            pl.BlockSpec((flat_rows, 1), lambda k, slot, first, start: (0, 0)),
            pl.BlockSpec((flat_rows, 1), lambda k, slot, first, start: (0, 0)),
        ],
        out_specs=pl.BlockSpec((None, flat_rows, HD), lambda k, slot, first, start: (k, 0, 0)),
    )
    return pl.pallas_call(
        attention_kernel,
        grid_spec=grid_spec,
        out_shape=jax.ShapeDtypeStruct((requests, flat_rows, HD), jnp.bfloat16),
    )(slot_index, firsts, starts, spread, slots, suffix_windows, query_rows, row_pairs)


def xor_tp(block, mask, n_tp):
    pairs = [(source, source ^ mask) for source in range(n_tp)]
    return lax.ppermute(block, "tp", pairs)


def from_partners(block, n_tp):
    if n_tp == 4:
        near = xor_tp(block, 1, n_tp)
        across = xor_tp(block, 2, n_tp)
        return [block, near, across, xor_tp(across, 1, n_tp)]
    return [block] + [xor_tp(block, mask, n_tp) for mask in range(1, n_tp)]


def shifted(block, shift, n_tp):
    pairs = [(source, (source + shift) % n_tp) for source in range(n_tp)]
    return lax.ppermute(block, "tp", pairs)


def local(
    residual,
    queries,
    suffix_kv,
    prefix_cache,
    out_weight,
    norm_gain,
    next_query_weight,
    lengths,
    tenant,
    owners,
    n_req,
    n_tp,
):
    row_count = queries.shape[0]
    head_count = queries.shape[1] // HD
    width = residual.shape[1]
    tp_index = lax.axis_index("tp")

    weight_pieces = []
    for mask in range(n_tp):
        partner = tp_index ^ mask
        piece = lax.dynamic_slice_in_dim(out_weight, partner * width, width, 1)
        weight_pieces.append(piece if mask == 0 else xor_tp(piece, mask, n_tp))

    head_ids = tp_index * head_count + jnp.arange(head_count, dtype=jnp.int32)
    pair_ids = head_ids // (QH // KVH) - tp_index
    select = (pair_ids[:, None] == jnp.arange(2, dtype=jnp.int32)[None, :]).astype(jnp.bfloat16)
    req_lengths = lengths[0]
    req_tenant = tenant[0]
    req_ends = jnp.cumsum(req_lengths)
    req_starts = req_ends - req_lengths
    position = jnp.arange(row_count, dtype=jnp.int32)
    request_ids = jnp.sum((position[:, None] >= req_ends[None, :]).astype(jnp.int32), axis=1)
    member = request_ids[:, None] == jnp.arange(req_lengths.shape[0], dtype=jnp.int32)[None, :]
    row_start = jnp.sum(jnp.where(member, req_starts[None, :], 0), axis=1)
    row_tenant = jnp.sum(jnp.where(member, req_tenant[None, :], 0), axis=1)
    score_scale = HD ** (-0.5)
    own_slot = jnp.transpose(
        prefix_cache.reshape(prefix_cache.shape[0], 2, 2, HD), (0, 2, 1, 3)
    ).reshape(prefix_cache.shape[0], -1)
    slots, slot_of_tenant = tenant_slots(own_slot, owners, n_req)
    suffix_rows = jnp.transpose(suffix_kv.reshape(row_count, 2, 2, HD), (0, 2, 1, 3)).reshape(
        row_count, -1
    )
    window = min(MOSTLEN, row_count)
    firsts = jnp.minimum(req_starts, row_count - window).astype(jnp.int32)
    head_select = jnp.transpose(select)[:, :, None, None]
    spreads = []
    suffix_windows = []
    for request in range(req_lengths.shape[0]):
        window_queries = lax.dynamic_slice_in_dim(queries, firsts[request], window, 0)
        window_queries = jnp.transpose(window_queries.reshape(window, head_count, HD), (1, 0, 2))
        spread = jnp.concatenate(
            [window_queries * head_select[0], window_queries * head_select[1]], axis=2
        )
        spreads.append((spread * score_scale).reshape(head_count * window, 2 * HD))
        suffix_windows.append(lax.dynamic_slice_in_dim(suffix_rows, firsts[request], window, 0))
    query_rows = (jnp.arange(head_count * window, dtype=jnp.int32) % window)[:, None]
    row_pairs = jnp.repeat(pair_ids.astype(jnp.int32), window)[:, None]
    slot_index = slot_of_tenant[req_tenant].astype(jnp.int32)
    results = window_attention(
        slot_index,
        firsts,
        req_starts.astype(jnp.int32),
        jnp.stack(spreads),
        slots,
        jnp.stack(suffix_windows),
        query_rows,
        row_pairs,
        own_slot.shape[0],
    ).reshape(-1, head_count, window, HD)
    attended = jnp.zeros((row_count, head_count * HD), jnp.bfloat16)
    window_offsets = jnp.arange(window, dtype=jnp.int32)
    for request in range(req_lengths.shape[0]):
        window_attended = jnp.transpose(results[request], (1, 0, 2)).reshape(window, -1)
        window_rows = firsts[request] + window_offsets
        mine = (window_rows >= req_starts[request]) & (window_rows < req_ends[request])
        kept = lax.dynamic_slice_in_dim(attended, firsts[request], window, 0)
        attended = lax.dynamic_update_slice_in_dim(
            attended, jnp.where(mine[:, None], window_attended, kept), firsts[request], 0
        )

    head_blocks = from_partners(attended, n_tp)
    projected = None
    for mask in range(n_tp):
        part = jnp.dot(head_blocks[mask], weight_pieces[mask], preferred_element_type=jnp.float32)
        projected = part if projected is None else projected + part
    new_residual = (residual.astype(jnp.float32) + projected).astype(jnp.bfloat16)

    blocks = from_partners(new_residual, n_tp)
    widened = [block.astype(jnp.float32) for block in blocks]
    square_sums = sum(jnp.sum(block * block, axis=1, keepdims=True) for block in widened)
    mean_square = square_sums / (width * n_tp)
    scale = lax.rsqrt(mean_square + 1e-05)
    gain = norm_gain.astype(jnp.float32)
    next_sums = None
    for mask in range(n_tp):
        source = tp_index ^ mask
        block_gain = lax.dynamic_slice_in_dim(gain, source * width, width, 0)
        block_weight = lax.dynamic_slice_in_dim(next_query_weight, source * width, width, 0)
        normed = (widened[mask] * scale * block_gain).astype(jnp.bfloat16)
        part = jnp.dot(normed, block_weight, preferred_element_type=jnp.float32)
        next_sums = part if next_sums is None else next_sums + part
    return (new_residual, next_sums.astype(jnp.bfloat16))


def solution(mesh):
    n_req = mesh.shape["req"]
    n_tp = mesh.shape["tp"]

    def body(*args):
        return local(*args, n_req=n_req, n_tp=n_tp)

    return jax.shard_map(
        body,
        mesh=mesh,
        in_specs=(
            P("req", "tp"),
            P("req", "tp"),
            P("req", "tp", None),
            P("req", "tp", None),
            P("tp", None),
            P(),
            P(None, "tp"),
            P("req", None),
            P("req", None),
            P(),
        ),
        out_specs=(P("req", "tp"), P("req", "tp")),
        check_vma=False,
    )
```

```python
import jax
import jax.numpy as jnp
from jax import lax
from jax.experimental import pallas as pl
from jax.experimental.pallas import tpu as pltpu
from jax.sharding import PartitionSpec as P

QH = 20
KVH = 5
HD = 64
TENANTS = 4
MOSTLEN = 128
GATHER_SLOTS_MAX = 16


def from_root(block, axis, source):
    block = jnp.where(lax.axis_index(axis) == source, block, jnp.zeros_like(block))
    return lax.psum(block, axis)


def pick_heads(pair_rows, select):
    split_pair = pair_rows.reshape(pair_rows.shape[0], 2, 2, HD)
    key_heads = jnp.einsum(
        "njd,hj->nhd", split_pair[:, :, 0], select, preferred_element_type=jnp.float32
    ).astype(jnp.bfloat16)
    value_heads = jnp.einsum(
        "njd,hj->nhd", split_pair[:, :, 1], select, preferred_element_type=jnp.float32
    ).astype(jnp.bfloat16)
    return (key_heads, value_heads)


def xor_permute(block, mask, n_req):
    pairs = [(source, source ^ mask) for source in range(n_req)]
    return lax.ppermute(block, "req", pairs)


def tenant_slots(own_slot, owners, n_req):
    if n_req <= GATHER_SLOTS_MAX and n_req % 2 == 0 and (n_req & (n_req - 1)) == 0:
        req_index = lax.axis_index("req")
        mine = [own_slot] + [
            xor_permute(own_slot, 2 * chip_mask, n_req) for chip_mask in range(1, n_req // 2)
        ]
        theirs = [xor_permute(block, 1, n_req) for block in mine]
        slots = jnp.concatenate(
            [block for pair in zip(mine, theirs) for block in pair], axis=0
        )
        chip_offset = (owners // 2) ^ (req_index // 2)
        other_core = (owners % 2) != (req_index % 2)
        return slots, 2 * chip_offset + other_core.astype(jnp.int32)
    blocks = [from_root(own_slot, "req", owners[tenant_id]) for tenant_id in range(TENANTS)]
    return jnp.concatenate(blocks, axis=0), jnp.arange(TENANTS, dtype=jnp.int32)


def attention_kernel(
    slot_ref, first_ref, start_ref, query_ref, prefix_ref, suffix_ref, row_ref, pair_ref, out_ref
):
    request = pl.program_id(0)
    first = first_ref[request]
    start = start_ref[request]
    spread = query_ref[...]
    pair_lanes = 2 * HD
    prefix_keys = prefix_ref[:, :pair_lanes]
    prefix_values = prefix_ref[:, pair_lanes:]
    suffix_keys = suffix_ref[:, :pair_lanes]
    suffix_values = suffix_ref[:, pair_lanes:]
    contract = (((1,), (1,)), ((), ()))
    prefix_scores = lax.dot_general(
        spread, prefix_keys, contract, preferred_element_type=jnp.float32
    )
    suffix_scores = lax.dot_general(
        spread, suffix_keys, contract, preferred_element_type=jnp.float32
    )
    key_position = first + lax.broadcasted_iota(jnp.int32, suffix_scores.shape, 1)
    query_position = first + row_ref[...]
    allowed = (key_position >= start) & (key_position <= query_position)
    suffix_scores = jnp.where(allowed, suffix_scores, -jnp.inf)
    row_top = jnp.maximum(
        jnp.max(prefix_scores, axis=1, keepdims=True),
        jnp.max(suffix_scores, axis=1, keepdims=True),
    )
    prefix_weights = jnp.exp(prefix_scores - row_top)
    suffix_weights = jnp.exp(suffix_scores - row_top)
    denominator = jnp.sum(prefix_weights, axis=1, keepdims=True) + jnp.sum(
        suffix_weights, axis=1, keepdims=True
    )
    accumulated = jnp.dot(
        prefix_weights.astype(jnp.bfloat16), prefix_values, preferred_element_type=jnp.float32
    ) + jnp.dot(
        suffix_weights.astype(jnp.bfloat16), suffix_values, preferred_element_type=jnp.float32
    )
    picked = jnp.where(pair_ref[...] > 0, accumulated[:, HD:], accumulated[:, :HD])
    out_ref[...] = (picked / denominator).astype(out_ref.dtype)


def window_attention(
    slot_index, firsts, starts, spread, slots, suffix_windows, query_rows, row_pairs, slot_rows
):
    requests, flat_rows, query_lanes = spread.shape
    window = suffix_windows.shape[1]
    lanes = slots.shape[1]
    grid_spec = pltpu.PrefetchScalarGridSpec(
        num_scalar_prefetch=3,
        grid=(requests,),
        in_specs=[
            pl.BlockSpec((None, flat_rows, query_lanes), lambda k, slot, first, start: (k, 0, 0)),
            pl.BlockSpec((slot_rows, lanes), lambda k, slot, first, start: (slot[k], 0)),
            pl.BlockSpec((None, window, lanes), lambda k, slot, first, start: (k, 0, 0)),
            pl.BlockSpec((flat_rows, 1), lambda k, slot, first, start: (0, 0)),
            pl.BlockSpec((flat_rows, 1), lambda k, slot, first, start: (0, 0)),
        ],
        out_specs=pl.BlockSpec((None, flat_rows, HD), lambda k, slot, first, start: (k, 0, 0)),
    )
    return pl.pallas_call(
        attention_kernel,
        grid_spec=grid_spec,
        out_shape=jax.ShapeDtypeStruct((requests, flat_rows, HD), jnp.bfloat16),
    )(slot_index, firsts, starts, spread, slots, suffix_windows, query_rows, row_pairs)


def xor_tp(block, mask, n_tp):
    pairs = [(source, source ^ mask) for source in range(n_tp)]
    return lax.ppermute(block, "tp", pairs)


def from_partners(block, n_tp):
    if n_tp == 4:
        near = xor_tp(block, 1, n_tp)
        across = xor_tp(block, 2, n_tp)
        return [block, near, across, xor_tp(across, 1, n_tp)]
    return [block] + [xor_tp(block, mask, n_tp) for mask in range(1, n_tp)]


def shifted(block, shift, n_tp):
    pairs = [(source, (source + shift) % n_tp) for source in range(n_tp)]
    return lax.ppermute(block, "tp", pairs)


def local(
    residual,
    queries,
    suffix_kv,
    prefix_cache,
    out_weight,
    norm_gain,
    next_query_weight,
    lengths,
    tenant,
    owners,
    n_req,
    n_tp,
):
    row_count = queries.shape[0]
    head_count = queries.shape[1] // HD
    width = residual.shape[1]
    tp_index = lax.axis_index("tp")

    weight_pieces = []
    for mask in range(n_tp):
        partner = tp_index ^ mask
        piece = lax.dynamic_slice_in_dim(out_weight, partner * width, width, 1)
        weight_pieces.append(piece if mask == 0 else xor_tp(piece, mask, n_tp))

    head_ids = tp_index * head_count + jnp.arange(head_count, dtype=jnp.int32)
    pair_ids = head_ids // (QH // KVH) - tp_index
    select = (pair_ids[:, None] == jnp.arange(2, dtype=jnp.int32)[None, :]).astype(jnp.bfloat16)
    req_lengths = lengths[0]
    req_tenant = tenant[0]
    req_ends = jnp.cumsum(req_lengths)
    req_starts = req_ends - req_lengths
    position = jnp.arange(row_count, dtype=jnp.int32)
    request_ids = jnp.sum((position[:, None] >= req_ends[None, :]).astype(jnp.int32), axis=1)
    member = request_ids[:, None] == jnp.arange(req_lengths.shape[0], dtype=jnp.int32)[None, :]
    row_start = jnp.sum(jnp.where(member, req_starts[None, :], 0), axis=1)
    row_tenant = jnp.sum(jnp.where(member, req_tenant[None, :], 0), axis=1)
    score_scale = HD ** (-0.5)
    own_slot = jnp.transpose(
        prefix_cache.reshape(prefix_cache.shape[0], 2, 2, HD), (0, 2, 1, 3)
    ).reshape(prefix_cache.shape[0], -1)
    slots, slot_of_tenant = tenant_slots(own_slot, owners, n_req)
    suffix_rows = jnp.transpose(suffix_kv.reshape(row_count, 2, 2, HD), (0, 2, 1, 3)).reshape(
        row_count, -1
    )
    window = min(MOSTLEN, row_count)
    firsts = jnp.minimum(req_starts, row_count - window).astype(jnp.int32)
    head_select = jnp.transpose(select)[:, :, None, None]
    spreads = []
    suffix_windows = []
    for request in range(req_lengths.shape[0]):
        window_queries = lax.dynamic_slice_in_dim(queries, firsts[request], window, 0)
        window_queries = jnp.transpose(window_queries.reshape(window, head_count, HD), (1, 0, 2))
        spread = jnp.concatenate(
            [window_queries * head_select[0], window_queries * head_select[1]], axis=2
        )
        spreads.append((spread * score_scale).reshape(head_count * window, 2 * HD))
        suffix_windows.append(lax.dynamic_slice_in_dim(suffix_rows, firsts[request], window, 0))
    query_rows = (jnp.arange(head_count * window, dtype=jnp.int32) % window)[:, None]
    row_pairs = jnp.repeat(pair_ids.astype(jnp.int32), window)[:, None]
    slot_index = slot_of_tenant[req_tenant].astype(jnp.int32)
    results = window_attention(
        slot_index,
        firsts,
        req_starts.astype(jnp.int32),
        jnp.stack(spreads),
        slots,
        jnp.stack(suffix_windows),
        query_rows,
        row_pairs,
        own_slot.shape[0],
    ).reshape(-1, head_count, window, HD)
    attended = jnp.zeros((row_count, head_count * HD), jnp.bfloat16)
    for request in range(req_lengths.shape[0]):
        window_attended = jnp.transpose(results[request], (1, 0, 2)).reshape(window, -1)
        placed = lax.dynamic_update_slice_in_dim(
            jnp.zeros_like(attended), window_attended, firsts[request], 0
        )
        attended = jnp.where((request_ids == request)[:, None], placed, attended)

    head_blocks = from_partners(attended, n_tp)
    projected = None
    for mask in range(n_tp):
        part = jnp.dot(head_blocks[mask], weight_pieces[mask], preferred_element_type=jnp.float32)
        projected = part if projected is None else projected + part
    new_residual = (residual.astype(jnp.float32) + projected).astype(jnp.bfloat16)

    blocks = from_partners(new_residual, n_tp)
    widened = [block.astype(jnp.float32) for block in blocks]
    square_sums = sum(jnp.sum(block * block, axis=1, keepdims=True) for block in widened)
    mean_square = square_sums / (width * n_tp)
    scale = lax.rsqrt(mean_square + 1e-05)
    gain = norm_gain.astype(jnp.float32)
    next_sums = None
    for mask in range(n_tp):
        source = tp_index ^ mask
        block_gain = lax.dynamic_slice_in_dim(gain, source * width, width, 0)
        block_weight = lax.dynamic_slice_in_dim(next_query_weight, source * width, width, 0)
        normed = (widened[mask] * scale * block_gain).astype(jnp.bfloat16)
        part = jnp.dot(normed, block_weight, preferred_element_type=jnp.float32)
        next_sums = part if next_sums is None else next_sums + part
    return (new_residual, next_sums.astype(jnp.bfloat16))


def solution(mesh):
    n_req = mesh.shape["req"]
    n_tp = mesh.shape["tp"]

    def body(*args):
        return local(*args, n_req=n_req, n_tp=n_tp)

    return jax.shard_map(
        body,
        mesh=mesh,
        in_specs=(
            P("req", "tp"),
            P("req", "tp"),
            P("req", "tp", None),
            P("req", "tp", None),
            P("tp", None),
            P(),
            P(None, "tp"),
            P("req", None),
            P("req", None),
            P(),
        ),
        out_specs=(P("req", "tp"), P("req", "tp")),
        check_vma=False,
    )
```
